32 devices in a mesh: groups: 2 (over y), orient: 8 (over z, x), tile: 2 (over core).
Axes of the slice: x: 2, y: 2, z: 4, core: 2. Of those that a mesh axis runs over, the one named last changes fastest.
Arguments:
- micrograph: bfloat16 [2048, 256], P(('groups', 'orient'), 'tile'), parts along dimension 0, may hold values from -6 to 6
- templates: bfloat16 [8, 192, 192], P('orient'), may hold values from -0.03125 to 0.03125
- defocus: int32 [16], P(('groups', 'orient')), parts along dimension 0, may hold values from 0 to 7
- ctf: float32 [16, 320, 320], P('groups'), parts along dimension 0, may hold values from -1 to 1
- usable: int32 [16, 2], P(('groups', 'orient'), 'tile'), parts along dimension 0, may hold values from 1 to 4, as said below
Outputs:
- peak_map: float32 [2048, 256], P(('groups', 'orient'), 'tile'), parts along dimension 0
- mean_map: float32 [2048, 256], P(('groups', 'orient'), 'tile'), parts along dimension 0
- square_map: float32 [2048, 256], P(('groups', 'orient'), 'tile'), parts along dimension 0
The draws below stay inside these ranges and needn't reach their ends.
There are 2 independent parts, one for each index of `groups`. The reference program is written for one: setup_inputs(seed, part) draws one part's arguments, and reference() takes and returns one part's arrays. A program takes and returns all parts, laid end to end along the dimension named above; an argument that names none is the same for every part. Nothing has to cross between parts.
Inputs may be any that keep to these rules, and one draw needn't show every extreme that they name: usable rows of each tile form its first usable x 32 rows; in every micrograph some tile has all 4 blocks usable.
All inputs are finite; a program needn't handle non-finite values.
Results may differ from the reference program's by a relative error of at most 0.0094.
Values may be sent and summed in bfloat16 or wider, within the bound.
No kernel may reach another device: no remote copies, remote signals or barrier semaphores. Data moves between devices by JAX's collectives and lax.ppermute only.
A program may use at most 128 MiB of HBM per device.

```python
import math
import jax
import jax.numpy as jnp
from jax import lax

C = 128
H = 96
B = 192
RB = 32
NDEF = 8
P_SIZE = 320
NB = 4
ORIENTS = 8
NR = 1024
NC = 256
N_ORIENT = 8
N_TILE = 2


def draw_usable(key, part):
    first_key, second_key, third_key = jax.random.split(key, 3)
    grid_shape = (N_ORIENT, N_TILE)
    one_draw = jax.random.randint(first_key, grid_shape, 1, NB + 1)
    two_draw = jax.random.randint(second_key, grid_shape, 1, NB + 1)
    blocks = jnp.minimum(one_draw, two_draw).reshape(-1)
    chosen_spot = jax.random.randint(third_key, (), 0, N_ORIENT * N_TILE)
    blocks = jnp.where(jnp.arange(N_ORIENT * N_TILE) == chosen_spot, NB, blocks)
    return blocks.reshape(grid_shape).astype(jnp.int32)


def touch_ends(array, rng, least, largest):
    extent = array.shape
    index_at = [jax.random.randint(jax.random.fold_in(rng, axis), (), 0, extent[axis]) for axis in range(len(extent))]
    array = array.at[tuple(index_at)].set(least)
    longest = extent.index(max(extent))
    index_at[longest] = (index_at[longest] + 1) % extent[longest]
    return array.at[tuple(index_at)].set(largest)


def block_scale(rng, dims, shards, least, largest):
    level = 1.0
    for dim, shards_of in shards:
        steps = jax.random.uniform(jax.random.fold_in(jax.random.fold_in(rng, 6), dim), (shards_of,), jnp.float32, least / len(shards), largest / len(shards))
        level = level * jnp.repeat(jnp.exp(steps), dims[dim] // shards_of).reshape((-1,) + (1,) * (len(dims) - 1 - dim))
    return level


def noise(key, extent, deviation, reach, cuts=(), kind=jnp.bfloat16):
    level = block_scale(key, extent, cuts, -0.22, 0.18) if cuts else 1.0
    values = jax.random.normal(key, extent, jnp.float32) * deviation * level
    return jnp.minimum(jnp.maximum(values, -reach), reach).astype(kind)


def setup_inputs(seed: int = 0, part: int = 0) -> dict:
    splits = jax.random.split(jax.random.key(seed), 6)
    own_keys = jax.random.split(jax.random.fold_in(splits[5], part), 6)
    micrograph = noise(own_keys[0], (NR, NC), 1.0, 6.0, ((0, 8), (1, 2)))
    templates = noise(splits[1], (ORIENTS, B, B), (B * B) ** -0.5, 0.03125, ((0, 8),))
    defocus = touch_ends(jax.random.randint(own_keys[2], (ORIENTS,), 0, NDEF), jax.random.fold_in(own_keys[2], 1), 0, NDEF - 1).astype(jnp.int32)
    ctf = jnp.clip(jax.random.uniform(own_keys[3], (NDEF, P_SIZE, P_SIZE), jnp.float32, -1.0, 1.0), -1.0, 1.0)
    usable = draw_usable(jax.random.fold_in(jax.random.fold_in(splits[5], part), 71), part)
    return {"micrograph": micrograph, "templates": templates, "defocus": defocus, "ctf": ctf, "usable": usable}


def twiddles(padded_size):
    position = jnp.arange(padded_size, dtype=jnp.int32)
    phase_index = (position[:, None] * position[None, :]) % padded_size
    angles = phase_index.astype(jnp.float32) * (2.0 * math.pi / padded_size)
    return jnp.cos(angles).astype(jnp.bfloat16), jnp.sin(angles).astype(jnp.bfloat16)


def fdot(left, right):
    return jnp.dot(left.astype(jnp.float32), right.astype(jnp.float32), precision=lax.Precision.HIGHEST)


def bmat(form, left, right):
    return jnp.einsum(form, left.astype(jnp.float32), right.astype(jnp.float32), precision=lax.Precision.HIGHEST)


def weighted_spectrum(template, plane_id, cosines, sines, ctf):
    box_size = template.shape[0]
    padded_size = cosines.shape[0]
    shifted = (jnp.arange(box_size, dtype=jnp.int32) - box_size // 2) % padded_size
    cos_rows = cosines[shifted]
    sin_rows = sines[shifted]
    cos_cols = cosines[:, shifted]
    sin_cols = sines[:, shifted]
    part_real = fdot(template, cos_rows).astype(jnp.bfloat16)
    part_imag = (-fdot(template, sin_rows)).astype(jnp.bfloat16)
    full_real = fdot(cos_cols, part_real) + fdot(sin_cols, part_imag)
    full_imag = fdot(cos_cols, part_imag) - fdot(sin_cols, part_real)
    weight = lax.dynamic_index_in_dim(ctf, plane_id, 0, keepdims=False)
    return jnp.stack([full_real * weight, full_imag * weight]).astype(jnp.bfloat16)


def reference(micrograph, templates, defocus, ctf, usable):
    cosines, sines = twiddles(P_SIZE)
    framed = jnp.pad(micrograph, H)
    row_index = (jnp.arange(N_ORIENT, dtype=jnp.int32) * C)[:, None] + jnp.arange(P_SIZE, dtype=jnp.int32)[None, :]
    col_index = (jnp.arange(N_TILE, dtype=jnp.int32) * C)[:, None] + jnp.arange(P_SIZE, dtype=jnp.int32)[None, :]
    tile_stack = framed[row_index[:, None, :, None], col_index[None, :, None, :]].reshape(N_ORIENT * N_TILE, P_SIZE, P_SIZE)
    half_real = bmat("tjk,kv->tjv", tile_stack, cosines).astype(jnp.bfloat16)
    half_imag = (-bmat("tjk,kv->tjv", tile_stack, sines)).astype(jnp.bfloat16)
    spec_real = (bmat("uj,tjv->tuv", cosines, half_real) + bmat("uj,tjv->tuv", sines, half_imag)).astype(jnp.bfloat16)
    spec_imag = (bmat("uj,tjv->tuv", cosines, half_imag) - bmat("uj,tjv->tuv", sines, half_real)).astype(jnp.bfloat16)
    spec_real32 = spec_real.astype(jnp.float32)
    spec_imag32 = spec_imag.astype(jnp.float32)
    row_cos = cosines[H:H + C]
    row_sin = sines[H:H + C]
    col_cos = cosines[:, H:H + C]
    col_sin = sines[:, H:H + C]
    scaling = 1.0 / (P_SIZE * P_SIZE)

    def one_slot(running, inputs):
        template, plane_id = inputs
        weighted = weighted_spectrum(template, plane_id, cosines, sines, ctf).astype(jnp.float32)
        prod_real = (spec_real32 * weighted[0] + spec_imag32 * weighted[1]).astype(jnp.bfloat16)
        prod_imag = (spec_imag32 * weighted[0] - spec_real32 * weighted[1]).astype(jnp.bfloat16)
        left_real = (bmat("rp,tpq->trq", row_cos, prod_real) - bmat("rp,tpq->trq", row_sin, prod_imag)).astype(jnp.bfloat16)
        left_imag = (bmat("rp,tpq->trq", row_cos, prod_imag) + bmat("rp,tpq->trq", row_sin, prod_real)).astype(jnp.bfloat16)
        correlation = (bmat("trq,qc->trc", left_real, col_cos) - bmat("trq,qc->trc", left_imag, col_sin)) * scaling
        peak_map, sum_map, squares = running
        return (jnp.maximum(peak_map, correlation), sum_map + correlation, squares + correlation * correlation), None

    count_tiles = N_ORIENT * N_TILE
    initial = (jnp.full((count_tiles, C, C), -jnp.inf, jnp.float32), jnp.zeros((count_tiles, C, C), jnp.float32), jnp.zeros((count_tiles, C, C), jnp.float32))
    running, unused = lax.scan(one_slot, initial, (templates, defocus))
    peak_map, sum_map, squares = running
    live_rows = jnp.arange(C, dtype=jnp.int32)[None, :] < RB * usable.reshape(-1)[:, None]
    row_mask = live_rows[:, :, None]

    def place(values):
        return values.reshape(N_ORIENT, N_TILE, C, C).transpose(0, 2, 1, 3).reshape(N_ORIENT * C, N_TILE * C)

    peak_out = place(jnp.where(row_mask, peak_map, 0.0))
    mean_out = place(jnp.where(row_mask, sum_map / ORIENTS, 0.0))
    square_out = place(jnp.where(row_mask, squares / ORIENTS, 0.0))
    return (peak_out, mean_out, square_out)
```

```python
import math

import jax
import jax.numpy as jnp
import ml_dtypes
import numpy as np
from jax import lax
from jax.sharding import PartitionSpec as P

RB = 32
CHUNK = 8


def extended(block, sides, width):
    for axis, dim in sides:
        count = lax.axis_size(axis)
        forward = [(i, i + 1) for i in range(count - 1)]
        backward = [(target, source) for source, target in forward]
        low = lax.ppermute(
            lax.slice_in_dim(block, block.shape[dim] - width, None, axis=dim), axis, forward
        )
        high = lax.ppermute(lax.slice_in_dim(block, 0, width, axis=dim), axis, backward)
        block = jnp.concatenate([low, block, high], axis=dim)
    return block


def twiddles(padded_size):
    position = np.arange(padded_size, dtype=np.int64)
    phase_index = (position[:, None] * position[None, :]) % padded_size
    angles = phase_index.astype(np.float32) * np.float32(2.0 * math.pi / padded_size)
    angles = angles.astype(np.float64)
    cosines = np.cos(angles).astype(np.float32).astype(ml_dtypes.bfloat16)
    sines = np.sin(angles).astype(np.float32).astype(ml_dtypes.bfloat16)
    return cosines, sines


def matmul(left, right):
    return jnp.dot(left, right, preferred_element_type=jnp.float32)


def body(micrograph, templates, defocus, ctf, usable):
    bf16 = jnp.bfloat16
    f32 = jnp.float32
    tile_width = micrograph.shape[0]
    padded_size = ctf.shape[1]
    box_size = templates.shape[1]
    margin = (padded_size - tile_width) // 2
    scaling = 1.0 / (padded_size * padded_size)
    n = padded_size
    cos_np, sin_np = twiddles(n)

    shifted = (np.arange(box_size) - box_size // 2) % n
    temp_rows = jnp.asarray(np.concatenate([cos_np[shifted, :], -sin_np[shifted, :]], axis=1))
    temp_cols = jnp.asarray(np.concatenate([cos_np[:, shifted], sin_np[:, shifted]], axis=0))
    half_mat = jnp.asarray(np.concatenate([cos_np, -sin_np], axis=1))
    spec_mat = jnp.asarray(np.concatenate([cos_np, sin_np], axis=0))
    row_mat = jnp.asarray(
        np.concatenate([cos_np[margin : margin + tile_width], sin_np[margin : margin + tile_width]], axis=0)
    )
    col_mat = jnp.asarray(
        np.concatenate([cos_np[:, margin : margin + tile_width], -sin_np[:, margin : margin + tile_width]], axis=0)
    )

    local_count = templates.shape[0]
    id_row = jnp.broadcast_to(defocus.astype(bf16)[:, None, None], (local_count, 1, box_size))
    packed = jnp.concatenate([templates, id_row], axis=1)
    gathered = lax.all_gather(packed, "orient", axis=0, tiled=True)
    all_templates = gathered[:, :box_size, :]
    all_ids = gathered[:, box_size, 0].astype(jnp.int32)
    total = all_templates.shape[0]

    padded = extended(micrograph, (("orient", 0), ("tile", 1)), margin)
    half = matmul(padded, half_mat).astype(bf16)
    spec_full = matmul(spec_mat, half)
    spec_real = (spec_full[:n, :n] + spec_full[n:, n:]).astype(bf16).astype(f32)
    spec_imag = (spec_full[:n, n:] - spec_full[n:, :n]).astype(bf16).astype(f32)

    def chunk_stats(chunk_templates, chunk_ids):
        count = chunk_templates.shape[0]
        part = jnp.einsum("okj,jv->kov", chunk_templates, temp_rows, preferred_element_type=f32).astype(bf16)
        full = jnp.einsum("pk,kov->pov", temp_cols, part, preferred_element_type=f32)
        full_real = full[:n, :, :n] + full[n:, :, n:]
        full_imag = full[:n, :, n:] - full[n:, :, :n]
        weight = jnp.take(ctf, chunk_ids, axis=0).transpose(1, 0, 2)
        w_real = (full_real * weight).astype(bf16).astype(f32)
        w_imag = (full_imag * weight).astype(bf16).astype(f32)
        s_real = spec_real[:, None, :]
        s_imag = spec_imag[:, None, :]
        prod_real = (s_real * w_real + s_imag * w_imag).astype(bf16)
        prod_imag = (s_imag * w_real - s_real * w_imag).astype(bf16)
        prod = jnp.stack([prod_real, prod_imag], axis=1).reshape(n, 2 * count * n)
        left = matmul(row_mat, prod).reshape(2 * tile_width, 2, count, n)
        left_real = (left[:tile_width, 0] - left[tile_width:, 1]).astype(bf16)
        left_imag = (left[:tile_width, 1] + left[tile_width:, 0]).astype(bf16)
        stacked = jnp.concatenate([left_real, left_imag], axis=-1).reshape(tile_width * count, 2 * n)
        corr = (matmul(stacked, col_mat) * scaling).reshape(tile_width, count, tile_width)
        return (jnp.max(corr, axis=1), jnp.sum(corr, axis=1), jnp.sum(corr * corr, axis=1))

    chunk = min(CHUNK, total)
    n_chunks = total // chunk
    if n_chunks == 1:
        peak_map, sum_map, squares = chunk_stats(all_templates, all_ids)
    else:

        def step(index, tallies):
            start = index * chunk
            part_templates = lax.dynamic_slice_in_dim(all_templates, start, chunk, 0)
            part_ids = lax.dynamic_slice_in_dim(all_ids, start, chunk, 0)
            peak_c, sum_c, sq_c = chunk_stats(part_templates, part_ids)
            return (jnp.maximum(tallies[0], peak_c), tallies[1] + sum_c, tallies[2] + sq_c)

        shape = (tile_width, tile_width)
        initial = (jnp.full(shape, -jnp.inf, f32), jnp.zeros(shape, f32), jnp.zeros(shape, f32))
        peak_map, sum_map, squares = lax.fori_loop(0, n_chunks, step, initial)

    live = usable[0, 0]
    row_mask = (jnp.arange(tile_width, dtype=jnp.int32) < RB * live)[:, None]
    orient_count = float(total)
    peak_out = jnp.where(row_mask, peak_map, 0.0)
    mean_out = jnp.where(row_mask, sum_map / orient_count, 0.0)
    square_out = jnp.where(row_mask, squares / orient_count, 0.0)
    return (peak_out, mean_out, square_out)


def solution(mesh):
    return jax.shard_map(
        body,
        mesh=mesh,
        in_specs=(
            P(("groups", "orient"), "tile"),
            P("orient", None, None),
            P(("groups", "orient")),
            P("groups", None, None),
            P(("groups", "orient"), "tile"),
        ),
        out_specs=(
            P(("groups", "orient"), "tile"),
            P(("groups", "orient"), "tile"),
            P(("groups", "orient"), "tile"),
        ),
        check_vma=False,
    )
```

```python
import math

import jax
import jax.numpy as jnp
import ml_dtypes
import numpy as np
from jax import lax
from jax.sharding import PartitionSpec as P

RB = 32
CHUNK = 8


def extended(block, sides, width):
    for axis, dim in sides:
        count = lax.axis_size(axis)
        forward = [(i, i + 1) for i in range(count - 1)]
        backward = [(target, source) for source, target in forward]
        low = lax.ppermute(
            lax.slice_in_dim(block, block.shape[dim] - width, None, axis=dim), axis, forward
        )
        high = lax.ppermute(lax.slice_in_dim(block, 0, width, axis=dim), axis, backward)
        block = jnp.concatenate([low, block, high], axis=dim)
    return block


def twiddles(padded_size):
    position = np.arange(padded_size, dtype=np.int64)
    phase_index = (position[:, None] * position[None, :]) % padded_size
    angles = phase_index.astype(np.float32) * np.float32(2.0 * math.pi / padded_size)
    angles = angles.astype(np.float64)
    cosines = np.cos(angles).astype(np.float32).astype(ml_dtypes.bfloat16)
    sines = np.sin(angles).astype(np.float32).astype(ml_dtypes.bfloat16)
    return cosines, sines


def matmul(left, right):
    return jnp.dot(left, right, preferred_element_type=jnp.float32)


def gather_orient(block):
    size = lax.axis_size("orient")
    index = lax.axis_index("orient")
    step = 1
    while step < size:
        pairs = [(i, i ^ step) for i in range(size) if (i ^ step) < size]
        other = lax.ppermute(block, "orient", pairs)
        low_side = (index // step) % 2 == 0
        block = jnp.where(low_side, jnp.concatenate([block, other], 0), jnp.concatenate([other, block], 0))
        step *= 2
    return block


def body(micrograph, templates, defocus, ctf, usable):
    bf16 = jnp.bfloat16
    f32 = jnp.float32
    tile_width = micrograph.shape[0]
    padded_size = ctf.shape[1]
    box_size = templates.shape[1]
    margin = (padded_size - tile_width) // 2
    scaling = 1.0 / (padded_size * padded_size)
    n = padded_size
    cos_np, sin_np = twiddles(n)

    shifted = (np.arange(box_size) - box_size // 2) % n
    cos_full = jnp.asarray(cos_np)
    sin_full = jnp.asarray(sin_np)
    cos_rows = jnp.asarray(cos_np[shifted, :])
    sin_rows = jnp.asarray(sin_np[shifted, :])
    row_cos = jnp.asarray(cos_np[margin : margin + tile_width])
    row_sin = jnp.asarray(sin_np[margin : margin + tile_width])

    local_count = templates.shape[0]
    flat_size = box_size * box_size
    id_block = jnp.broadcast_to(defocus.astype(bf16)[:, None], (local_count, 128))
    packed = jnp.concatenate([templates.reshape(local_count, flat_size), id_block], axis=1)
    gathered = gather_orient(packed)
    total = gathered.shape[0]
    all_templates = gathered[:, :flat_size].reshape(total, box_size, box_size)
    all_ids = gathered[:, flat_size].astype(jnp.int32)

    padded = extended(micrograph, (("orient", 0), ("tile", 1)), margin)
    half_real = matmul(padded, cos_full).astype(bf16)
    half_imag = (-matmul(padded, sin_full)).astype(bf16)
    spec_real = (matmul(cos_full, half_real) + matmul(sin_full, half_imag)).astype(bf16).astype(f32)
    spec_imag = (matmul(cos_full, half_imag) - matmul(sin_full, half_real)).astype(bf16).astype(f32)

    def chunk_stats(chunk_templates, chunk_ids):
        part_real = jnp.einsum("okj,jq->okq", chunk_templates, cos_rows, preferred_element_type=f32).astype(bf16)
        part_imag = (-jnp.einsum("okj,jq->okq", chunk_templates, sin_rows, preferred_element_type=f32)).astype(bf16)
        full_real = jnp.einsum("kp,okq->opq", cos_rows, part_real, preferred_element_type=f32) + jnp.einsum(
            "kp,okq->opq", sin_rows, part_imag, preferred_element_type=f32
        )
        full_imag = jnp.einsum("kp,okq->opq", cos_rows, part_imag, preferred_element_type=f32) - jnp.einsum(
            "kp,okq->opq", sin_rows, part_real, preferred_element_type=f32
        )
        weight = jnp.take(ctf, chunk_ids, axis=0)
        w_real = (full_real * weight).astype(bf16).astype(f32)
        w_imag = (full_imag * weight).astype(bf16).astype(f32)
        prod_real = (spec_real * w_real + spec_imag * w_imag).astype(bf16)
        prod_imag = (spec_imag * w_real - spec_real * w_imag).astype(bf16)
        left_real = (
            jnp.einsum("rp,opq->orq", row_cos, prod_real, preferred_element_type=f32)
            - jnp.einsum("rp,opq->orq", row_sin, prod_imag, preferred_element_type=f32)
        ).astype(bf16)
        left_imag = (
            jnp.einsum("rp,opq->orq", row_cos, prod_imag, preferred_element_type=f32)
            + jnp.einsum("rp,opq->orq", row_sin, prod_real, preferred_element_type=f32)
        ).astype(bf16)
        corr = jnp.einsum("orq,cq->orc", left_real, row_cos, preferred_element_type=f32) - jnp.einsum(
            "orq,cq->orc", left_imag, row_sin, preferred_element_type=f32
        )
        corr = corr * scaling
        return (jnp.max(corr, axis=0), jnp.sum(corr, axis=0), jnp.sum(corr * corr, axis=0))

    chunk = min(CHUNK, total)
    n_chunks = total // chunk
    if n_chunks == 1:
        peak_map, sum_map, squares = chunk_stats(all_templates, all_ids)
    else:

        def step(index, tallies):
            start = index * chunk
            part_templates = lax.dynamic_slice_in_dim(all_templates, start, chunk, 0)
            part_ids = lax.dynamic_slice_in_dim(all_ids, start, chunk, 0)
            peak_c, sum_c, sq_c = chunk_stats(part_templates, part_ids)
            return (jnp.maximum(tallies[0], peak_c), tallies[1] + sum_c, tallies[2] + sq_c)

        shape = (tile_width, tile_width)
        initial = (jnp.full(shape, -jnp.inf, f32), jnp.zeros(shape, f32), jnp.zeros(shape, f32))
        peak_map, sum_map, squares = lax.fori_loop(0, n_chunks, step, initial)

    live = usable[0, 0]
    row_mask = (jnp.arange(tile_width, dtype=jnp.int32) < RB * live)[:, None]
    orient_count = float(total)
    peak_out = jnp.where(row_mask, peak_map, 0.0)
    mean_out = jnp.where(row_mask, sum_map / orient_count, 0.0)
    square_out = jnp.where(row_mask, squares / orient_count, 0.0)
    return (peak_out, mean_out, square_out)


def solution(mesh):
    return jax.shard_map(
        body,
        mesh=mesh,
        in_specs=(
            P(("groups", "orient"), "tile"),
            P("orient", None, None),
            P(("groups", "orient")),
            P("groups", None, None),
            P(("groups", "orient"), "tile"),
        ),
        out_specs=(
            P(("groups", "orient"), "tile"),
            P(("groups", "orient"), "tile"),
            P(("groups", "orient"), "tile"),
        ),
        check_vma=False,
    )
```

```python
import math

import jax
import jax.numpy as jnp
import ml_dtypes
import numpy as np
from jax import lax
from jax.sharding import PartitionSpec as P

RB = 32
CHUNK = 8


def twiddles(padded_size):
    position = np.arange(padded_size, dtype=np.int64)
    phase_index = (position[:, None] * position[None, :]) % padded_size
    angles = phase_index.astype(np.float32) * np.float32(2.0 * math.pi / padded_size)
    angles = angles.astype(np.float64)
    cosines = np.cos(angles).astype(np.float32).astype(ml_dtypes.bfloat16)
    sines = np.sin(angles).astype(np.float32).astype(ml_dtypes.bfloat16)
    return cosines, sines


def matmul(left, right):
    return jnp.dot(left, right, preferred_element_type=jnp.float32)


def halo_window(block, width):
    rows, cols = block.shape
    count_o = lax.axis_size("orient")
    count_t = lax.axis_size("tile")
    axes = ("orient", "tile")
    row_part = {-1: slice(rows - width, rows), 0: slice(0, rows), 1: slice(0, width)}
    col_part = {-1: slice(cols - width, cols), 0: slice(0, cols), 1: slice(0, width)}
    grid = []
    for d_o in (-1, 0, 1):
        line = []
        for d_t in (-1, 0, 1):
            piece = block[row_part[d_o], col_part[d_t]]
            if d_o or d_t:
                pairs = []
                for o in range(count_o):
                    for t in range(count_t):
                        so, st = o + d_o, t + d_t
                        if 0 <= so < count_o and 0 <= st < count_t:
                            pairs.append((so * count_t + st, o * count_t + t))
                piece = lax.ppermute(piece, axes, pairs)
            line.append(piece)
        grid.append(jnp.concatenate(line, axis=1))
    return jnp.concatenate(grid, axis=0)


def exchange_orient(block):
    size = lax.axis_size("orient")
    if size <= 8:
        pieces = [block]
        for shift in range(1, size):
            pieces.append(lax.ppermute(block, "orient", [(i, (i + shift) % size) for i in range(size)]))
        return jnp.concatenate(pieces, axis=0)
    step = 1
    while step < size:
        other = lax.ppermute(block, "orient", [(i, i ^ step) for i in range(size)])
        block = jnp.concatenate([block, other], axis=0)
        step *= 2
    return block


def body(micrograph, templates, defocus, ctf, usable):
    bf16 = jnp.bfloat16
    f32 = jnp.float32
    tile_width = micrograph.shape[0]
    padded_size = ctf.shape[1]
    box_size = templates.shape[1]
    margin = (padded_size - tile_width) // 2
    scaling = 1.0 / (padded_size * padded_size)
    n = padded_size
    cos_np, sin_np = twiddles(n)

    cos_full, sin_full = lax.optimization_barrier((jnp.asarray(cos_np), jnp.asarray(sin_np)))
    low = n - box_size // 2
    cos_rows = jnp.concatenate([cos_full[low:], cos_full[: box_size - (n - low)]], axis=0)
    sin_rows = jnp.concatenate([sin_full[low:], sin_full[: box_size - (n - low)]], axis=0)
    cos_cols = cos_rows.T
    sin_cols = sin_rows.T
    row_cos = cos_full[margin : margin + tile_width]
    row_sin = sin_full[margin : margin + tile_width]
    col_cos = row_cos.T
    col_sin = row_sin.T

    local_count = templates.shape[0]
    flat_size = box_size * box_size
    id_block = jnp.broadcast_to(defocus.astype(bf16)[:, None], (local_count, 128))
    packed = jnp.concatenate([templates.reshape(local_count, flat_size), id_block], axis=1)
    gathered = exchange_orient(packed)
    total = gathered.shape[0]
    all_templates = gathered[:, :flat_size].reshape(total, box_size, box_size)
    all_ids = gathered[:, flat_size].astype(jnp.int32)

    padded = halo_window(micrograph, margin)
    half_real = matmul(padded, cos_full).astype(bf16)
    half_imag = (-matmul(padded, sin_full)).astype(bf16)
    spec_real = (matmul(cos_full, half_real) + matmul(sin_full, half_imag)).astype(bf16).astype(f32)
    spec_imag = (matmul(cos_full, half_imag) - matmul(sin_full, half_real)).astype(bf16).astype(f32)
    spec_real = spec_real[:, None, :]
    spec_imag = spec_imag[:, None, :]

    def chunk_stats(chunk_templates, chunk_ids):
        count = chunk_templates.shape[0]
        stacked = jnp.transpose(chunk_templates, (1, 0, 2)).reshape(box_size * count, box_size)
        part_real = matmul(stacked, cos_rows).astype(bf16).reshape(box_size, count * n)
        part_imag = (-matmul(stacked, sin_rows)).astype(bf16).reshape(box_size, count * n)
        full_real = (matmul(cos_cols, part_real) + matmul(sin_cols, part_imag)).reshape(n, count, n)
        full_imag = (matmul(cos_cols, part_imag) - matmul(sin_cols, part_real)).reshape(n, count, n)
        weight = jnp.stack(
            [lax.dynamic_index_in_dim(ctf, chunk_ids[o], 0, keepdims=False) for o in range(count)], axis=1
        )
        w_real = (full_real * weight).astype(bf16).astype(f32)
        w_imag = (full_imag * weight).astype(bf16).astype(f32)
        prod_real = (spec_real * w_real + spec_imag * w_imag).astype(bf16).reshape(n, count * n)
        prod_imag = (spec_imag * w_real - spec_real * w_imag).astype(bf16).reshape(n, count * n)
        left_real = (matmul(row_cos, prod_real) - matmul(row_sin, prod_imag)).astype(bf16)
        left_imag = (matmul(row_cos, prod_imag) + matmul(row_sin, prod_real)).astype(bf16)
        left_real = left_real.reshape(tile_width * count, n)
        left_imag = left_imag.reshape(tile_width * count, n)
        corr = (matmul(left_real, col_cos) - matmul(left_imag, col_sin)) * scaling
        corr = corr.reshape(tile_width, count, tile_width)
        return (jnp.max(corr, axis=1), jnp.sum(corr, axis=1), jnp.sum(corr * corr, axis=1))

    chunk = min(CHUNK, total)
    n_chunks = total // chunk
    if n_chunks == 1:
        peak_map, sum_map, squares = chunk_stats(all_templates, all_ids)
    else:

        def step(index, tallies):
            start = index * chunk
            part_templates = lax.dynamic_slice_in_dim(all_templates, start, chunk, 0)
            part_ids = lax.dynamic_slice_in_dim(all_ids, start, chunk, 0)
            peak_c, sum_c, sq_c = chunk_stats(part_templates, part_ids)
            return (jnp.maximum(tallies[0], peak_c), tallies[1] + sum_c, tallies[2] + sq_c)

        shape = (tile_width, tile_width)
        initial = (jnp.full(shape, -jnp.inf, f32), jnp.zeros(shape, f32), jnp.zeros(shape, f32))
        peak_map, sum_map, squares = lax.fori_loop(0, n_chunks, step, initial)

    live = usable[0, 0]
    row_mask = (jnp.arange(tile_width, dtype=jnp.int32) < RB * live)[:, None]
    orient_count = float(total)
    peak_out = jnp.where(row_mask, peak_map, 0.0)
    mean_out = jnp.where(row_mask, sum_map / orient_count, 0.0)
    square_out = jnp.where(row_mask, squares / orient_count, 0.0)
    return (peak_out, mean_out, square_out)


def solution(mesh):
    return jax.shard_map(
        body,
        mesh=mesh,
        in_specs=(
            P(("groups", "orient"), "tile"),
            P("orient", None, None),
            P(("groups", "orient")),
            P("groups", None, None),
            P(("groups", "orient"), "tile"),
        ),
        out_specs=(
            P(("groups", "orient"), "tile"),
            P(("groups", "orient"), "tile"),
            P(("groups", "orient"), "tile"),
        ),
        check_vma=False,
    )
```

```python
import math

import jax
import jax.numpy as jnp
import ml_dtypes
import numpy as np
from jax import lax
from jax.sharding import PartitionSpec as P

RB = 32
CHUNK = 8


def extended(block, sides, width):
    for axis, dim in sides:
        count = lax.axis_size(axis)
        forward = [(i, i + 1) for i in range(count - 1)]
        backward = [(target, source) for source, target in forward]
        low = lax.ppermute(
            lax.slice_in_dim(block, block.shape[dim] - width, None, axis=dim), axis, forward
        )
        high = lax.ppermute(lax.slice_in_dim(block, 0, width, axis=dim), axis, backward)
        block = jnp.concatenate([low, block, high], axis=dim)
    return block


def twiddles(padded_size):
    position = np.arange(padded_size, dtype=np.int64)
    phase_index = (position[:, None] * position[None, :]) % padded_size
    angles = phase_index.astype(np.float32) * np.float32(2.0 * math.pi / padded_size)
    angles = angles.astype(np.float64)
    cosines = np.cos(angles).astype(np.float32).astype(ml_dtypes.bfloat16)
    sines = np.sin(angles).astype(np.float32).astype(ml_dtypes.bfloat16)
    return cosines, sines


def matmul(left, right):
    return jnp.dot(left, right, preferred_element_type=jnp.float32)


def exchange_rounds(block):
    size = lax.axis_size("orient")
    rounds = [block]
    step = 1
    while step * 2 < size:
        step *= 2
    held = block
    while step >= 1:
        other = lax.ppermute(held, "orient", [(i, i ^ step) for i in range(size)])
        rounds.append(other)
        held = jnp.concatenate([held, other], axis=0)
        step //= 2
    return rounds


def body(micrograph, templates, defocus, ctf, usable):
    bf16 = jnp.bfloat16
    f32 = jnp.float32
    tile_width = micrograph.shape[0]
    padded_size = ctf.shape[1]
    box_size = templates.shape[1]
    margin = (padded_size - tile_width) // 2
    scaling = 1.0 / (padded_size * padded_size)
    n = padded_size
    cos_np, sin_np = twiddles(n)

    cos_full, sin_full = lax.optimization_barrier((jnp.asarray(cos_np), jnp.asarray(sin_np)))
    low = n - box_size // 2
    cos_rows = jnp.concatenate([cos_full[low:], cos_full[: box_size - (n - low)]], axis=0)
    sin_rows = jnp.concatenate([sin_full[low:], sin_full[: box_size - (n - low)]], axis=0)
    cos_cols = cos_rows.T
    sin_cols = sin_rows.T
    row_cos = cos_full[margin : margin + tile_width]
    row_sin = sin_full[margin : margin + tile_width]
    col_cos = row_cos.T
    col_sin = row_sin.T

    local_count = templates.shape[0]
    flat_size = box_size * box_size
    id_block = jnp.broadcast_to(defocus.astype(bf16)[:, None], (local_count, 128))
    packed = jnp.concatenate([templates.reshape(local_count, flat_size), id_block], axis=1)
    arrivals = exchange_rounds(packed)
    total = sum(piece.shape[0] for piece in arrivals)

    padded = extended(micrograph, (("orient", 0), ("tile", 1)), margin)
    half_real = matmul(padded, cos_full).astype(bf16)
    half_imag = (-matmul(padded, sin_full)).astype(bf16)
    spec_real = (matmul(cos_full, half_real) + matmul(sin_full, half_imag)).astype(bf16).astype(f32)
    spec_imag = (matmul(cos_full, half_imag) - matmul(sin_full, half_real)).astype(bf16).astype(f32)

    def batched(shared, count):
        return jnp.broadcast_to(shared[None], (count,) + shared.shape)

    def chunk_stats(chunk):
        count = chunk.shape[0]
        chunk_templates = chunk[:, :flat_size].reshape(count, box_size, box_size)
        chunk_ids = chunk[:, flat_size].astype(jnp.int32)
        part_real = jnp.einsum("okj,jq->okq", chunk_templates, cos_rows, preferred_element_type=f32).astype(bf16)
        part_imag = (-jnp.einsum("okj,jq->okq", chunk_templates, sin_rows, preferred_element_type=f32)).astype(bf16)
        left_c = batched(cos_cols, count)
        left_s = batched(sin_cols, count)
        full_real = jnp.einsum("opk,okq->opq", left_c, part_real, preferred_element_type=f32) + jnp.einsum(
            "opk,okq->opq", left_s, part_imag, preferred_element_type=f32
        )
        full_imag = jnp.einsum("opk,okq->opq", left_c, part_imag, preferred_element_type=f32) - jnp.einsum(
            "opk,okq->opq", left_s, part_real, preferred_element_type=f32
        )
        weight = jnp.stack([lax.dynamic_index_in_dim(ctf, chunk_ids[o], 0, keepdims=False) for o in range(count)])
        w_real = (full_real * weight).astype(bf16).astype(f32)
        w_imag = (full_imag * weight).astype(bf16).astype(f32)
        prod_real = (spec_real * w_real + spec_imag * w_imag).astype(bf16)
        prod_imag = (spec_imag * w_real - spec_real * w_imag).astype(bf16)
        rc = batched(row_cos, count)
        rs = batched(row_sin, count)
        left_real = (
            jnp.einsum("orp,opq->orq", rc, prod_real, preferred_element_type=f32)
            - jnp.einsum("orp,opq->orq", rs, prod_imag, preferred_element_type=f32)
        ).astype(bf16)
        left_imag = (
            jnp.einsum("orp,opq->orq", rc, prod_imag, preferred_element_type=f32)
            + jnp.einsum("orp,opq->orq", rs, prod_real, preferred_element_type=f32)
        ).astype(bf16)
        corr = jnp.einsum("orq,qc->orc", left_real, col_cos, preferred_element_type=f32) - jnp.einsum(
            "orq,qc->orc", left_imag, col_sin, preferred_element_type=f32
        )
        corr = corr * scaling
        return (jnp.max(corr, axis=0), jnp.sum(corr, axis=0), jnp.sum(corr * corr, axis=0))

    peak_map = sum_map = squares = None
    for piece in arrivals:
        for start in range(0, piece.shape[0], CHUNK):
            stats = chunk_stats(piece[start : start + CHUNK])
            if peak_map is None:
                peak_map, sum_map, squares = stats
            else:
                peak_map = jnp.maximum(peak_map, stats[0])
                sum_map = sum_map + stats[1]
                squares = squares + stats[2]

    live = usable[0, 0]
    row_mask = (jnp.arange(tile_width, dtype=jnp.int32) < RB * live)[:, None]
    orient_count = float(total)
    peak_out = jnp.where(row_mask, peak_map, 0.0)
    mean_out = jnp.where(row_mask, sum_map / orient_count, 0.0)
    square_out = jnp.where(row_mask, squares / orient_count, 0.0)
    return (peak_out, mean_out, square_out)


def solution(mesh):
    return jax.shard_map(
        body,
        mesh=mesh,
        in_specs=(
            P(("groups", "orient"), "tile"),
            P("orient", None, None),
            P(("groups", "orient")),
            P("groups", None, None),
            P(("groups", "orient"), "tile"),
        ),
        out_specs=(
            P(("groups", "orient"), "tile"),
            P(("groups", "orient"), "tile"),
            P(("groups", "orient"), "tile"),
        ),
        check_vma=False,
    )
```

```python
import math

import jax
import jax.numpy as jnp
import ml_dtypes
import numpy as np
from jax import lax
from jax.sharding import PartitionSpec as P

RB = 32
CHUNK = 8


def extended(block, sides, width):
    for axis, dim in sides:
        count = lax.axis_size(axis)
        forward = [(i, i + 1) for i in range(count - 1)]
        backward = [(target, source) for source, target in forward]
        low = lax.ppermute(
            lax.slice_in_dim(block, block.shape[dim] - width, None, axis=dim), axis, forward
        )
        high = lax.ppermute(lax.slice_in_dim(block, 0, width, axis=dim), axis, backward)
        block = jnp.concatenate([low, block, high], axis=dim)
    return block


def twiddles(padded_size):
    position = np.arange(padded_size, dtype=np.int64)
    phase_index = (position[:, None] * position[None, :]) % padded_size
    angles = phase_index.astype(np.float32) * np.float32(2.0 * math.pi / padded_size)
    angles = angles.astype(np.float64)
    cosines = np.cos(angles).astype(np.float32).astype(ml_dtypes.bfloat16)
    sines = np.sin(angles).astype(np.float32).astype(ml_dtypes.bfloat16)
    return cosines, sines


def matmul(left, right):
    return jnp.dot(left, right, preferred_element_type=jnp.float32)


def exchange_rounds(block):
    size = lax.axis_size("orient")
    step = 1
    while step * 2 < size:
        step *= 2
    rounds = [block]
    held = block
    while step >= 1:
        other = lax.ppermute(held, "orient", [(i, i ^ step) for i in range(size)])
        if step > 1:
            other, rounds[-1] = lax.optimization_barrier((other, rounds[-1]))
        rounds.append(other)
        held = jnp.concatenate([held, other], axis=0)
        step //= 2
    return rounds


def body(micrograph, templates, defocus, ctf, usable):
    bf16 = jnp.bfloat16
    f32 = jnp.float32
    tile_width = micrograph.shape[0]
    padded_size = ctf.shape[1]
    box_size = templates.shape[1]
    margin = (padded_size - tile_width) // 2
    scaling = 1.0 / (padded_size * padded_size)
    n = padded_size
    cos_np, sin_np = twiddles(n)

    cos_full, sin_full = lax.optimization_barrier((jnp.asarray(cos_np), jnp.asarray(sin_np)))
    low = n - box_size // 2
    cos_rows = jnp.concatenate([cos_full[low:], cos_full[: box_size - (n - low)]], axis=0)
    sin_rows = jnp.concatenate([sin_full[low:], sin_full[: box_size - (n - low)]], axis=0)
    cos_cols = cos_rows.T
    sin_cols = sin_rows.T
    row_cos = cos_full[margin : margin + tile_width]
    row_sin = sin_full[margin : margin + tile_width]
    col_cos = row_cos.T
    col_sin = row_sin.T

    local_count = templates.shape[0]
    flat_size = box_size * box_size
    id_block = jnp.broadcast_to(defocus.astype(bf16)[:, None], (local_count, 128))
    packed = jnp.concatenate([templates.reshape(local_count, flat_size), id_block], axis=1)
    arrivals = exchange_rounds(packed)
    total = sum(piece.shape[0] for piece in arrivals)

    padded = extended(micrograph, (("orient", 0), ("tile", 1)), margin)
    half_real = matmul(padded, cos_full).astype(bf16)
    half_imag = (-matmul(padded, sin_full)).astype(bf16)
    spec_real = (matmul(cos_full, half_real) + matmul(sin_full, half_imag)).astype(bf16).astype(f32)
    spec_imag = (matmul(cos_full, half_imag) - matmul(sin_full, half_real)).astype(bf16).astype(f32)

    def batched(shared, count):
        return jnp.broadcast_to(shared[None], (count,) + shared.shape)

    def chunk_stats(chunk):
        count = chunk.shape[0]
        chunk_templates = chunk[:, :flat_size].reshape(count, box_size, box_size)
        chunk_ids = chunk[:, flat_size].astype(jnp.int32)
        part_real = jnp.einsum("okj,jq->okq", chunk_templates, cos_rows, preferred_element_type=f32).astype(bf16)
        part_imag = (-jnp.einsum("okj,jq->okq", chunk_templates, sin_rows, preferred_element_type=f32)).astype(bf16)
        left_c = batched(cos_cols, count)
        left_s = batched(sin_cols, count)
        full_real = jnp.einsum("opk,okq->opq", left_c, part_real, preferred_element_type=f32) + jnp.einsum(
            "opk,okq->opq", left_s, part_imag, preferred_element_type=f32
        )
        full_imag = jnp.einsum("opk,okq->opq", left_c, part_imag, preferred_element_type=f32) - jnp.einsum(
            "opk,okq->opq", left_s, part_real, preferred_element_type=f32
        )
        weight = jnp.stack([lax.dynamic_index_in_dim(ctf, chunk_ids[o], 0, keepdims=False) for o in range(count)])
        w_real = (full_real * weight).astype(bf16).astype(f32)
        w_imag = (full_imag * weight).astype(bf16).astype(f32)
        prod_real = (spec_real * w_real + spec_imag * w_imag).astype(bf16)
        prod_imag = (spec_imag * w_real - spec_real * w_imag).astype(bf16)
        rc = batched(row_cos, count)
        rs = batched(row_sin, count)
        left_real = (
            jnp.einsum("orp,opq->orq", rc, prod_real, preferred_element_type=f32)
            - jnp.einsum("orp,opq->orq", rs, prod_imag, preferred_element_type=f32)
        ).astype(bf16)
        left_imag = (
            jnp.einsum("orp,opq->orq", rc, prod_imag, preferred_element_type=f32)
            + jnp.einsum("orp,opq->orq", rs, prod_real, preferred_element_type=f32)
        ).astype(bf16)
        corr = jnp.einsum("orq,qc->orc", left_real, col_cos, preferred_element_type=f32) - jnp.einsum(
            "orq,qc->orc", left_imag, col_sin, preferred_element_type=f32
        )
        corr = corr * scaling
        return (jnp.max(corr, axis=0), jnp.sum(corr, axis=0), jnp.sum(corr * corr, axis=0))

    peak_map = sum_map = squares = None
    for piece in arrivals:
        for start in range(0, piece.shape[0], CHUNK):
            stats = chunk_stats(piece[start : start + CHUNK])
            if peak_map is None:
                peak_map, sum_map, squares = stats
            else:
                peak_map = jnp.maximum(peak_map, stats[0])
                sum_map = sum_map + stats[1]
                squares = squares + stats[2]

    live = usable[0, 0]
    row_mask = (jnp.arange(tile_width, dtype=jnp.int32) < RB * live)[:, None]
    orient_count = float(total)
    peak_out = jnp.where(row_mask, peak_map, 0.0)
    mean_out = jnp.where(row_mask, sum_map / orient_count, 0.0)
    square_out = jnp.where(row_mask, squares / orient_count, 0.0)
    return (peak_out, mean_out, square_out)


def solution(mesh):
    return jax.shard_map(
        body,
        mesh=mesh,
        in_specs=(
            P(("groups", "orient"), "tile"),
            P("orient", None, None),
            P(("groups", "orient")),
            P("groups", None, None),
            P(("groups", "orient"), "tile"),
        ),
        out_specs=(
            P(("groups", "orient"), "tile"),
            P(("groups", "orient"), "tile"),
            P(("groups", "orient"), "tile"),
        ),
        check_vma=False,
    )
```

```python
import functools
import math

import jax
import jax.numpy as jnp
import ml_dtypes
import numpy as np
from jax import lax
from jax.experimental import pallas as pl
from jax.experimental.pallas import tpu as pltpu
from jax.sharding import PartitionSpec as P

RB = 32
CHUNK = 8


def extended(block, sides, width):
    for axis, dim in sides:
        count = lax.axis_size(axis)
        forward = [(i, i + 1) for i in range(count - 1)]
        backward = [(target, source) for source, target in forward]
        low = lax.ppermute(
            lax.slice_in_dim(block, block.shape[dim] - width, None, axis=dim), axis, forward
        )
        high = lax.ppermute(lax.slice_in_dim(block, 0, width, axis=dim), axis, backward)
        block = jnp.concatenate([low, block, high], axis=dim)
    return block


def twiddles(padded_size):
    position = np.arange(padded_size, dtype=np.int64)
    phase_index = (position[:, None] * position[None, :]) % padded_size
    angles = phase_index.astype(np.float32) * np.float32(2.0 * math.pi / padded_size)
    angles = angles.astype(np.float64)
    cosines = np.cos(angles).astype(np.float32).astype(ml_dtypes.bfloat16)
    sines = np.sin(angles).astype(np.float32).astype(ml_dtypes.bfloat16)
    return cosines, sines


def matmul(left, right):
    return jnp.dot(left, right, preferred_element_type=jnp.float32)


def gather_orient(block):
    size = lax.axis_size("orient")
    index = lax.axis_index("orient")
    step = 1
    while step < size:
        pairs = [(i, i ^ step) for i in range(size) if (i ^ step) < size]
        other = lax.ppermute(block, "orient", pairs)
        low_side = (index // step) % 2 == 0
        block = jnp.where(low_side, jnp.concatenate([block, other], 0), jnp.concatenate([other, block], 0))
        step *= 2
    return block


def correlate_kernel(ids_ref, tmpl_ref, ctf_ref, spec_r_ref, spec_i_ref, cos_rows_ref, sin_rows_ref,
                     cos_cols_ref, sin_cols_ref, row_cos_ref, row_sin_ref, col_cos_ref, col_sin_ref,
                     peak_ref, sum_ref, sq_ref, *, scaling):
    bf16 = jnp.bfloat16
    f32 = jnp.float32
    o = pl.program_id(0)

    def mm(a, b):
        return jnp.dot(a, b, preferred_element_type=f32)

    template = tmpl_ref[0]
    part_real = mm(template, cos_rows_ref[...]).astype(bf16)
    part_imag = (-mm(template, sin_rows_ref[...])).astype(bf16)
    cos_cols = cos_cols_ref[...]
    sin_cols = sin_cols_ref[...]
    full_real = mm(cos_cols, part_real) + mm(sin_cols, part_imag)
    full_imag = mm(cos_cols, part_imag) - mm(sin_cols, part_real)
    weight = ctf_ref[0]
    w_real = (full_real * weight).astype(bf16).astype(f32)
    w_imag = (full_imag * weight).astype(bf16).astype(f32)
    spec_real = spec_r_ref[...]
    spec_imag = spec_i_ref[...]
    prod_real = (spec_real * w_real + spec_imag * w_imag).astype(bf16)
    prod_imag = (spec_imag * w_real - spec_real * w_imag).astype(bf16)
    row_cos = row_cos_ref[...]
    row_sin = row_sin_ref[...]
    left_real = (mm(row_cos, prod_real) - mm(row_sin, prod_imag)).astype(bf16)
    left_imag = (mm(row_cos, prod_imag) + mm(row_sin, prod_real)).astype(bf16)
    corr = (mm(left_real, col_cos_ref[...]) - mm(left_imag, col_sin_ref[...])) * scaling

    @pl.when(o == 0)
    def _():
        peak_ref[...] = corr
        sum_ref[...] = corr
        sq_ref[...] = corr * corr

    @pl.when(o > 0)
    def _():
        peak_ref[...] = jnp.maximum(peak_ref[...], corr)
        sum_ref[...] = sum_ref[...] + corr
        sq_ref[...] = sq_ref[...] + corr * corr


def correlate(ids, all_templates, ctf, spec_real, spec_imag, tables, scaling):
    count, box, _ = all_templates.shape
    n = ctf.shape[1]
    tile = tables[4].shape[0]
    full = lambda shape: pl.BlockSpec(shape, lambda o, ids: (0,) * len(shape))
    in_specs = [
        pl.BlockSpec((1, box, box), lambda o, ids: (o, 0, 0)),
        pl.BlockSpec((1, n, n), lambda o, ids: (ids[o], 0, 0)),
        full((n, n)),
        full((n, n)),
    ] + [full(t.shape) for t in tables]
    out_block = full((tile, tile))
    grid_spec = pltpu.PrefetchScalarGridSpec(
        num_scalar_prefetch=1,
        grid=(count,),
        in_specs=in_specs,
        out_specs=[out_block, out_block, out_block],
    )
    out_shape = [jax.ShapeDtypeStruct((tile, tile), jnp.float32)] * 3
    return pl.pallas_call(
        functools.partial(correlate_kernel, scaling=scaling),
        grid_spec=grid_spec,
        out_shape=out_shape,
        compiler_params=pltpu.CompilerParams(dimension_semantics=("arbitrary",)),
    )(ids, all_templates, ctf, spec_real, spec_imag, *tables)


def body(micrograph, templates, defocus, ctf, usable):
    bf16 = jnp.bfloat16
    f32 = jnp.float32
    tile_width = micrograph.shape[0]
    padded_size = ctf.shape[1]
    box_size = templates.shape[1]
    margin = (padded_size - tile_width) // 2
    scaling = 1.0 / (padded_size * padded_size)
    n = padded_size
    cos_np, sin_np = twiddles(n)

    cos_full, sin_full = lax.optimization_barrier((jnp.asarray(cos_np), jnp.asarray(sin_np)))
    low = n - box_size // 2
    cos_rows = jnp.concatenate([cos_full[low:], cos_full[: box_size - (n - low)]], axis=0)
    sin_rows = jnp.concatenate([sin_full[low:], sin_full[: box_size - (n - low)]], axis=0)
    cos_cols = cos_rows.T
    sin_cols = sin_rows.T
    row_cos = cos_full[margin : margin + tile_width]
    row_sin = sin_full[margin : margin + tile_width]
    col_cos = row_cos.T
    col_sin = row_sin.T

    local_count = templates.shape[0]
    flat_size = box_size * box_size
    id_block = jnp.broadcast_to(defocus.astype(bf16)[:, None], (local_count, 128))
    packed = jnp.concatenate([templates.reshape(local_count, flat_size), id_block], axis=1)
    gathered = gather_orient(packed)
    total = gathered.shape[0]
    all_templates = gathered[:, :flat_size].reshape(total, box_size, box_size)
    all_ids = gathered[:, flat_size].astype(jnp.int32)

    padded = extended(micrograph, (("orient", 0), ("tile", 1)), margin)
    half_real = matmul(padded, cos_full).astype(bf16)
    half_imag = (-matmul(padded, sin_full)).astype(bf16)
    spec_real = (matmul(cos_full, half_real) + matmul(sin_full, half_imag)).astype(bf16).astype(f32)
    spec_imag = (matmul(cos_full, half_imag) - matmul(sin_full, half_real)).astype(bf16).astype(f32)

    tables = (cos_rows, sin_rows, cos_cols, sin_cols, row_cos, row_sin, col_cos, col_sin)
    peak_map, sum_map, squares = correlate(all_ids, all_templates, ctf, spec_real, spec_imag, tables, scaling)

    live = usable[0, 0]
    row_mask = (jnp.arange(tile_width, dtype=jnp.int32) < RB * live)[:, None]
    orient_count = float(total)
    peak_out = jnp.where(row_mask, peak_map, 0.0)
    mean_out = jnp.where(row_mask, sum_map / orient_count, 0.0)
    square_out = jnp.where(row_mask, squares / orient_count, 0.0)
    return (peak_out, mean_out, square_out)


def solution(mesh):
    return jax.shard_map(
        body,
        mesh=mesh,
        in_specs=(
            P(("groups", "orient"), "tile"),
            P("orient", None, None),
            P(("groups", "orient")),
            P("groups", None, None),
            P(("groups", "orient"), "tile"),
        ),
        out_specs=(
            P(("groups", "orient"), "tile"),
            P(("groups", "orient"), "tile"),
            P(("groups", "orient"), "tile"),
        ),
        check_vma=False,
    )
```

```python
import functools
import math

import jax
import jax.numpy as jnp
import ml_dtypes
import numpy as np
from jax import lax
from jax.experimental import pallas as pl
from jax.experimental.pallas import tpu as pltpu
from jax.sharding import PartitionSpec as P

RB = 32
CHUNK = 8


def extended(block, sides, width):
    for axis, dim in sides:
        count = lax.axis_size(axis)
        forward = [(i, i + 1) for i in range(count - 1)]
        backward = [(target, source) for source, target in forward]
        low = lax.ppermute(
            lax.slice_in_dim(block, block.shape[dim] - width, None, axis=dim), axis, forward
        )
        high = lax.ppermute(lax.slice_in_dim(block, 0, width, axis=dim), axis, backward)
        block = jnp.concatenate([low, block, high], axis=dim)
    return block


def twiddles(padded_size):
    position = np.arange(padded_size, dtype=np.int64)
    phase_index = (position[:, None] * position[None, :]) % padded_size
    angles = phase_index.astype(np.float32) * np.float32(2.0 * math.pi / padded_size)
    angles = angles.astype(np.float64)
    cosines = np.cos(angles).astype(np.float32).astype(ml_dtypes.bfloat16)
    sines = np.sin(angles).astype(np.float32).astype(ml_dtypes.bfloat16)
    return cosines, sines


def matmul(left, right):
    return jnp.dot(left, right, preferred_element_type=jnp.float32)


def exchange_rounds(block):
    size = lax.axis_size("orient")
    step = 1
    while step * 2 < size:
        step *= 2
    rounds = [block]
    held = block
    while step >= 1:
        other = lax.ppermute(held, "orient", [(i, i ^ step) for i in range(size)])
        if len(rounds) > 1:
            other, rounds[-1] = lax.optimization_barrier((other, rounds[-1]))
        rounds.append(other)
        held = jnp.concatenate([held, other], axis=0)
        step //= 2
    return rounds


def correlate_kernel(ids_ref, tmpl_ref, ctf_ref, spec_r_ref, spec_i_ref, cos_rows_ref, sin_rows_ref,
                     cos_cols_ref, sin_cols_ref, row_cos_ref, row_sin_ref, col_cos_ref, col_sin_ref,
                     prev_peak_ref, prev_sum_ref, prev_sq_ref, peak_ref, sum_ref, sq_ref, *, scaling):
    bf16 = jnp.bfloat16
    f32 = jnp.float32
    o = pl.program_id(0)

    def mm(a, b):
        return jnp.dot(a, b, preferred_element_type=f32)

    template = tmpl_ref[0]
    part_real = mm(template, cos_rows_ref[...]).astype(bf16)
    part_imag = (-mm(template, sin_rows_ref[...])).astype(bf16)
    cos_cols = cos_cols_ref[...]
    sin_cols = sin_cols_ref[...]
    full_real = mm(cos_cols, part_real) + mm(sin_cols, part_imag)
    full_imag = mm(cos_cols, part_imag) - mm(sin_cols, part_real)
    weight = ctf_ref[0]
    w_real = (full_real * weight).astype(bf16).astype(f32)
    w_imag = (full_imag * weight).astype(bf16).astype(f32)
    spec_real = spec_r_ref[...]
    spec_imag = spec_i_ref[...]
    prod_real = (spec_real * w_real + spec_imag * w_imag).astype(bf16)
    prod_imag = (spec_imag * w_real - spec_real * w_imag).astype(bf16)
    row_cos = row_cos_ref[...]
    row_sin = row_sin_ref[...]
    left_real = (mm(row_cos, prod_real) - mm(row_sin, prod_imag)).astype(bf16)
    left_imag = (mm(row_cos, prod_imag) + mm(row_sin, prod_real)).astype(bf16)
    corr = (mm(left_real, col_cos_ref[...]) - mm(left_imag, col_sin_ref[...])) * scaling

    @pl.when(o == 0)
    def _():
        peak_ref[...] = jnp.maximum(prev_peak_ref[...], corr)
        sum_ref[...] = prev_sum_ref[...] + corr
        sq_ref[...] = prev_sq_ref[...] + corr * corr

    @pl.when(o > 0)
    def _():
        peak_ref[...] = jnp.maximum(peak_ref[...], corr)
        sum_ref[...] = sum_ref[...] + corr
        sq_ref[...] = sq_ref[...] + corr * corr


def correlate(ids, all_templates, ctf, spec_real, spec_imag, tables, scaling, previous):
    count, box, _ = all_templates.shape
    n = ctf.shape[1]
    tile = tables[4].shape[0]
    full = lambda shape: pl.BlockSpec(shape, lambda o, ids: (0,) * len(shape))
    in_specs = [
        pl.BlockSpec((1, box, box), lambda o, ids: (o, 0, 0)),
        pl.BlockSpec((1, n, n), lambda o, ids: (ids[o], 0, 0)),
        full((n, n)),
        full((n, n)),
    ] + [full(t.shape) for t in tables] + [full((tile, tile))] * 3
    out_block = full((tile, tile))
    grid_spec = pltpu.PrefetchScalarGridSpec(
        num_scalar_prefetch=1,
        grid=(count,),
        in_specs=in_specs,
        out_specs=[out_block, out_block, out_block],
    )
    out_shape = [jax.ShapeDtypeStruct((tile, tile), jnp.float32)] * 3
    return pl.pallas_call(
        functools.partial(correlate_kernel, scaling=scaling),
        grid_spec=grid_spec,
        out_shape=out_shape,
        compiler_params=pltpu.CompilerParams(dimension_semantics=("arbitrary",)),
        input_output_aliases={5 + len(tables): 0, 6 + len(tables): 1, 7 + len(tables): 2},
    )(ids, all_templates, ctf, spec_real, spec_imag, *tables, *previous)


def body(micrograph, templates, defocus, ctf, usable):
    bf16 = jnp.bfloat16
    f32 = jnp.float32
    tile_width = micrograph.shape[0]
    padded_size = ctf.shape[1]
    box_size = templates.shape[1]
    margin = (padded_size - tile_width) // 2
    scaling = 1.0 / (padded_size * padded_size)
    n = padded_size
    cos_np, sin_np = twiddles(n)

    cos_full, sin_full = lax.optimization_barrier((jnp.asarray(cos_np), jnp.asarray(sin_np)))
    low = n - box_size // 2
    cos_rows = jnp.concatenate([cos_full[low:], cos_full[: box_size - (n - low)]], axis=0)
    sin_rows = jnp.concatenate([sin_full[low:], sin_full[: box_size - (n - low)]], axis=0)
    cos_cols = cos_rows.T
    sin_cols = sin_rows.T
    row_cos = cos_full[margin : margin + tile_width]
    row_sin = sin_full[margin : margin + tile_width]
    col_cos = row_cos.T
    col_sin = row_sin.T

    local_count = templates.shape[0]
    flat_size = box_size * box_size
    id_block = jnp.broadcast_to(defocus.astype(bf16)[:, None], (local_count, 128))
    packed = jnp.concatenate([templates.reshape(local_count, flat_size), id_block], axis=1)
    arrivals = exchange_rounds(packed)
    total = sum(piece.shape[0] for piece in arrivals)

    padded = extended(micrograph, (("orient", 0), ("tile", 1)), margin)
    half_real = matmul(padded, cos_full).astype(bf16)
    half_imag = (-matmul(padded, sin_full)).astype(bf16)
    spec_real = (matmul(cos_full, half_real) + matmul(sin_full, half_imag)).astype(bf16).astype(f32)
    spec_imag = (matmul(cos_full, half_imag) - matmul(sin_full, half_real)).astype(bf16).astype(f32)

    tables = (cos_rows, sin_rows, cos_cols, sin_cols, row_cos, row_sin, col_cos, col_sin)
    shape = (tile_width, tile_width)
    stats = (jnp.full(shape, -jnp.inf, f32), jnp.zeros(shape, f32), jnp.zeros(shape, f32))
    for piece in arrivals:
        count = piece.shape[0]
        piece_templates = piece[:, :flat_size].reshape(count, box_size, box_size)
        piece_ids = piece[:, flat_size].astype(jnp.int32)
        stats = correlate(piece_ids, piece_templates, ctf, spec_real, spec_imag, tables, scaling, stats)
    peak_map, sum_map, squares = stats

    live = usable[0, 0]
    row_mask = (jnp.arange(tile_width, dtype=jnp.int32) < RB * live)[:, None]
    orient_count = float(total)
    peak_out = jnp.where(row_mask, peak_map, 0.0)
    mean_out = jnp.where(row_mask, sum_map / orient_count, 0.0)
    square_out = jnp.where(row_mask, squares / orient_count, 0.0)
    return (peak_out, mean_out, square_out)


def solution(mesh):
    return jax.shard_map(
        body,
        mesh=mesh,
        in_specs=(
            P(("groups", "orient"), "tile"),
            P("orient", None, None),
            P(("groups", "orient")),
            P("groups", None, None),
            P(("groups", "orient"), "tile"),
        ),
        out_specs=(
            P(("groups", "orient"), "tile"),
            P(("groups", "orient"), "tile"),
            P(("groups", "orient"), "tile"),
        ),
        check_vma=False,
    )
```

```python
import functools
import math

import jax
import jax.numpy as jnp
import ml_dtypes
import numpy as np
from jax import lax
from jax.experimental import pallas as pl
from jax.experimental.pallas import tpu as pltpu
from jax.sharding import PartitionSpec as P

RB = 32
CHUNK = 8


def extended(block, sides, width):
    for axis, dim in sides:
        count = lax.axis_size(axis)
        forward = [(i, i + 1) for i in range(count - 1)]
        backward = [(target, source) for source, target in forward]
        low = lax.ppermute(
            lax.slice_in_dim(block, block.shape[dim] - width, None, axis=dim), axis, forward
        )
        high = lax.ppermute(lax.slice_in_dim(block, 0, width, axis=dim), axis, backward)
        block = jnp.concatenate([low, block, high], axis=dim)
    return block


def twiddles(padded_size):
    position = np.arange(padded_size, dtype=np.int64)
    phase_index = (position[:, None] * position[None, :]) % padded_size
    angles = phase_index.astype(np.float32) * np.float32(2.0 * math.pi / padded_size)
    angles = angles.astype(np.float64)
    cosines = np.cos(angles).astype(np.float32).astype(ml_dtypes.bfloat16)
    sines = np.sin(angles).astype(np.float32).astype(ml_dtypes.bfloat16)
    return cosines, sines


def matmul(left, right):
    return jnp.dot(left, right, preferred_element_type=jnp.float32)


def exchange_rounds(block):
    size = lax.axis_size("orient")
    step = 1
    while step * 2 < size:
        step *= 2
    rounds = [block]
    held = block
    while step >= 1:
        other = lax.ppermute(held, "orient", [(i, i ^ step) for i in range(size)])
        if len(rounds) > 1:
            other, rounds[-1] = lax.optimization_barrier((other, rounds[-1]))
        rounds.append(other)
        held = jnp.concatenate([held, other], axis=0)
        step //= 2
    return rounds


def swap(payload, pairs):
    return lax.ppermute(payload, "orient", [(a, b) for a, b in pairs] + [(b, a) for a, b in pairs])


def exchange_with_rows(block, tile, width):
    size = lax.axis_size("orient")
    index = lax.axis_index("orient")
    odd = index % 2 == 1
    low_rows = tile[tile.shape[0] - width :]
    high_rows = tile[:width]
    flat = block.shape[1]
    rows_size = width * tile.shape[1]

    def send(held, rows, pairs):
        payload = jnp.concatenate([held.reshape(-1), rows.reshape(-1)])
        got = swap(payload, pairs)
        count = held.shape[0]
        return got[: count * flat].reshape(count, flat), got[count * flat :].reshape(width, tile.shape[1])

    first, rows_one = send(block, jnp.where(odd, high_rows, low_rows), [(2 * i, 2 * i + 1) for i in range(size // 2)])
    held = jnp.concatenate([block, first], axis=0)
    second_pairs = [(2 * i + 1, 2 * i + 2) for i in range(size // 2 - 1)] + [(0, size - 1)]
    second, rows_two = send(held, jnp.where(odd, low_rows, high_rows), second_pairs)
    held = jnp.concatenate([held, second], axis=0)
    third_pairs = [(0, size // 2), (size - 1, size // 2 - 1), (1, size // 2 + 1), (2, size // 2 + 2)]
    third = swap(held, third_pairs)
    zero = jnp.zeros_like(rows_one)
    top = jnp.where(odd, rows_one, jnp.where(index == 0, zero, rows_two))
    bottom = jnp.where(odd, jnp.where(index == size - 1, zero, rows_two), rows_one)
    return [held, third], jnp.concatenate([top, tile, bottom], axis=0)


def correlate_kernel(ids_ref, tmpl_ref, ctf_ref, spec_r_ref, spec_i_ref, cos_rows_ref, sin_rows_ref,
                     cos_cols_ref, sin_cols_ref, row_cos_ref, row_sin_ref, col_cos_ref, col_sin_ref,
                     prev_peak_ref, prev_sum_ref, prev_sq_ref, peak_ref, sum_ref, sq_ref, *, scaling):
    bf16 = jnp.bfloat16
    f32 = jnp.float32
    o = pl.program_id(0)

    def mm(a, b):
        return jnp.dot(a, b, preferred_element_type=f32)

    template = tmpl_ref[0]
    part_real = mm(template, cos_rows_ref[...]).astype(bf16)
    part_imag = (-mm(template, sin_rows_ref[...])).astype(bf16)
    cos_cols = cos_cols_ref[...]
    sin_cols = sin_cols_ref[...]
    full_real = mm(cos_cols, part_real) + mm(sin_cols, part_imag)
    full_imag = mm(cos_cols, part_imag) - mm(sin_cols, part_real)
    weight = ctf_ref[0]
    w_real = (full_real * weight).astype(bf16).astype(f32)
    w_imag = (full_imag * weight).astype(bf16).astype(f32)
    spec_real = spec_r_ref[...]
    spec_imag = spec_i_ref[...]
    prod_real = (spec_real * w_real + spec_imag * w_imag).astype(bf16)
    prod_imag = (spec_imag * w_real - spec_real * w_imag).astype(bf16)
    row_cos = row_cos_ref[...]
    row_sin = row_sin_ref[...]
    left_real = (mm(row_cos, prod_real) - mm(row_sin, prod_imag)).astype(bf16)
    left_imag = (mm(row_cos, prod_imag) + mm(row_sin, prod_real)).astype(bf16)
    corr = (mm(left_real, col_cos_ref[...]) - mm(left_imag, col_sin_ref[...])) * scaling

    @pl.when(o == 0)
    def _():
        peak_ref[...] = jnp.maximum(prev_peak_ref[...], corr)
        sum_ref[...] = prev_sum_ref[...] + corr
        sq_ref[...] = prev_sq_ref[...] + corr * corr

    @pl.when(o > 0)
    def _():
        peak_ref[...] = jnp.maximum(peak_ref[...], corr)
        sum_ref[...] = sum_ref[...] + corr
        sq_ref[...] = sq_ref[...] + corr * corr


def correlate(ids, all_templates, ctf, spec_real, spec_imag, tables, scaling, previous):
    count, box, _ = all_templates.shape
    n = ctf.shape[1]
    tile = tables[4].shape[0]
    full = lambda shape: pl.BlockSpec(shape, lambda o, ids: (0,) * len(shape))
    in_specs = [
        pl.BlockSpec((1, box, box), lambda o, ids: (o, 0, 0)),
        pl.BlockSpec((1, n, n), lambda o, ids: (ids[o], 0, 0)),
        full((n, n)),
        full((n, n)),
    ] + [full(t.shape) for t in tables] + [full((tile, tile))] * 3
    out_block = full((tile, tile))
    grid_spec = pltpu.PrefetchScalarGridSpec(
        num_scalar_prefetch=1,
        grid=(count,),
        in_specs=in_specs,
        out_specs=[out_block, out_block, out_block],
    )
    out_shape = [jax.ShapeDtypeStruct((tile, tile), jnp.float32)] * 3
    return pl.pallas_call(
        functools.partial(correlate_kernel, scaling=scaling),
        grid_spec=grid_spec,
        out_shape=out_shape,
        compiler_params=pltpu.CompilerParams(dimension_semantics=("arbitrary",)),
        input_output_aliases={5 + len(tables): 0, 6 + len(tables): 1, 7 + len(tables): 2},
    )(ids, all_templates, ctf, spec_real, spec_imag, *tables, *previous)


def body(micrograph, templates, defocus, ctf, usable):
    bf16 = jnp.bfloat16
    f32 = jnp.float32
    tile_width = micrograph.shape[0]
    padded_size = ctf.shape[1]
    box_size = templates.shape[1]
    margin = (padded_size - tile_width) // 2
    scaling = 1.0 / (padded_size * padded_size)
    n = padded_size
    cos_np, sin_np = twiddles(n)

    cos_full, sin_full = lax.optimization_barrier((jnp.asarray(cos_np), jnp.asarray(sin_np)))
    low = n - box_size // 2
    cos_rows = jnp.concatenate([cos_full[low:], cos_full[: box_size - (n - low)]], axis=0)
    sin_rows = jnp.concatenate([sin_full[low:], sin_full[: box_size - (n - low)]], axis=0)
    cos_cols = cos_rows.T
    sin_cols = sin_rows.T
    row_cos = cos_full[margin : margin + tile_width]
    row_sin = sin_full[margin : margin + tile_width]
    col_cos = row_cos.T
    col_sin = row_sin.T

    local_count = templates.shape[0]
    flat_size = box_size * box_size
    id_block = jnp.broadcast_to(defocus.astype(bf16)[:, None], (local_count, 128))
    packed = jnp.concatenate([templates.reshape(local_count, flat_size), id_block], axis=1)
    if lax.axis_size("orient") == 8 and local_count == 1:
        arrivals, row_padded = exchange_with_rows(packed, micrograph, margin)
        padded = extended(row_padded, (("tile", 1),), margin)
    else:
        arrivals = exchange_rounds(packed)
        padded = extended(micrograph, (("orient", 0), ("tile", 1)), margin)
    total = sum(piece.shape[0] for piece in arrivals)

    half_real = matmul(padded, cos_full).astype(bf16)
    half_imag = (-matmul(padded, sin_full)).astype(bf16)
    spec_real = (matmul(cos_full, half_real) + matmul(sin_full, half_imag)).astype(bf16).astype(f32)
    spec_imag = (matmul(cos_full, half_imag) - matmul(sin_full, half_real)).astype(bf16).astype(f32)

    tables = (cos_rows, sin_rows, cos_cols, sin_cols, row_cos, row_sin, col_cos, col_sin)
    shape = (tile_width, tile_width)
    stats = (jnp.full(shape, -jnp.inf, f32), jnp.zeros(shape, f32), jnp.zeros(shape, f32))
    for piece in arrivals:
        count = piece.shape[0]
        piece_templates = piece[:, :flat_size].reshape(count, box_size, box_size)
        piece_ids = piece[:, flat_size].astype(jnp.int32)
        stats = correlate(piece_ids, piece_templates, ctf, spec_real, spec_imag, tables, scaling, stats)
    peak_map, sum_map, squares = stats

    live = usable[0, 0]
    row_mask = (jnp.arange(tile_width, dtype=jnp.int32) < RB * live)[:, None]
    orient_count = float(total)
    peak_out = jnp.where(row_mask, peak_map, 0.0)
    mean_out = jnp.where(row_mask, sum_map / orient_count, 0.0)
    square_out = jnp.where(row_mask, squares / orient_count, 0.0)
    return (peak_out, mean_out, square_out)


def solution(mesh):
    return jax.shard_map(
        body,
        mesh=mesh,
        in_specs=(
            P(("groups", "orient"), "tile"),
            P("orient", None, None),
            P(("groups", "orient")),
            P("groups", None, None),
            P(("groups", "orient"), "tile"),
        ),
        out_specs=(
            P(("groups", "orient"), "tile"),
            P(("groups", "orient"), "tile"),
            P(("groups", "orient"), "tile"),
        ),
        check_vma=False,
    )
```

```python
import functools
import math

import jax
import jax.numpy as jnp
import ml_dtypes
import numpy as np
from jax import lax
from jax.experimental import pallas as pl
from jax.experimental.pallas import tpu as pltpu
from jax.sharding import PartitionSpec as P

RB = 32
CHUNK = 8


def extended(block, sides, width):
    for axis, dim in sides:
        count = lax.axis_size(axis)
        forward = [(i, i + 1) for i in range(count - 1)]
        backward = [(target, source) for source, target in forward]
        low = lax.ppermute(
            lax.slice_in_dim(block, block.shape[dim] - width, None, axis=dim), axis, forward
        )
        high = lax.ppermute(lax.slice_in_dim(block, 0, width, axis=dim), axis, backward)
        block = jnp.concatenate([low, block, high], axis=dim)
    return block


def twiddles(padded_size):
    position = np.arange(padded_size, dtype=np.int64)
    phase_index = (position[:, None] * position[None, :]) % padded_size
    angles = phase_index.astype(np.float32) * np.float32(2.0 * math.pi / padded_size)
    angles = angles.astype(np.float64)
    cosines = np.cos(angles).astype(np.float32).astype(ml_dtypes.bfloat16)
    sines = np.sin(angles).astype(np.float32).astype(ml_dtypes.bfloat16)
    return cosines, sines


def matmul(left, right):
    return jnp.dot(left, right, preferred_element_type=jnp.float32)


def exchange_rounds(block):
    size = lax.axis_size("orient")
    step = 1
    while step * 2 < size:
        step *= 2
    rounds = [block]
    held = block
    while step >= 1:
        other = lax.ppermute(held, "orient", [(i, i ^ step) for i in range(size)])
        if len(rounds) > 1:
            other, rounds[-1] = lax.optimization_barrier((other, rounds[-1]))
        rounds.append(other)
        held = jnp.concatenate([held, other], axis=0)
        step //= 2
    return rounds


def swap(payload, pairs):
    return lax.ppermute(payload, "orient", [(a, b) for a, b in pairs] + [(b, a) for a, b in pairs])


def exchange_with_rows(block, tile, width):
    size = lax.axis_size("orient")
    index = lax.axis_index("orient")
    odd = index % 2 == 1
    low_rows = tile[tile.shape[0] - width :]
    high_rows = tile[:width]
    lanes = block.shape[1]
    carried = width * tile.shape[1] // lanes

    def send(held, rows, pairs):
        payload = jnp.concatenate([held, rows.reshape(carried, lanes)], axis=0)
        got = swap(payload, pairs)
        return got[: held.shape[0]], got[held.shape[0] :].reshape(width, tile.shape[1])

    first, rows_one = send(block, jnp.where(odd, high_rows, low_rows), [(2 * i, 2 * i + 1) for i in range(size // 2)])
    held = jnp.concatenate([block, first], axis=0)
    second_pairs = [(2 * i + 1, 2 * i + 2) for i in range(size // 2 - 1)] + [(0, size - 1)]
    second, rows_two = send(held, jnp.where(odd, low_rows, high_rows), second_pairs)
    held = jnp.concatenate([held, second], axis=0)
    third_pairs = [(0, size // 2), (size - 1, size // 2 - 1), (1, size // 2 + 1), (2, size // 2 + 2)]
    third = swap(held, third_pairs)
    zero = jnp.zeros_like(rows_one)
    top = jnp.where(odd, rows_one, jnp.where(index == 0, zero, rows_two))
    bottom = jnp.where(odd, jnp.where(index == size - 1, zero, rows_two), rows_one)
    return [held, third], jnp.concatenate([top, tile, bottom], axis=0)


def correlate_kernel(ids_ref, tmpl_ref, ctf_ref, spec_r_ref, spec_i_ref, cos_rows_ref, sin_rows_ref,
                     cols_ref, rows_ref, col_cos_ref, col_sin_ref,
                     prev_peak_ref, prev_sum_ref, prev_sq_ref, peak_ref, sum_ref, sq_ref, *, scaling):
    bf16 = jnp.bfloat16
    f32 = jnp.float32
    o = pl.program_id(0)

    def mm(a, b):
        return jnp.dot(a, b, preferred_element_type=f32)

    template = tmpl_ref[0]
    part_real = mm(template, cos_rows_ref[...]).astype(bf16)
    part_imag = (-mm(template, sin_rows_ref[...])).astype(bf16)
    cols = cols_ref[...]
    n = cols.shape[0] // 2
    from_real = mm(cols, part_real)
    from_imag = mm(cols, part_imag)
    full_real = from_real[:n] + from_imag[n:]
    full_imag = from_imag[:n] - from_real[n:]
    weight = ctf_ref[0]
    w_real = (full_real * weight).astype(bf16).astype(f32)
    w_imag = (full_imag * weight).astype(bf16).astype(f32)
    spec_real = spec_r_ref[...].astype(f32)
    spec_imag = spec_i_ref[...].astype(f32)
    prod_real = (spec_real * w_real + spec_imag * w_imag).astype(bf16)
    prod_imag = (spec_imag * w_real - spec_real * w_imag).astype(bf16)
    rows = rows_ref[...]
    tile = rows.shape[0] // 2
    left_from_real = mm(rows, prod_real)
    left_from_imag = mm(rows, prod_imag)
    left_real = (left_from_real[:tile] - left_from_imag[tile:]).astype(bf16)
    left_imag = (left_from_imag[:tile] + left_from_real[tile:]).astype(bf16)
    corr = (mm(left_real, col_cos_ref[...]) - mm(left_imag, col_sin_ref[...])) * scaling

    @pl.when(o == 0)
    def _():
        peak_ref[...] = jnp.maximum(prev_peak_ref[...], corr)
        sum_ref[...] = prev_sum_ref[...] + corr
        sq_ref[...] = prev_sq_ref[...] + corr * corr

    @pl.when(o > 0)
    def _():
        peak_ref[...] = jnp.maximum(peak_ref[...], corr)
        sum_ref[...] = sum_ref[...] + corr
        sq_ref[...] = sq_ref[...] + corr * corr


def correlate(ids, all_templates, ctf, spec_real, spec_imag, tables, scaling, previous):
    count = all_templates.shape[0]
    box = all_templates.shape[2]
    n = ctf.shape[1]
    tile = tables[4].shape[1]
    full = lambda shape: pl.BlockSpec(shape, lambda o, ids: (0,) * len(shape))
    in_specs = [
        pl.BlockSpec((1, box, box), lambda o, ids: (o, 0, 0)),
        pl.BlockSpec((1, n, n), lambda o, ids: (ids[o], 0, 0)),
        full((n, n)),
        full((n, n)),
    ] + [full(t.shape) for t in tables] + [full((tile, tile))] * 3
    out_block = full((tile, tile))
    grid_spec = pltpu.PrefetchScalarGridSpec(
        num_scalar_prefetch=1,
        grid=(count,),
        in_specs=in_specs,
        out_specs=[out_block, out_block, out_block],
    )
    out_shape = [jax.ShapeDtypeStruct((tile, tile), jnp.float32)] * 3
    return pl.pallas_call(
        functools.partial(correlate_kernel, scaling=scaling),
        grid_spec=grid_spec,
        out_shape=out_shape,
        compiler_params=pltpu.CompilerParams(dimension_semantics=("arbitrary",)),
        input_output_aliases={5 + len(tables): 0, 6 + len(tables): 1, 7 + len(tables): 2},
    )(ids, all_templates, ctf, spec_real, spec_imag, *tables, *previous)


def body(micrograph, templates, defocus, ctf, usable):
    bf16 = jnp.bfloat16
    f32 = jnp.float32
    tile_width = micrograph.shape[0]
    padded_size = ctf.shape[1]
    box_size = templates.shape[1]
    margin = (padded_size - tile_width) // 2
    scaling = 1.0 / (padded_size * padded_size)
    n = padded_size
    cos_np, sin_np = twiddles(n)

    cos_full, sin_full = lax.optimization_barrier((jnp.asarray(cos_np), jnp.asarray(sin_np)))
    low = n - box_size // 2
    cos_rows = jnp.concatenate([cos_full[low:], cos_full[: box_size - (n - low)]], axis=0)
    sin_rows = jnp.concatenate([sin_full[low:], sin_full[: box_size - (n - low)]], axis=0)
    cos_cols = cos_rows.T
    sin_cols = sin_rows.T
    row_cos = cos_full[margin : margin + tile_width]
    row_sin = sin_full[margin : margin + tile_width]
    col_cos = row_cos.T
    col_sin = row_sin.T

    local_count = templates.shape[0]
    id_rows = jnp.broadcast_to(defocus.astype(bf16)[:, None, None], (local_count, 8, box_size))
    block_rows = box_size + 8
    packed = jnp.concatenate([templates, id_rows], axis=1).reshape(local_count * block_rows, box_size)
    if lax.axis_size("orient") == 8 and local_count == 1 and (margin * tile_width) % box_size == 0:
        arrivals, row_padded = exchange_with_rows(packed, micrograph, margin)
        padded = extended(row_padded, (("tile", 1),), margin)
    else:
        arrivals = exchange_rounds(packed)
        padded = extended(micrograph, (("orient", 0), ("tile", 1)), margin)
    total = sum(piece.shape[0] for piece in arrivals) // block_rows

    half_real = matmul(padded, cos_full).astype(bf16)
    half_imag = (-matmul(padded, sin_full)).astype(bf16)
    spec_real = (matmul(cos_full, half_real) + matmul(sin_full, half_imag)).astype(bf16)
    spec_imag = (matmul(cos_full, half_imag) - matmul(sin_full, half_real)).astype(bf16)

    tables = (
        cos_rows,
        sin_rows,
        jnp.concatenate([cos_cols, sin_cols], axis=0),
        jnp.concatenate([row_cos, row_sin], axis=0),
        col_cos,
        col_sin,
    )
    shape = (tile_width, tile_width)
    stats = (jnp.full(shape, -jnp.inf, f32), jnp.zeros(shape, f32), jnp.zeros(shape, f32))
    for piece in arrivals:
        count = piece.shape[0] // block_rows
        piece = piece.reshape(count, block_rows, box_size)
        piece_ids = piece[:, box_size, 0].astype(jnp.int32)
        stats = correlate(piece_ids, piece, ctf, spec_real, spec_imag, tables, scaling, stats)
    peak_map, sum_map, squares = stats

    live = usable[0, 0]
    row_mask = (jnp.arange(tile_width, dtype=jnp.int32) < RB * live)[:, None]
    orient_count = float(total)
    peak_out = jnp.where(row_mask, peak_map, 0.0)
    mean_out = jnp.where(row_mask, sum_map / orient_count, 0.0)
    square_out = jnp.where(row_mask, squares / orient_count, 0.0)
    return (peak_out, mean_out, square_out)


def solution(mesh):
    return jax.shard_map(
        body,
        mesh=mesh,
        in_specs=(
            P(("groups", "orient"), "tile"),
            P("orient", None, None),
            P(("groups", "orient")),
            P("groups", None, None),
            P(("groups", "orient"), "tile"),
        ),
        out_specs=(
            P(("groups", "orient"), "tile"),
            P(("groups", "orient"), "tile"),
            P(("groups", "orient"), "tile"),
        ),
        check_vma=False,
    )
```

```python
import functools
import math

import jax
import jax.numpy as jnp
import ml_dtypes
import numpy as np
from jax import lax
from jax.experimental import pallas as pl
from jax.experimental.pallas import tpu as pltpu
from jax.sharding import PartitionSpec as P

RB = 32
CHUNK = 8


def extended(block, sides, width):
    for axis, dim in sides:
        count = lax.axis_size(axis)
        forward = [(i, i + 1) for i in range(count - 1)]
        backward = [(target, source) for source, target in forward]
        low = lax.ppermute(
            lax.slice_in_dim(block, block.shape[dim] - width, None, axis=dim), axis, forward
        )
        high = lax.ppermute(lax.slice_in_dim(block, 0, width, axis=dim), axis, backward)
        block = jnp.concatenate([low, block, high], axis=dim)
    return block


def twiddles(padded_size):
    position = np.arange(padded_size, dtype=np.int64)
    phase_index = (position[:, None] * position[None, :]) % padded_size
    angles = phase_index.astype(np.float32) * np.float32(2.0 * math.pi / padded_size)
    angles = angles.astype(np.float64)
    cosines = np.cos(angles).astype(np.float32).astype(ml_dtypes.bfloat16)
    sines = np.sin(angles).astype(np.float32).astype(ml_dtypes.bfloat16)
    return cosines, sines


def matmul(left, right):
    return jnp.dot(left, right, preferred_element_type=jnp.float32)


def exchange_rounds(block):
    size = lax.axis_size("orient")
    step = 1
    while step * 2 < size:
        step *= 2
    rounds = [block]
    held = block
    while step >= 1:
        other = lax.ppermute(held, "orient", [(i, i ^ step) for i in range(size)])
        if len(rounds) > 1:
            other, rounds[-1] = lax.optimization_barrier((other, rounds[-1]))
        rounds.append(other)
        held = jnp.concatenate([held, other], axis=0)
        step //= 2
    return rounds


def swap(payload, pairs):
    return lax.ppermute(payload, "orient", [(a, b) for a, b in pairs] + [(b, a) for a, b in pairs])


def exchange_with_rows(block, tile, width):
    size = lax.axis_size("orient")
    index = lax.axis_index("orient")
    odd = index % 2 == 1
    low_rows = tile[tile.shape[0] - width :]
    high_rows = tile[:width]
    lanes = block.shape[1]
    carried = width * tile.shape[1] // lanes

    def send(held, rows, pairs):
        payload = jnp.concatenate([held, rows.reshape(carried, lanes)], axis=0)
        got = swap(payload, pairs)
        return got[: held.shape[0]], got[held.shape[0] :].reshape(width, tile.shape[1])

    first, rows_one = send(block, jnp.where(odd, high_rows, low_rows), [(2 * i, 2 * i + 1) for i in range(size // 2)])
    held = jnp.concatenate([block, first], axis=0)
    second_pairs = [(2 * i + 1, 2 * i + 2) for i in range(size // 2 - 1)] + [(0, size - 1)]
    second, rows_two = send(held, jnp.where(odd, low_rows, high_rows), second_pairs)
    held = jnp.concatenate([held, second], axis=0)
    third_pairs = [(0, size // 2), (size - 1, size // 2 - 1), (1, size // 2 + 1), (2, size // 2 + 2)]
    cores = lax.axis_size("tile")
    share = held.shape[0] // cores
    core = lax.axis_index("tile")
    mine = lax.dynamic_slice_in_dim(held, core * share, share, 0)
    third = swap(mine, third_pairs)
    arrivals = [held, third]
    zero = jnp.zeros_like(rows_one)
    top = jnp.where(odd, rows_one, jnp.where(index == 0, zero, rows_two))
    bottom = jnp.where(odd, jnp.where(index == size - 1, zero, rows_two), rows_one)
    return arrivals, jnp.concatenate([top, tile, bottom], axis=0)


def correlate_kernel(ids_ref, tmpl_ref, ctf_ref, spec_r_ref, spec_i_ref, cos_rows_ref, sin_rows_ref,
                     cols_ref, rows_ref, col_cos_ref, col_sin_ref,
                     prev_peak_ref, prev_sum_ref, prev_sq_ref, peak_ref, sum_ref, sq_ref, *, scaling):
    bf16 = jnp.bfloat16
    f32 = jnp.float32
    o = pl.program_id(0)

    def mm(a, b):
        return jnp.dot(a, b, preferred_element_type=f32)

    template = tmpl_ref[0]
    part_real = mm(template, cos_rows_ref[...]).astype(bf16)
    part_imag = (-mm(template, sin_rows_ref[...])).astype(bf16)
    cols = cols_ref[...]
    n = cols.shape[0] // 2
    from_real = mm(cols, part_real)
    from_imag = mm(cols, part_imag)
    full_real = from_real[:n] + from_imag[n:]
    full_imag = from_imag[:n] - from_real[n:]
    weight = ctf_ref[0]
    w_real = (full_real * weight).astype(bf16).astype(f32)
    w_imag = (full_imag * weight).astype(bf16).astype(f32)
    spec_real = spec_r_ref[...].astype(f32)
    spec_imag = spec_i_ref[...].astype(f32)
    prod_real = (spec_real * w_real + spec_imag * w_imag).astype(bf16)
    prod_imag = (spec_imag * w_real - spec_real * w_imag).astype(bf16)
    rows = rows_ref[...]
    tile = rows.shape[0] // 2
    left_from_real = mm(rows, prod_real)
    left_from_imag = mm(rows, prod_imag)
    left_real = (left_from_real[:tile] - left_from_imag[tile:]).astype(bf16)
    left_imag = (left_from_imag[:tile] + left_from_real[tile:]).astype(bf16)
    corr = (mm(left_real, col_cos_ref[...]) - mm(left_imag, col_sin_ref[...])) * scaling

    @pl.when(o == 0)
    def _():
        peak_ref[...] = jnp.maximum(prev_peak_ref[...], corr)
        sum_ref[...] = prev_sum_ref[...] + corr
        sq_ref[...] = prev_sq_ref[...] + corr * corr

    @pl.when(o > 0)
    def _():
        peak_ref[...] = jnp.maximum(peak_ref[...], corr)
        sum_ref[...] = sum_ref[...] + corr
        sq_ref[...] = sq_ref[...] + corr * corr


def correlate(ids, all_templates, ctf, spec_real, spec_imag, tables, scaling, previous):
    count = all_templates.shape[0]
    box = all_templates.shape[2]
    n = ctf.shape[1]
    tile = tables[4].shape[1]
    full = lambda shape: pl.BlockSpec(shape, lambda o, ids: (0,) * len(shape))
    in_specs = [
        pl.BlockSpec((1, box, box), lambda o, ids: (o, 0, 0)),
        pl.BlockSpec((1, n, n), lambda o, ids: (ids[o], 0, 0)),
        full((n, n)),
        full((n, n)),
    ] + [full(t.shape) for t in tables] + [full((tile, tile))] * 3
    out_block = full((tile, tile))
    grid_spec = pltpu.PrefetchScalarGridSpec(
        num_scalar_prefetch=1,
        grid=(count,),
        in_specs=in_specs,
        out_specs=[out_block, out_block, out_block],
    )
    out_shape = [jax.ShapeDtypeStruct((tile, tile), jnp.float32)] * 3
    return pl.pallas_call(
        functools.partial(correlate_kernel, scaling=scaling),
        grid_spec=grid_spec,
        out_shape=out_shape,
        compiler_params=pltpu.CompilerParams(dimension_semantics=("arbitrary",)),
        input_output_aliases={5 + len(tables): 0, 6 + len(tables): 1, 7 + len(tables): 2},
    )(ids, all_templates, ctf, spec_real, spec_imag, *tables, *previous)


def body(micrograph, templates, defocus, ctf, usable):
    bf16 = jnp.bfloat16
    f32 = jnp.float32
    tile_width = micrograph.shape[0]
    padded_size = ctf.shape[1]
    box_size = templates.shape[1]
    margin = (padded_size - tile_width) // 2
    scaling = 1.0 / (padded_size * padded_size)
    n = padded_size
    cos_np, sin_np = twiddles(n)

    cos_full, sin_full = lax.optimization_barrier((jnp.asarray(cos_np), jnp.asarray(sin_np)))
    low = n - box_size // 2
    cos_rows = jnp.concatenate([cos_full[low:], cos_full[: box_size - (n - low)]], axis=0)
    sin_rows = jnp.concatenate([sin_full[low:], sin_full[: box_size - (n - low)]], axis=0)
    cos_cols = cos_rows.T
    sin_cols = sin_rows.T
    row_cos = cos_full[margin : margin + tile_width]
    row_sin = sin_full[margin : margin + tile_width]
    col_cos = row_cos.T
    col_sin = row_sin.T

    local_count = templates.shape[0]
    id_rows = jnp.broadcast_to(defocus.astype(bf16)[:, None, None], (local_count, 8, box_size))
    block_rows = box_size + 8
    packed = jnp.concatenate([templates, id_rows], axis=1).reshape(local_count * block_rows, box_size)
    split_last = lax.axis_size("orient") == 8 and lax.axis_size("tile") == 2
    split_last = split_last and local_count == 1 and (margin * tile_width) % box_size == 0
    if split_last:
        arrivals, row_padded = exchange_with_rows(packed, micrograph, margin)
        padded = extended(row_padded, (("tile", 1),), margin)
    else:
        arrivals = exchange_rounds(packed)
        padded = extended(micrograph, (("orient", 0), ("tile", 1)), margin)
    total = sum(piece.shape[0] for piece in arrivals) // block_rows

    half_real = matmul(padded, cos_full).astype(bf16)
    half_imag = (-matmul(padded, sin_full)).astype(bf16)
    spec_real = (matmul(cos_full, half_real) + matmul(sin_full, half_imag)).astype(bf16)
    spec_imag = (matmul(cos_full, half_imag) - matmul(sin_full, half_real)).astype(bf16)

    tables = (
        cos_rows,
        sin_rows,
        jnp.concatenate([cos_cols, sin_cols], axis=0),
        jnp.concatenate([row_cos, row_sin], axis=0),
        col_cos,
        col_sin,
    )
    shape = (tile_width, tile_width)
    stats = (jnp.full(shape, -jnp.inf, f32), jnp.zeros(shape, f32), jnp.zeros(shape, f32))
    def run(piece, stats):
        count = piece.shape[0] // block_rows
        piece = piece.reshape(count, block_rows, box_size)
        piece_ids = piece[:, box_size, 0].astype(jnp.int32)
        return correlate(piece_ids, piece, ctf, spec_real, spec_imag, tables, scaling, stats)

    if split_last:
        stats = run(arrivals[0], stats)
        half, stats = lax.optimization_barrier((arrivals[1], stats))
        other_half = lax.ppermute(half, "tile", [(0, 1), (1, 0)])
        stats = run(half, stats)
        stats = run(other_half, stats)
        total = (arrivals[0].shape[0] + 2 * half.shape[0]) // block_rows
    else:
        for piece in arrivals:
            stats = run(piece, stats)
    peak_map, sum_map, squares = stats

    live = usable[0, 0]
    row_mask = (jnp.arange(tile_width, dtype=jnp.int32) < RB * live)[:, None]
    orient_count = float(total)
    peak_out = jnp.where(row_mask, peak_map, 0.0)
    mean_out = jnp.where(row_mask, sum_map / orient_count, 0.0)
    square_out = jnp.where(row_mask, squares / orient_count, 0.0)
    return (peak_out, mean_out, square_out)


def solution(mesh):
    return jax.shard_map(
        body,
        mesh=mesh,
        in_specs=(
            P(("groups", "orient"), "tile"),
            P("orient", None, None),
            P(("groups", "orient")),
            P("groups", None, None),
            P(("groups", "orient"), "tile"),
        ),
        out_specs=(
            P(("groups", "orient"), "tile"),
            P(("groups", "orient"), "tile"),
            P(("groups", "orient"), "tile"),
        ),
        check_vma=False,
    )
```

```python
import functools
import math

import jax
import jax.numpy as jnp
import ml_dtypes
import numpy as np
from jax import lax
from jax.experimental import pallas as pl
from jax.experimental.pallas import tpu as pltpu
from jax.sharding import PartitionSpec as P

RB = 32
CHUNK = 8


def extended(block, sides, width):
    for axis, dim in sides:
        count = lax.axis_size(axis)
        forward = [(i, i + 1) for i in range(count - 1)]
        backward = [(target, source) for source, target in forward]
        low = lax.ppermute(
            lax.slice_in_dim(block, block.shape[dim] - width, None, axis=dim), axis, forward
        )
        high = lax.ppermute(lax.slice_in_dim(block, 0, width, axis=dim), axis, backward)
        block = jnp.concatenate([low, block, high], axis=dim)
    return block


def twiddles(padded_size):
    position = np.arange(padded_size, dtype=np.int64)
    phase_index = (position[:, None] * position[None, :]) % padded_size
    angles = phase_index.astype(np.float32) * np.float32(2.0 * math.pi / padded_size)
    angles = angles.astype(np.float64)
    cosines = np.cos(angles).astype(np.float32).astype(ml_dtypes.bfloat16)
    sines = np.sin(angles).astype(np.float32).astype(ml_dtypes.bfloat16)
    return cosines, sines


def matmul(left, right):
    return jnp.dot(left, right, preferred_element_type=jnp.float32)


def exchange_rounds(block):
    size = lax.axis_size("orient")
    step = 1
    while step * 2 < size:
        step *= 2
    rounds = [block]
    held = block
    while step >= 1:
        other = lax.ppermute(held, "orient", [(i, i ^ step) for i in range(size)])
        if len(rounds) > 1:
            other, rounds[-1] = lax.optimization_barrier((other, rounds[-1]))
        rounds.append(other)
        held = jnp.concatenate([held, other], axis=0)
        step //= 2
    return rounds


def swap(payload, pairs):
    return lax.ppermute(payload, "orient", [(a, b) for a, b in pairs] + [(b, a) for a, b in pairs])


def exchange_with_rows(block, tile, width):
    size = lax.axis_size("orient")
    index = lax.axis_index("orient")
    odd = index % 2 == 1
    low_rows = tile[tile.shape[0] - width :]
    high_rows = tile[:width]
    lanes = block.shape[1]
    carried = width * tile.shape[1] // lanes

    def send(held, rows, pairs):
        payload = jnp.concatenate([held, rows.reshape(carried, lanes)], axis=0)
        got = swap(payload, pairs)
        return got[: held.shape[0]], got[held.shape[0] :].reshape(width, tile.shape[1])

    first, rows_one = send(block, jnp.where(odd, high_rows, low_rows), [(2 * i, 2 * i + 1) for i in range(size // 2)])
    held = jnp.concatenate([block, first], axis=0)
    second_pairs = [(2 * i + 1, 2 * i + 2) for i in range(size // 2 - 1)] + [(0, size - 1)]
    second, rows_two = send(held, jnp.where(odd, low_rows, high_rows), second_pairs)
    held = jnp.concatenate([held, second], axis=0)
    third_pairs = [(0, size // 2), (size - 1, size // 2 - 1), (1, size // 2 + 1), (2, size // 2 + 2)]
    cores = lax.axis_size("tile")
    share = held.shape[0] // cores
    core = lax.axis_index("tile")
    mine = lax.dynamic_slice_in_dim(held, core * share, share, 0)
    third = swap(mine, third_pairs)
    arrivals = [held, third]
    zero = jnp.zeros_like(rows_one)
    top = jnp.where(odd, rows_one, jnp.where(index == 0, zero, rows_two))
    bottom = jnp.where(odd, jnp.where(index == size - 1, zero, rows_two), rows_one)
    return arrivals, jnp.concatenate([top, tile, bottom], axis=0)


def correlate_kernel(ids_ref, tmpl_ref, ctf_ref, spec_r_ref, spec_i_ref, cos_rows_ref, sin_rows_ref,
                     cols_ref, rows_ref, col_cos_ref, col_sin_ref, *refs, scaling):
    if len(refs) == 6:
        prev_peak_ref, prev_sum_ref, prev_sq_ref, peak_ref, sum_ref, sq_ref = refs
    else:
        peak_ref, sum_ref, sq_ref = refs
    bf16 = jnp.bfloat16
    f32 = jnp.float32
    o = pl.program_id(0)

    def mm(a, b):
        return jnp.dot(a, b, preferred_element_type=f32)

    template = tmpl_ref[0]
    part_real = mm(template, cos_rows_ref[...]).astype(bf16)
    part_imag = (-mm(template, sin_rows_ref[...])).astype(bf16)
    cols = cols_ref[...]
    n = cols.shape[0] // 2
    from_real = mm(cols, part_real)
    from_imag = mm(cols, part_imag)
    full_real = from_real[:n] + from_imag[n:]
    full_imag = from_imag[:n] - from_real[n:]
    weight = ctf_ref[0]
    w_real = (full_real * weight).astype(bf16).astype(f32)
    w_imag = (full_imag * weight).astype(bf16).astype(f32)
    spec_real = spec_r_ref[...].astype(f32)
    spec_imag = spec_i_ref[...].astype(f32)
    prod_real = (spec_real * w_real + spec_imag * w_imag).astype(bf16)
    prod_imag = (spec_imag * w_real - spec_real * w_imag).astype(bf16)
    rows = rows_ref[...]
    tile = rows.shape[0] // 2
    left_from_real = mm(rows, prod_real)
    left_from_imag = mm(rows, prod_imag)
    left_real = (left_from_real[:tile] - left_from_imag[tile:]).astype(bf16)
    left_imag = (left_from_imag[:tile] + left_from_real[tile:]).astype(bf16)
    corr = (mm(left_real, col_cos_ref[...]) - mm(left_imag, col_sin_ref[...])) * scaling

    @pl.when(o == 0)
    def _():
        if len(refs) == 6:
            peak_ref[...] = jnp.maximum(prev_peak_ref[...], corr)
            sum_ref[...] = prev_sum_ref[...] + corr
            sq_ref[...] = prev_sq_ref[...] + corr * corr
        else:
            peak_ref[...] = corr
            sum_ref[...] = corr
            sq_ref[...] = corr * corr

    @pl.when(o > 0)
    def _():
        peak_ref[...] = jnp.maximum(peak_ref[...], corr)
        sum_ref[...] = sum_ref[...] + corr
        sq_ref[...] = sq_ref[...] + corr * corr


def correlate(ids, all_templates, ctf, spec_real, spec_imag, tables, scaling, previous):
    count = all_templates.shape[0]
    box = all_templates.shape[2]
    n = ctf.shape[1]
    tile = tables[4].shape[1]
    full = lambda shape: pl.BlockSpec(shape, lambda o, ids: (0,) * len(shape))
    in_specs = [
        pl.BlockSpec((1, box, box), lambda o, ids: (o, 0, 0)),
        pl.BlockSpec((1, n, n), lambda o, ids: (ids[o], 0, 0)),
        full((n, n)),
        full((n, n)),
    ] + [full(t.shape) for t in tables] + [full((tile, tile))] * len(previous)
    out_block = full((tile, tile))
    grid_spec = pltpu.PrefetchScalarGridSpec(
        num_scalar_prefetch=1,
        grid=(count,),
        in_specs=in_specs,
        out_specs=[out_block, out_block, out_block],
    )
    out_shape = [jax.ShapeDtypeStruct((tile, tile), jnp.float32)] * 3
    return pl.pallas_call(
        functools.partial(correlate_kernel, scaling=scaling),
        grid_spec=grid_spec,
        out_shape=out_shape,
        compiler_params=pltpu.CompilerParams(dimension_semantics=("arbitrary",)),
        input_output_aliases={5 + len(tables) + i: i for i in range(len(previous))},
    )(ids, all_templates, ctf, spec_real, spec_imag, *tables, *previous)


def body(micrograph, templates, defocus, ctf, usable):
    bf16 = jnp.bfloat16
    f32 = jnp.float32
    tile_width = micrograph.shape[0]
    padded_size = ctf.shape[1]
    box_size = templates.shape[1]
    margin = (padded_size - tile_width) // 2
    scaling = 1.0 / (padded_size * padded_size)
    n = padded_size
    cos_np, sin_np = twiddles(n)

    cos_full, sin_full = lax.optimization_barrier((jnp.asarray(cos_np), jnp.asarray(sin_np)))
    low = n - box_size // 2
    cos_rows = jnp.concatenate([cos_full[low:], cos_full[: box_size - (n - low)]], axis=0)
    sin_rows = jnp.concatenate([sin_full[low:], sin_full[: box_size - (n - low)]], axis=0)
    cos_cols = cos_rows.T
    sin_cols = sin_rows.T
    row_cos = cos_full[margin : margin + tile_width]
    row_sin = sin_full[margin : margin + tile_width]
    col_cos = row_cos.T
    col_sin = row_sin.T

    local_count = templates.shape[0]
    id_rows = jnp.broadcast_to(defocus.astype(bf16)[:, None, None], (local_count, 8, box_size))
    block_rows = box_size + 8
    packed = jnp.concatenate([templates, id_rows], axis=1).reshape(local_count * block_rows, box_size)
    split_last = lax.axis_size("orient") == 8 and lax.axis_size("tile") == 2
    split_last = split_last and local_count == 1 and (margin * tile_width) % box_size == 0
    if split_last:
        arrivals, row_padded = exchange_with_rows(packed, micrograph, margin)
        padded = extended(row_padded, (("tile", 1),), margin)
    else:
        arrivals = exchange_rounds(packed)
        padded = extended(micrograph, (("orient", 0), ("tile", 1)), margin)
    total = sum(piece.shape[0] for piece in arrivals) // block_rows

    half_real = matmul(padded, cos_full).astype(bf16)
    half_imag = (-matmul(padded, sin_full)).astype(bf16)
    spec_real = (matmul(cos_full, half_real) + matmul(sin_full, half_imag)).astype(bf16)
    spec_imag = (matmul(cos_full, half_imag) - matmul(sin_full, half_real)).astype(bf16)

    tables = (
        cos_rows,
        sin_rows,
        jnp.concatenate([cos_cols, sin_cols], axis=0),
        jnp.concatenate([row_cos, row_sin], axis=0),
        col_cos,
        col_sin,
    )
    shape = (tile_width, tile_width)
    stats = ()
    def run(piece, stats):
        count = piece.shape[0] // block_rows
        piece = piece.reshape(count, block_rows, box_size)
        piece_ids = piece[:, box_size, 0].astype(jnp.int32)
        return correlate(piece_ids, piece, ctf, spec_real, spec_imag, tables, scaling, stats)

    if split_last:
        stats = run(arrivals[0], stats)
        half, stats = lax.optimization_barrier((arrivals[1], stats))
        other_half = lax.ppermute(half, "tile", [(0, 1), (1, 0)])
        stats = run(jnp.concatenate([half, other_half], axis=0), stats)
        total = (arrivals[0].shape[0] + 2 * half.shape[0]) // block_rows
    else:
        for piece in arrivals:
            stats = run(piece, stats)
    peak_map, sum_map, squares = stats

    live = usable[0, 0]
    row_mask = (jnp.arange(tile_width, dtype=jnp.int32) < RB * live)[:, None]
    orient_count = float(total)
    peak_out = jnp.where(row_mask, peak_map, 0.0)
    mean_out = jnp.where(row_mask, sum_map / orient_count, 0.0)
    square_out = jnp.where(row_mask, squares / orient_count, 0.0)
    return (peak_out, mean_out, square_out)


def solution(mesh):
    return jax.shard_map(
        body,
        mesh=mesh,
        in_specs=(
            P(("groups", "orient"), "tile"),
            P("orient", None, None),
            P(("groups", "orient")),
            P("groups", None, None),
            P(("groups", "orient"), "tile"),
        ),
        out_specs=(
            P(("groups", "orient"), "tile"),
            P(("groups", "orient"), "tile"),
            P(("groups", "orient"), "tile"),
        ),
        check_vma=False,
    )
```

```python
import functools
import math

import jax
import jax.numpy as jnp
import ml_dtypes
import numpy as np
from jax import lax
from jax.experimental import pallas as pl
from jax.experimental.pallas import tpu as pltpu
from jax.sharding import PartitionSpec as P

RB = 32
CHUNK = 8


def extended(block, sides, width):
    for axis, dim in sides:
        count = lax.axis_size(axis)
        forward = [(i, i + 1) for i in range(count - 1)]
        backward = [(target, source) for source, target in forward]
        low = lax.ppermute(
            lax.slice_in_dim(block, block.shape[dim] - width, None, axis=dim), axis, forward
        )
        high = lax.ppermute(lax.slice_in_dim(block, 0, width, axis=dim), axis, backward)
        block = jnp.concatenate([low, block, high], axis=dim)
    return block


def twiddles(padded_size):
    position = np.arange(padded_size, dtype=np.int64)
    phase_index = (position[:, None] * position[None, :]) % padded_size
    angles = phase_index.astype(np.float32) * np.float32(2.0 * math.pi / padded_size)
    angles = angles.astype(np.float64)
    cosines = np.cos(angles).astype(np.float32).astype(ml_dtypes.bfloat16)
    sines = np.sin(angles).astype(np.float32).astype(ml_dtypes.bfloat16)
    return cosines, sines


def matmul(left, right):
    return jnp.dot(left, right, preferred_element_type=jnp.float32)


def exchange_rounds(block):
    size = lax.axis_size("orient")
    step = 1
    while step * 2 < size:
        step *= 2
    rounds = [block]
    held = block
    while step >= 1:
        other = lax.ppermute(held, "orient", [(i, i ^ step) for i in range(size)])
        if len(rounds) > 1:
            other, rounds[-1] = lax.optimization_barrier((other, rounds[-1]))
        rounds.append(other)
        held = jnp.concatenate([held, other], axis=0)
        step //= 2
    return rounds


def swap(payload, pairs):
    return lax.ppermute(payload, "orient", [(a, b) for a, b in pairs] + [(b, a) for a, b in pairs])


def exchange_with_rows(block, tile, width):
    size = lax.axis_size("orient")
    index = lax.axis_index("orient")
    odd = index % 2 == 1
    low_rows = tile[tile.shape[0] - width :]
    high_rows = tile[:width]
    lanes = block.shape[1]
    carried = width * tile.shape[1] // lanes

    def send(held, rows, pairs):
        payload = jnp.concatenate([held, rows.reshape(carried, lanes)], axis=0)
        got = swap(payload, pairs)
        return got[: held.shape[0]], got[held.shape[0] :].reshape(width, tile.shape[1])

    first, rows_one = send(block, jnp.where(odd, high_rows, low_rows), [(2 * i, 2 * i + 1) for i in range(size // 2)])
    held = jnp.concatenate([block, first], axis=0)
    second_pairs = [(2 * i + 1, 2 * i + 2) for i in range(size // 2 - 1)] + [(0, size - 1)]
    second, rows_two = send(held, jnp.where(odd, low_rows, high_rows), second_pairs)
    held = jnp.concatenate([held, second], axis=0)
    third_pairs = [(0, size // 2), (size - 1, size // 2 - 1), (1, size // 2 + 1), (2, size // 2 + 2)]
    cores = lax.axis_size("tile")
    share = held.shape[0] // cores
    core = lax.axis_index("tile")
    mine = lax.dynamic_slice_in_dim(held, core * share, share, 0)
    third = swap(mine, third_pairs)
    arrivals = [held, third]
    zero = jnp.zeros_like(rows_one)
    top = jnp.where(odd, rows_one, jnp.where(index == 0, zero, rows_two))
    bottom = jnp.where(odd, jnp.where(index == size - 1, zero, rows_two), rows_one)
    return arrivals, jnp.concatenate([top, tile, bottom], axis=0)


def correlate_kernel(ids_ref, live_ref, tmpl_ref, ctf_ref, spec_r_ref, spec_i_ref, cos_rows_ref, sin_rows_ref,
                     cols_ref, rows_ref, col_cos_ref, col_sin_ref, *refs, scaling, total, block):
    if len(refs) == 6:
        prev_peak_ref, prev_sum_ref, prev_sq_ref, peak_ref, sum_ref, sq_ref = refs
    else:
        peak_ref, sum_ref, sq_ref = refs
    bf16 = jnp.bfloat16
    f32 = jnp.float32
    o = pl.program_id(0)

    def mm(a, b):
        return jnp.dot(a, b, preferred_element_type=f32)

    template = tmpl_ref[0]
    part_real = mm(template, cos_rows_ref[...]).astype(bf16)
    part_imag = (-mm(template, sin_rows_ref[...])).astype(bf16)
    cols = cols_ref[...]
    n = cols.shape[0] // 2
    from_real = mm(cols, part_real)
    from_imag = mm(cols, part_imag)
    full_real = from_real[:n] + from_imag[n:]
    full_imag = from_imag[:n] - from_real[n:]
    weight = ctf_ref[0]
    w_real = (full_real * weight).astype(bf16).astype(f32)
    w_imag = (full_imag * weight).astype(bf16).astype(f32)
    spec_real = spec_r_ref[...].astype(f32)
    spec_imag = spec_i_ref[...].astype(f32)
    prod_real = (spec_real * w_real + spec_imag * w_imag).astype(bf16)
    prod_imag = (spec_imag * w_real - spec_real * w_imag).astype(bf16)
    rows = rows_ref[...]
    tile = rows.shape[0] // 2
    left_from_real = mm(rows, prod_real)
    left_from_imag = mm(rows, prod_imag)
    left_real = (left_from_real[:tile] - left_from_imag[tile:]).astype(bf16)
    left_imag = (left_from_imag[:tile] + left_from_real[tile:]).astype(bf16)
    corr = (mm(left_real, col_cos_ref[...]) - mm(left_imag, col_sin_ref[...])) * scaling

    @pl.when(o == 0)
    def _():
        if len(refs) == 6:
            peak_ref[...] = jnp.maximum(prev_peak_ref[...], corr)
            sum_ref[...] = prev_sum_ref[...] + corr
            sq_ref[...] = prev_sq_ref[...] + corr * corr
        else:
            peak_ref[...] = corr
            sum_ref[...] = corr
            sq_ref[...] = corr * corr

    @pl.when(o > 0)
    def _():
        peak_ref[...] = jnp.maximum(peak_ref[...], corr)
        sum_ref[...] = sum_ref[...] + corr
        sq_ref[...] = sq_ref[...] + corr * corr

    if total:
        @pl.when(o == pl.num_programs(0) - 1)
        def _():
            rows_at = lax.broadcasted_iota(jnp.int32, peak_ref.shape, 0)
            live = rows_at < block * live_ref[0]
            peak_ref[...] = jnp.where(live, peak_ref[...], 0.0)
            sum_ref[...] = jnp.where(live, sum_ref[...] / total, 0.0)
            sq_ref[...] = jnp.where(live, sq_ref[...] / total, 0.0)


def correlate(ids, live, all_templates, ctf, spec_real, spec_imag, tables, scaling, previous, total):
    count = all_templates.shape[0]
    box = all_templates.shape[2]
    n = ctf.shape[1]
    tile = tables[4].shape[1]
    full = lambda shape: pl.BlockSpec(shape, lambda o, ids, live: (0,) * len(shape))
    in_specs = [
        pl.BlockSpec((1, box, box), lambda o, ids, live: (o, 0, 0)),
        pl.BlockSpec((1, n, n), lambda o, ids, live: (ids[o], 0, 0)),
        full((n, n)),
        full((n, n)),
    ] + [full(t.shape) for t in tables] + [full((tile, tile))] * len(previous)
    out_block = full((tile, tile))
    grid_spec = pltpu.PrefetchScalarGridSpec(
        num_scalar_prefetch=2,
        grid=(count,),
        in_specs=in_specs,
        out_specs=[out_block, out_block, out_block],
    )
    out_shape = [jax.ShapeDtypeStruct((tile, tile), jnp.float32)] * 3
    return pl.pallas_call(
        functools.partial(correlate_kernel, scaling=scaling, total=total, block=RB),
        grid_spec=grid_spec,
        out_shape=out_shape,
        compiler_params=pltpu.CompilerParams(dimension_semantics=("arbitrary",)),
        input_output_aliases={6 + len(tables) + i: i for i in range(len(previous))},
    )(ids, live, all_templates, ctf, spec_real, spec_imag, *tables, *previous)


def body(micrograph, templates, defocus, ctf, usable):
    bf16 = jnp.bfloat16
    f32 = jnp.float32
    tile_width = micrograph.shape[0]
    padded_size = ctf.shape[1]
    box_size = templates.shape[1]
    margin = (padded_size - tile_width) // 2
    scaling = 1.0 / (padded_size * padded_size)
    n = padded_size
    cos_np, sin_np = twiddles(n)

    cos_full, sin_full = lax.optimization_barrier((jnp.asarray(cos_np), jnp.asarray(sin_np)))
    low = n - box_size // 2
    cos_rows = jnp.concatenate([cos_full[low:], cos_full[: box_size - (n - low)]], axis=0)
    sin_rows = jnp.concatenate([sin_full[low:], sin_full[: box_size - (n - low)]], axis=0)
    cos_cols = cos_rows.T
    sin_cols = sin_rows.T
    row_cos = cos_full[margin : margin + tile_width]
    row_sin = sin_full[margin : margin + tile_width]
    col_cos = row_cos.T
    col_sin = row_sin.T

    local_count = templates.shape[0]
    id_rows = jnp.broadcast_to(defocus.astype(bf16)[:, None, None], (local_count, 8, box_size))
    block_rows = box_size + 8
    packed = jnp.concatenate([templates, id_rows], axis=1).reshape(local_count * block_rows, box_size)
    split_last = lax.axis_size("orient") == 8 and lax.axis_size("tile") == 2
    split_last = split_last and local_count == 1 and (margin * tile_width) % box_size == 0
    if split_last:
        arrivals, row_padded = exchange_with_rows(packed, micrograph, margin)
        core = lax.axis_index("tile")
        edge = jnp.where(core == 0, row_padded[:, tile_width - margin :], row_padded[:, :margin])
        got = lax.ppermute(edge, "tile", [(0, 1), (1, 0)])
        zero = jnp.zeros_like(got)
        padded = jnp.concatenate(
            [jnp.where(core == 0, zero, got), row_padded, jnp.where(core == 0, got, zero)], axis=1
        )
    else:
        arrivals = exchange_rounds(packed)
        padded = extended(micrograph, (("orient", 0), ("tile", 1)), margin)
    total = sum(piece.shape[0] for piece in arrivals) // block_rows

    half_real = matmul(padded, cos_full).astype(bf16)
    half_imag = (-matmul(padded, sin_full)).astype(bf16)
    spec_real = (matmul(cos_full, half_real) + matmul(sin_full, half_imag)).astype(bf16)
    spec_imag = (matmul(cos_full, half_imag) - matmul(sin_full, half_real)).astype(bf16)

    tables = (
        cos_rows,
        sin_rows,
        jnp.concatenate([cos_cols, sin_cols], axis=0),
        jnp.concatenate([row_cos, row_sin], axis=0),
        col_cos,
        col_sin,
    )
    shape = (tile_width, tile_width)
    stats = ()
    live = usable.reshape(-1)[:1]

    def run(piece, stats, total=0):
        count = piece.shape[0] // block_rows
        piece = piece.reshape(count, block_rows, box_size)
        piece_ids = piece[:, box_size, 0].astype(jnp.int32)
        return correlate(piece_ids, live, piece, ctf, spec_real, spec_imag, tables, scaling, stats, total)

    if split_last:
        stats = run(arrivals[0], stats)
        half, stats = lax.optimization_barrier((arrivals[1], stats))
        other_half = lax.ppermute(half, "tile", [(0, 1), (1, 0)])
        total = (arrivals[0].shape[0] + 2 * half.shape[0]) // block_rows
        stats = run(jnp.concatenate([half, other_half], axis=0), stats, float(total))
    else:
        for last, piece in enumerate(arrivals, 1 - len(arrivals)):
            stats = run(piece, stats, 0 if last else float(total))
    return stats


def solution(mesh):
    return jax.shard_map(
        body,
        mesh=mesh,
        in_specs=(
            P(("groups", "orient"), "tile"),
            P("orient", None, None),
            P(("groups", "orient")),
            P("groups", None, None),
            P(("groups", "orient"), "tile"),
        ),
        out_specs=(
            P(("groups", "orient"), "tile"),
            P(("groups", "orient"), "tile"),
            P(("groups", "orient"), "tile"),
        ),
        check_vma=False,
    )
```

```python
import functools
import math

import jax
import jax.numpy as jnp
import ml_dtypes
import numpy as np
from jax import lax
from jax.experimental import pallas as pl
from jax.experimental.pallas import tpu as pltpu
from jax.sharding import PartitionSpec as P

RB = 32
CHUNK = 8


def extended(block, sides, width):
    for axis, dim in sides:
        count = lax.axis_size(axis)
        forward = [(i, i + 1) for i in range(count - 1)]
        backward = [(target, source) for source, target in forward]
        low = lax.ppermute(
            lax.slice_in_dim(block, block.shape[dim] - width, None, axis=dim), axis, forward
        )
        high = lax.ppermute(lax.slice_in_dim(block, 0, width, axis=dim), axis, backward)
        block = jnp.concatenate([low, block, high], axis=dim)
    return block


def twiddles(padded_size):
    position = np.arange(padded_size, dtype=np.int64)
    phase_index = (position[:, None] * position[None, :]) % padded_size
    angles = phase_index.astype(np.float32) * np.float32(2.0 * math.pi / padded_size)
    angles = angles.astype(np.float64)
    cosines = np.cos(angles).astype(np.float32).astype(ml_dtypes.bfloat16)
    sines = np.sin(angles).astype(np.float32).astype(ml_dtypes.bfloat16)
    return cosines, sines


def matmul(left, right):
    return jnp.dot(left, right, preferred_element_type=jnp.float32)


def exchange_rounds(block):
    size = lax.axis_size("orient")
    step = 1
    while step * 2 < size:
        step *= 2
    rounds = [block]
    held = block
    while step >= 1:
        other = lax.ppermute(held, "orient", [(i, i ^ step) for i in range(size)])
        if len(rounds) > 1:
            other, rounds[-1] = lax.optimization_barrier((other, rounds[-1]))
        rounds.append(other)
        held = jnp.concatenate([held, other], axis=0)
        step //= 2
    return rounds


def swap(payload, pairs):
    return lax.ppermute(payload, "orient", [(a, b) for a, b in pairs] + [(b, a) for a, b in pairs])


def exchange_with_rows(block, tile, width):
    size = lax.axis_size("orient")
    index = lax.axis_index("orient")
    odd = index % 2 == 1
    low_rows = tile[tile.shape[0] - width :]
    high_rows = tile[:width]
    lanes = block.shape[1]
    carried = width * tile.shape[1] // lanes

    def send(held, rows, pairs):
        payload = jnp.concatenate([held, rows.reshape(carried, lanes)], axis=0)
        got = swap(payload, pairs)
        return got[: held.shape[0]], got[held.shape[0] :].reshape(width, tile.shape[1])

    first, rows_one = send(block, jnp.where(odd, high_rows, low_rows), [(2 * i, 2 * i + 1) for i in range(size // 2)])
    held = jnp.concatenate([block, first], axis=0)
    core = lax.axis_index("tile")
    share = block.shape[0]
    mine = lax.dynamic_slice_in_dim(held, core * share, share, 0)
    second_pairs = [(2 * i + 1, 2 * i + 2) for i in range(size // 2 - 1)] + [(0, size - 1)]
    second, rows_two = send(mine, jnp.where(odd, low_rows, high_rows), second_pairs)
    third_pairs = [(0, size // 2), (size - 1, size // 2 - 1), (1, size // 2 + 1), (2, size // 2 + 2)]
    third = swap(jnp.concatenate([mine, second], axis=0), third_pairs)
    second_other = lax.ppermute(second, "tile", [(0, 1), (1, 0)])
    arrivals = [jnp.concatenate([held, second, second_other], axis=0), third]
    zero = jnp.zeros_like(rows_one)
    top = jnp.where(odd, rows_one, jnp.where(index == 0, zero, rows_two))
    bottom = jnp.where(odd, jnp.where(index == size - 1, zero, rows_two), rows_one)
    return arrivals, jnp.concatenate([top, tile, bottom], axis=0)


def correlate_kernel(ids_ref, live_ref, tmpl_ref, ctf_ref, spec_r_ref, spec_i_ref, cos_rows_ref, sin_rows_ref,
                     cols_ref, rows_ref, col_cos_ref, col_sin_ref, *refs, scaling, total, block):
    if len(refs) == 6:
        prev_peak_ref, prev_sum_ref, prev_sq_ref, peak_ref, sum_ref, sq_ref = refs
    else:
        peak_ref, sum_ref, sq_ref = refs
    bf16 = jnp.bfloat16
    f32 = jnp.float32
    o = pl.program_id(0)

    def mm(a, b):
        return jnp.dot(a, b, preferred_element_type=f32)

    template = tmpl_ref[0]
    part_real = mm(template, cos_rows_ref[...]).astype(bf16)
    part_imag = (-mm(template, sin_rows_ref[...])).astype(bf16)
    cols = cols_ref[...]
    n = cols.shape[0] // 2
    from_real = mm(cols, part_real)
    from_imag = mm(cols, part_imag)
    full_real = from_real[:n] + from_imag[n:]
    full_imag = from_imag[:n] - from_real[n:]
    weight = ctf_ref[0]
    w_real = (full_real * weight).astype(bf16).astype(f32)
    w_imag = (full_imag * weight).astype(bf16).astype(f32)
    spec_real = spec_r_ref[...].astype(f32)
    spec_imag = spec_i_ref[...].astype(f32)
    prod_real = (spec_real * w_real + spec_imag * w_imag).astype(bf16)
    prod_imag = (spec_imag * w_real - spec_real * w_imag).astype(bf16)
    rows = rows_ref[...]
    tile = rows.shape[0] // 2
    left_from_real = mm(rows, prod_real)
    left_from_imag = mm(rows, prod_imag)
    left_real = (left_from_real[:tile] - left_from_imag[tile:]).astype(bf16)
    left_imag = (left_from_imag[:tile] + left_from_real[tile:]).astype(bf16)
    corr = (mm(left_real, col_cos_ref[...]) - mm(left_imag, col_sin_ref[...])) * scaling

    @pl.when(o == 0)
    def _():
        if len(refs) == 6:
            peak_ref[...] = jnp.maximum(prev_peak_ref[...], corr)
            sum_ref[...] = prev_sum_ref[...] + corr
            sq_ref[...] = prev_sq_ref[...] + corr * corr
        else:
            peak_ref[...] = corr
            sum_ref[...] = corr
            sq_ref[...] = corr * corr

    @pl.when(o > 0)
    def _():
        peak_ref[...] = jnp.maximum(peak_ref[...], corr)
        sum_ref[...] = sum_ref[...] + corr
        sq_ref[...] = sq_ref[...] + corr * corr

    if total:
        @pl.when(o == pl.num_programs(0) - 1)
        def _():
            rows_at = lax.broadcasted_iota(jnp.int32, peak_ref.shape, 0)
            live = rows_at < block * live_ref[0]
            peak_ref[...] = jnp.where(live, peak_ref[...], 0.0)
            sum_ref[...] = jnp.where(live, sum_ref[...] / total, 0.0)
            sq_ref[...] = jnp.where(live, sq_ref[...] / total, 0.0)


def correlate(ids, live, all_templates, ctf, spec_real, spec_imag, tables, scaling, previous, total):
    count = all_templates.shape[0]
    box = all_templates.shape[2]
    n = ctf.shape[1]
    tile = tables[4].shape[1]
    full = lambda shape: pl.BlockSpec(shape, lambda o, ids, live: (0,) * len(shape))
    in_specs = [
        pl.BlockSpec((1, box, box), lambda o, ids, live: (o, 0, 0)),
        pl.BlockSpec((1, n, n), lambda o, ids, live: (ids[o], 0, 0)),
        full((n, n)),
        full((n, n)),
    ] + [full(t.shape) for t in tables] + [full((tile, tile))] * len(previous)
    out_block = full((tile, tile))
    grid_spec = pltpu.PrefetchScalarGridSpec(
        num_scalar_prefetch=2,
        grid=(count,),
        in_specs=in_specs,
        out_specs=[out_block, out_block, out_block],
    )
    out_shape = [jax.ShapeDtypeStruct((tile, tile), jnp.float32)] * 3
    return pl.pallas_call(
        functools.partial(correlate_kernel, scaling=scaling, total=total, block=RB),
        grid_spec=grid_spec,
        out_shape=out_shape,
        compiler_params=pltpu.CompilerParams(dimension_semantics=("arbitrary",)),
        input_output_aliases={6 + len(tables) + i: i for i in range(len(previous))},
    )(ids, live, all_templates, ctf, spec_real, spec_imag, *tables, *previous)


def body(micrograph, templates, defocus, ctf, usable):
    bf16 = jnp.bfloat16
    f32 = jnp.float32
    tile_width = micrograph.shape[0]
    padded_size = ctf.shape[1]
    box_size = templates.shape[1]
    margin = (padded_size - tile_width) // 2
    scaling = 1.0 / (padded_size * padded_size)
    n = padded_size
    cos_np, sin_np = twiddles(n)

    cos_full, sin_full = lax.optimization_barrier((jnp.asarray(cos_np), jnp.asarray(sin_np)))
    low = n - box_size // 2
    cos_rows = jnp.concatenate([cos_full[low:], cos_full[: box_size - (n - low)]], axis=0)
    sin_rows = jnp.concatenate([sin_full[low:], sin_full[: box_size - (n - low)]], axis=0)
    cos_cols = cos_rows.T
    sin_cols = sin_rows.T
    row_cos = cos_full[margin : margin + tile_width]
    row_sin = sin_full[margin : margin + tile_width]
    col_cos = row_cos.T
    col_sin = row_sin.T

    local_count = templates.shape[0]
    id_rows = jnp.broadcast_to(defocus.astype(bf16)[:, None, None], (local_count, 8, box_size))
    block_rows = box_size + 8
    packed = jnp.concatenate([templates, id_rows], axis=1).reshape(local_count * block_rows, box_size)
    split_last = lax.axis_size("orient") == 8 and lax.axis_size("tile") == 2
    split_last = split_last and local_count == 1 and (margin * tile_width) % box_size == 0
    if split_last:
        arrivals, row_padded = exchange_with_rows(packed, micrograph, margin)
        core = lax.axis_index("tile")
        edge = jnp.where(core == 0, row_padded[:, tile_width - margin :], row_padded[:, :margin])
        got = lax.ppermute(edge, "tile", [(0, 1), (1, 0)])
        zero = jnp.zeros_like(got)
        padded = jnp.concatenate(
            [jnp.where(core == 0, zero, got), row_padded, jnp.where(core == 0, got, zero)], axis=1
        )
    else:
        arrivals = exchange_rounds(packed)
        padded = extended(micrograph, (("orient", 0), ("tile", 1)), margin)
    total = sum(piece.shape[0] for piece in arrivals) // block_rows

    half_real = matmul(padded, cos_full).astype(bf16)
    half_imag = (-matmul(padded, sin_full)).astype(bf16)
    spec_real = (matmul(cos_full, half_real) + matmul(sin_full, half_imag)).astype(bf16)
    spec_imag = (matmul(cos_full, half_imag) - matmul(sin_full, half_real)).astype(bf16)

    tables = (
        cos_rows,
        sin_rows,
        jnp.concatenate([cos_cols, sin_cols], axis=0),
        jnp.concatenate([row_cos, row_sin], axis=0),
        col_cos,
        col_sin,
    )
    shape = (tile_width, tile_width)
    stats = ()
    live = usable.reshape(-1)[:1]

    def run(piece, stats, total=0):
        count = piece.shape[0] // block_rows
        piece = piece.reshape(count, block_rows, box_size)
        piece_ids = piece[:, box_size, 0].astype(jnp.int32)
        return correlate(piece_ids, live, piece, ctf, spec_real, spec_imag, tables, scaling, stats, total)

    if split_last:
        stats = run(arrivals[0], stats)
        half, stats = lax.optimization_barrier((arrivals[1], stats))
        other_half = lax.ppermute(half, "tile", [(0, 1), (1, 0)])
        total = (arrivals[0].shape[0] + 2 * half.shape[0]) // block_rows
        stats = run(jnp.concatenate([half, other_half], axis=0), stats, float(total))
    else:
        for last, piece in enumerate(arrivals, 1 - len(arrivals)):
            stats = run(piece, stats, 0 if last else float(total))
    return stats


def solution(mesh):
    return jax.shard_map(
        body,
        mesh=mesh,
        in_specs=(
            P(("groups", "orient"), "tile"),
            P("orient", None, None),
            P(("groups", "orient")),
            P("groups", None, None),
            P(("groups", "orient"), "tile"),
        ),
        out_specs=(
            P(("groups", "orient"), "tile"),
            P(("groups", "orient"), "tile"),
            P(("groups", "orient"), "tile"),
        ),
        check_vma=False,
    )
```

```python
import functools
import math

import jax
import jax.numpy as jnp
import ml_dtypes
import numpy as np
from jax import lax
from jax.experimental import pallas as pl
from jax.experimental.pallas import tpu as pltpu
from jax.sharding import PartitionSpec as P

RB = 32
CHUNK = 8


def extended(block, sides, width):
    for axis, dim in sides:
        count = lax.axis_size(axis)
        forward = [(i, i + 1) for i in range(count - 1)]
        backward = [(target, source) for source, target in forward]
        low = lax.ppermute(
            lax.slice_in_dim(block, block.shape[dim] - width, None, axis=dim), axis, forward
        )
        high = lax.ppermute(lax.slice_in_dim(block, 0, width, axis=dim), axis, backward)
        block = jnp.concatenate([low, block, high], axis=dim)
    return block


def twiddles(padded_size):
    position = np.arange(padded_size, dtype=np.int64)
    phase_index = (position[:, None] * position[None, :]) % padded_size
    angles = phase_index.astype(np.float32) * np.float32(2.0 * math.pi / padded_size)
    angles = angles.astype(np.float64)
    cosines = np.cos(angles).astype(np.float32).astype(ml_dtypes.bfloat16)
    sines = np.sin(angles).astype(np.float32).astype(ml_dtypes.bfloat16)
    return cosines, sines


def matmul(left, right):
    return jnp.dot(left, right, preferred_element_type=jnp.float32)


def exchange_rounds(block):
    size = lax.axis_size("orient")
    step = 1
    while step * 2 < size:
        step *= 2
    rounds = [block]
    held = block
    while step >= 1:
        other = lax.ppermute(held, "orient", [(i, i ^ step) for i in range(size)])
        if len(rounds) > 1:
            other, rounds[-1] = lax.optimization_barrier((other, rounds[-1]))
        rounds.append(other)
        held = jnp.concatenate([held, other], axis=0)
        step //= 2
    return rounds


def swap(payload, pairs):
    return lax.ppermute(payload, "orient", [(a, b) for a, b in pairs] + [(b, a) for a, b in pairs])


def exchange_with_rows(block, tile, width):
    size = lax.axis_size("orient")
    index = lax.axis_index("orient")
    odd = index % 2 == 1
    lanes = block.shape[1]

    def edge_rows(bottom):
        start = jnp.where(bottom, tile.shape[0] - width, 0)
        return lax.dynamic_slice_in_dim(tile, start, width, 0)

    def send(held, rows, pairs):
        padded_rows = jnp.pad(rows, ((0, 0), (0, lanes - rows.shape[1])))
        got = swap(jnp.concatenate([held, padded_rows], axis=0), pairs)
        return got[: held.shape[0]], got[held.shape[0] :, : tile.shape[1]]

    first, rows_one = send(block, edge_rows(jnp.logical_not(odd)), [(2 * i, 2 * i + 1) for i in range(size // 2)])
    held = jnp.concatenate([block, first], axis=0)
    core = lax.axis_index("tile")
    share = block.shape[0]
    mine = lax.dynamic_slice_in_dim(held, core * share, share, 0)
    second_pairs = [(2 * i + 1, 2 * i + 2) for i in range(size // 2 - 1)] + [(0, size - 1)]
    second, rows_two = send(mine, edge_rows(odd), second_pairs)
    third_pairs = [(0, size // 2), (size - 1, size // 2 - 1), (1, size // 2 + 1), (2, size // 2 + 2)]
    third = swap(jnp.concatenate([mine, second], axis=0), third_pairs)
    second_other = lax.ppermute(second, "tile", [(0, 1), (1, 0)])
    arrivals = [jnp.concatenate([held, second, second_other], axis=0), third]
    zero = jnp.zeros_like(rows_one)
    top = jnp.where(odd, rows_one, jnp.where(index == 0, zero, rows_two))
    bottom = jnp.where(odd, jnp.where(index == size - 1, zero, rows_two), rows_one)
    return arrivals, jnp.concatenate([top, tile, bottom], axis=0)


def correlate_kernel(ids_ref, live_ref, tmpl_ref, ctf_ref, spec_r_ref, spec_i_ref, cos_rows_ref, sin_rows_ref,
                     cols_ref, rows_ref, col_cos_ref, col_sin_ref, *refs, scaling, total, block):
    if len(refs) == 6:
        prev_peak_ref, prev_sum_ref, prev_sq_ref, peak_ref, sum_ref, sq_ref = refs
    else:
        peak_ref, sum_ref, sq_ref = refs
    bf16 = jnp.bfloat16
    f32 = jnp.float32
    o = pl.program_id(0)

    def mm(a, b):
        return jnp.dot(a, b, preferred_element_type=f32)

    template = tmpl_ref[0]
    part_real = mm(template, cos_rows_ref[...]).astype(bf16)
    part_imag = (-mm(template, sin_rows_ref[...])).astype(bf16)
    cols = cols_ref[...]
    n = cols.shape[0] // 2
    from_real = mm(cols, part_real)
    from_imag = mm(cols, part_imag)
    full_real = from_real[:n] + from_imag[n:]
    full_imag = from_imag[:n] - from_real[n:]
    weight = ctf_ref[0]
    w_real = (full_real * weight).astype(bf16).astype(f32)
    w_imag = (full_imag * weight).astype(bf16).astype(f32)
    spec_real = spec_r_ref[...].astype(f32)
    spec_imag = spec_i_ref[...].astype(f32)
    prod_real = (spec_real * w_real + spec_imag * w_imag).astype(bf16)
    prod_imag = (spec_imag * w_real - spec_real * w_imag).astype(bf16)
    rows = rows_ref[...]
    tile = rows.shape[0] // 2
    left_from_real = mm(rows, prod_real)
    left_from_imag = mm(rows, prod_imag)
    left_real = (left_from_real[:tile] - left_from_imag[tile:]).astype(bf16)
    left_imag = (left_from_imag[:tile] + left_from_real[tile:]).astype(bf16)
    corr = (mm(left_real, col_cos_ref[...]) - mm(left_imag, col_sin_ref[...])) * scaling

    @pl.when(o == 0)
    def _():
        if len(refs) == 6:
            peak_ref[...] = jnp.maximum(prev_peak_ref[...], corr)
            sum_ref[...] = prev_sum_ref[...] + corr
            sq_ref[...] = prev_sq_ref[...] + corr * corr
        else:
            peak_ref[...] = corr
            sum_ref[...] = corr
            sq_ref[...] = corr * corr

    @pl.when(o > 0)
    def _():
        peak_ref[...] = jnp.maximum(peak_ref[...], corr)
        sum_ref[...] = sum_ref[...] + corr
        sq_ref[...] = sq_ref[...] + corr * corr

    if total:
        @pl.when(o == pl.num_programs(0) - 1)
        def _():
            rows_at = lax.broadcasted_iota(jnp.int32, peak_ref.shape, 0)
            live = rows_at < block * live_ref[0]
            peak_ref[...] = jnp.where(live, peak_ref[...], 0.0)
            sum_ref[...] = jnp.where(live, sum_ref[...] / total, 0.0)
            sq_ref[...] = jnp.where(live, sq_ref[...] / total, 0.0)


def correlate(ids, live, all_templates, ctf, spec_real, spec_imag, tables, scaling, previous, total):
    count = all_templates.shape[0]
    box = all_templates.shape[2]
    n = ctf.shape[1]
    tile = tables[4].shape[1]
    full = lambda shape: pl.BlockSpec(shape, lambda o, ids, live: (0,) * len(shape))
    in_specs = [
        pl.BlockSpec((1, box, box), lambda o, ids, live: (o, 0, 0)),
        pl.BlockSpec((1, n, n), lambda o, ids, live: (ids[o], 0, 0)),
        full((n, n)),
        full((n, n)),
    ] + [full(t.shape) for t in tables] + [full((tile, tile))] * len(previous)
    out_block = full((tile, tile))
    grid_spec = pltpu.PrefetchScalarGridSpec(
        num_scalar_prefetch=2,
        grid=(count,),
        in_specs=in_specs,
        out_specs=[out_block, out_block, out_block],
    )
    out_shape = [jax.ShapeDtypeStruct((tile, tile), jnp.float32)] * 3
    return pl.pallas_call(
        functools.partial(correlate_kernel, scaling=scaling, total=total, block=RB),
        grid_spec=grid_spec,
        out_shape=out_shape,
        compiler_params=pltpu.CompilerParams(dimension_semantics=("arbitrary",)),
        input_output_aliases={6 + len(tables) + i: i for i in range(len(previous))},
    )(ids, live, all_templates, ctf, spec_real, spec_imag, *tables, *previous)


def body(micrograph, templates, defocus, ctf, usable):
    bf16 = jnp.bfloat16
    f32 = jnp.float32
    tile_width = micrograph.shape[0]
    padded_size = ctf.shape[1]
    box_size = templates.shape[1]
    margin = (padded_size - tile_width) // 2
    scaling = 1.0 / (padded_size * padded_size)
    n = padded_size
    cos_np, sin_np = twiddles(n)

    cos_full, sin_full = lax.optimization_barrier((jnp.asarray(cos_np), jnp.asarray(sin_np)))
    low = n - box_size // 2
    cos_rows = jnp.concatenate([cos_full[low:], cos_full[: box_size - (n - low)]], axis=0)
    sin_rows = jnp.concatenate([sin_full[low:], sin_full[: box_size - (n - low)]], axis=0)
    cos_cols = cos_rows.T
    sin_cols = sin_rows.T
    row_cos = cos_full[margin : margin + tile_width]
    row_sin = sin_full[margin : margin + tile_width]
    col_cos = row_cos.T
    col_sin = row_sin.T

    local_count = templates.shape[0]
    id_rows = jnp.broadcast_to(defocus.astype(bf16)[:, None, None], (local_count, 8, box_size))
    block_rows = box_size + 8
    packed = jnp.concatenate([templates, id_rows], axis=1).reshape(local_count * block_rows, box_size)
    split_last = lax.axis_size("orient") == 8 and lax.axis_size("tile") == 2
    split_last = split_last and local_count == 1 and tile_width <= box_size
    if split_last:
        arrivals, row_padded = exchange_with_rows(packed, micrograph, margin)
        core = lax.axis_index("tile")
        edge = jnp.where(core == 0, row_padded[:, tile_width - margin :], row_padded[:, :margin])
        got = lax.ppermute(edge, "tile", [(0, 1), (1, 0)])
        zero = jnp.zeros_like(got)
        padded = jnp.concatenate(
            [jnp.where(core == 0, zero, got), row_padded, jnp.where(core == 0, got, zero)], axis=1
        )
    else:
        arrivals = exchange_rounds(packed)
        padded = extended(micrograph, (("orient", 0), ("tile", 1)), margin)
    total = sum(piece.shape[0] for piece in arrivals) // block_rows

    half_real = matmul(padded, cos_full).astype(bf16)
    half_imag = (-matmul(padded, sin_full)).astype(bf16)
    spec_real = (matmul(cos_full, half_real) + matmul(sin_full, half_imag)).astype(bf16)
    spec_imag = (matmul(cos_full, half_imag) - matmul(sin_full, half_real)).astype(bf16)

    tables = (
        cos_rows,
        sin_rows,
        jnp.concatenate([cos_cols, sin_cols], axis=0),
        jnp.concatenate([row_cos, row_sin], axis=0),
        col_cos,
        col_sin,
    )
    shape = (tile_width, tile_width)
    stats = ()
    live = usable.reshape(-1)[:1]

    def run(piece, stats, total=0):
        count = piece.shape[0] // block_rows
        piece = piece.reshape(count, block_rows, box_size)
        piece_ids = piece[:, box_size, 0].astype(jnp.int32)
        return correlate(piece_ids, live, piece, ctf, spec_real, spec_imag, tables, scaling, stats, total)

    if split_last:
        stats = run(arrivals[0], stats)
        half, stats = lax.optimization_barrier((arrivals[1], stats))
        other_half = lax.ppermute(half, "tile", [(0, 1), (1, 0)])
        total = (arrivals[0].shape[0] + 2 * half.shape[0]) // block_rows
        stats = run(jnp.concatenate([half, other_half], axis=0), stats, float(total))
    else:
        for last, piece in enumerate(arrivals, 1 - len(arrivals)):
            stats = run(piece, stats, 0 if last else float(total))
    return stats


def solution(mesh):
    return jax.shard_map(
        body,
        mesh=mesh,
        in_specs=(
            P(("groups", "orient"), "tile"),
            P("orient", None, None),
            P(("groups", "orient")),
            P("groups", None, None),
            P(("groups", "orient"), "tile"),
        ),
        out_specs=(
            P(("groups", "orient"), "tile"),
            P(("groups", "orient"), "tile"),
            P(("groups", "orient"), "tile"),
        ),
        check_vma=False,
    )
```

```python
import functools
import math

import jax
import jax.numpy as jnp
import ml_dtypes
import numpy as np
from jax import lax
from jax.experimental import pallas as pl
from jax.experimental.pallas import tpu as pltpu
from jax.sharding import PartitionSpec as P

RB = 32
CHUNK = 8


def extended(block, sides, width):
    for axis, dim in sides:
        count = lax.axis_size(axis)
        forward = [(i, i + 1) for i in range(count - 1)]
        backward = [(target, source) for source, target in forward]
        low = lax.ppermute(
            lax.slice_in_dim(block, block.shape[dim] - width, None, axis=dim), axis, forward
        )
        high = lax.ppermute(lax.slice_in_dim(block, 0, width, axis=dim), axis, backward)
        block = jnp.concatenate([low, block, high], axis=dim)
    return block


def twiddles(padded_size):
    position = np.arange(padded_size, dtype=np.int64)
    phase_index = (position[:, None] * position[None, :]) % padded_size
    angles = phase_index.astype(np.float32) * np.float32(2.0 * math.pi / padded_size)
    angles = angles.astype(np.float64)
    cosines = np.cos(angles).astype(np.float32).astype(ml_dtypes.bfloat16)
    sines = np.sin(angles).astype(np.float32).astype(ml_dtypes.bfloat16)
    return cosines, sines


def matmul(left, right):
    return jnp.dot(left, right, preferred_element_type=jnp.float32)


def exchange_rounds(block):
    size = lax.axis_size("orient")
    step = 1
    while step * 2 < size:
        step *= 2
    rounds = [block]
    held = block
    while step >= 1:
        other = lax.ppermute(held, "orient", [(i, i ^ step) for i in range(size)])
        if len(rounds) > 1:
            other, rounds[-1] = lax.optimization_barrier((other, rounds[-1]))
        rounds.append(other)
        held = jnp.concatenate([held, other], axis=0)
        step //= 2
    return rounds


def swap(payload, pairs):
    return lax.ppermute(payload, "orient", [(a, b) for a, b in pairs] + [(b, a) for a, b in pairs])


def exchange_with_rows(parts, tile, width):
    size = lax.axis_size("orient")
    index = lax.axis_index("orient")
    odd = index % 2 == 1
    lanes = parts[0].shape[1]
    block = jnp.concatenate(parts, axis=0)

    def edge_rows(bottom):
        start = jnp.where(bottom, tile.shape[0] - width, 0)
        return lax.dynamic_slice_in_dim(tile, start, width, 0)

    def send(held, rows, pairs):
        held = held if isinstance(held, list) else [held]
        padded_rows = jnp.pad(rows, ((0, 0), (0, lanes - rows.shape[1])))
        got = swap(jnp.concatenate(held + [padded_rows], axis=0), pairs)
        count = sum(piece.shape[0] for piece in held)
        return got[:count], got[count:, : tile.shape[1]]

    first, rows_one = send(list(parts), edge_rows(jnp.logical_not(odd)), [(2 * i, 2 * i + 1) for i in range(size // 2)])
    held = jnp.concatenate([block, first], axis=0)
    core = lax.axis_index("tile")
    share = block.shape[0]
    mine = lax.dynamic_slice_in_dim(held, core * share, share, 0)
    second_pairs = [(2 * i + 1, 2 * i + 2) for i in range(size // 2 - 1)] + [(0, size - 1)]
    second, rows_two = send(mine, edge_rows(odd), second_pairs)
    third_pairs = [(0, size // 2), (size - 1, size // 2 - 1), (1, size // 2 + 1), (2, size // 2 + 2)]
    third = swap(jnp.concatenate([mine, second], axis=0), third_pairs)
    second_other = lax.ppermute(second, "tile", [(0, 1), (1, 0)])
    arrivals = [jnp.concatenate([held, second, second_other], axis=0), third]
    zero = jnp.zeros_like(rows_one)
    top = jnp.where(odd, rows_one, jnp.where(index == 0, zero, rows_two))
    bottom = jnp.where(odd, jnp.where(index == size - 1, zero, rows_two), rows_one)
    return arrivals, jnp.concatenate([top, tile, bottom], axis=0)


def correlate_kernel(ids_ref, live_ref, tmpl_ref, ctf_ref, spec_r_ref, spec_i_ref, cos_rows_ref, sin_rows_ref,
                     cols_ref, rows_ref, col_cos_ref, col_sin_ref, *refs, scaling, total, block):
    if len(refs) == 6:
        prev_peak_ref, prev_sum_ref, prev_sq_ref, peak_ref, sum_ref, sq_ref = refs
    else:
        peak_ref, sum_ref, sq_ref = refs
    bf16 = jnp.bfloat16
    f32 = jnp.float32
    o = pl.program_id(0)

    def mm(a, b):
        return jnp.dot(a, b, preferred_element_type=f32)

    template = tmpl_ref[0]
    part_real = mm(template, cos_rows_ref[...]).astype(bf16)
    part_imag = (-mm(template, sin_rows_ref[...])).astype(bf16)
    cols = cols_ref[...]
    n = cols.shape[0] // 2
    from_real = mm(cols, part_real)
    from_imag = mm(cols, part_imag)
    full_real = from_real[:n] + from_imag[n:]
    full_imag = from_imag[:n] - from_real[n:]
    weight = ctf_ref[0]
    w_real = (full_real * weight).astype(bf16).astype(f32)
    w_imag = (full_imag * weight).astype(bf16).astype(f32)
    spec_real = spec_r_ref[...].astype(f32)
    spec_imag = spec_i_ref[...].astype(f32)
    prod_real = (spec_real * w_real + spec_imag * w_imag).astype(bf16)
    prod_imag = (spec_imag * w_real - spec_real * w_imag).astype(bf16)
    rows = rows_ref[...]
    tile = rows.shape[0] // 2
    left_from_real = mm(rows, prod_real)
    left_from_imag = mm(rows, prod_imag)
    left_real = (left_from_real[:tile] - left_from_imag[tile:]).astype(bf16)
    left_imag = (left_from_imag[:tile] + left_from_real[tile:]).astype(bf16)
    corr = (mm(left_real, col_cos_ref[...]) - mm(left_imag, col_sin_ref[...])) * scaling

    @pl.when(o == 0)
    def _():
        if len(refs) == 6:
            peak_ref[...] = jnp.maximum(prev_peak_ref[...], corr)
            sum_ref[...] = prev_sum_ref[...] + corr
            sq_ref[...] = prev_sq_ref[...] + corr * corr
        else:
            peak_ref[...] = corr
            sum_ref[...] = corr
            sq_ref[...] = corr * corr

    @pl.when(o > 0)
    def _():
        peak_ref[...] = jnp.maximum(peak_ref[...], corr)
        sum_ref[...] = sum_ref[...] + corr
        sq_ref[...] = sq_ref[...] + corr * corr

    if total:
        @pl.when(o == pl.num_programs(0) - 1)
        def _():
            rows_at = lax.broadcasted_iota(jnp.int32, peak_ref.shape, 0)
            live = rows_at < block * live_ref[0]
            peak_ref[...] = jnp.where(live, peak_ref[...], 0.0)
            sum_ref[...] = jnp.where(live, sum_ref[...] / total, 0.0)
            sq_ref[...] = jnp.where(live, sq_ref[...] / total, 0.0)


def correlate(ids, live, all_templates, ctf, spec_real, spec_imag, tables, scaling, previous, total):
    count = all_templates.shape[0]
    box = all_templates.shape[2]
    n = ctf.shape[1]
    tile = tables[4].shape[1]
    full = lambda shape: pl.BlockSpec(shape, lambda o, ids, live: (0,) * len(shape))
    in_specs = [
        pl.BlockSpec((1, box, box), lambda o, ids, live: (o, 0, 0)),
        pl.BlockSpec((1, n, n), lambda o, ids, live: (ids[o], 0, 0)),
        full((n, n)),
        full((n, n)),
    ] + [full(t.shape) for t in tables] + [full((tile, tile))] * len(previous)
    out_block = full((tile, tile))
    grid_spec = pltpu.PrefetchScalarGridSpec(
        num_scalar_prefetch=2,
        grid=(count,),
        in_specs=in_specs,
        out_specs=[out_block, out_block, out_block],
    )
    out_shape = [jax.ShapeDtypeStruct((tile, tile), jnp.float32)] * 3
    return pl.pallas_call(
        functools.partial(correlate_kernel, scaling=scaling, total=total, block=RB),
        grid_spec=grid_spec,
        out_shape=out_shape,
        compiler_params=pltpu.CompilerParams(dimension_semantics=("arbitrary",)),
        input_output_aliases={6 + len(tables) + i: i for i in range(len(previous))},
    )(ids, live, all_templates, ctf, spec_real, spec_imag, *tables, *previous)


def body(micrograph, templates, defocus, ctf, usable):
    bf16 = jnp.bfloat16
    f32 = jnp.float32
    tile_width = micrograph.shape[0]
    padded_size = ctf.shape[1]
    box_size = templates.shape[1]
    margin = (padded_size - tile_width) // 2
    scaling = 1.0 / (padded_size * padded_size)
    n = padded_size
    cos_np, sin_np = twiddles(n)

    cos_full, sin_full = lax.optimization_barrier((jnp.asarray(cos_np), jnp.asarray(sin_np)))
    low = n - box_size // 2
    cos_rows = jnp.concatenate([cos_full[low:], cos_full[: box_size - (n - low)]], axis=0)
    sin_rows = jnp.concatenate([sin_full[low:], sin_full[: box_size - (n - low)]], axis=0)
    cos_cols = cos_rows.T
    sin_cols = sin_rows.T
    row_cos = cos_full[margin : margin + tile_width]
    row_sin = sin_full[margin : margin + tile_width]
    col_cos = row_cos.T
    col_sin = row_sin.T

    local_count = templates.shape[0]
    id_rows = jnp.broadcast_to(defocus.astype(bf16)[:, None, None], (local_count, 8, box_size))
    block_rows = box_size + 8
    packed = jnp.concatenate([templates, id_rows], axis=1).reshape(local_count * block_rows, box_size)
    split_last = lax.axis_size("orient") == 8 and lax.axis_size("tile") == 2
    split_last = split_last and local_count == 1 and tile_width <= box_size
    if split_last:
        arrivals, row_padded = exchange_with_rows([templates[0], id_rows[0]], micrograph, margin)
        core = lax.axis_index("tile")
        edge = jnp.where(core == 0, row_padded[:, tile_width - margin :], row_padded[:, :margin])
        got = lax.ppermute(edge, "tile", [(0, 1), (1, 0)])
        zero = jnp.zeros_like(got)
        padded = jnp.concatenate(
            [jnp.where(core == 0, zero, got), row_padded, jnp.where(core == 0, got, zero)], axis=1
        )
    else:
        arrivals = exchange_rounds(packed)
        padded = extended(micrograph, (("orient", 0), ("tile", 1)), margin)
    total = sum(piece.shape[0] for piece in arrivals) // block_rows

    half_real = matmul(padded, cos_full).astype(bf16)
    half_imag = (-matmul(padded, sin_full)).astype(bf16)
    spec_real = (matmul(cos_full, half_real) + matmul(sin_full, half_imag)).astype(bf16)
    spec_imag = (matmul(cos_full, half_imag) - matmul(sin_full, half_real)).astype(bf16)

    tables = (
        cos_rows,
        sin_rows,
        jnp.concatenate([cos_cols, sin_cols], axis=0),
        jnp.concatenate([row_cos, row_sin], axis=0),
        col_cos,
        col_sin,
    )
    shape = (tile_width, tile_width)
    stats = ()
    live = usable.reshape(-1)[:1]

    def run(piece, stats, total=0):
        count = piece.shape[0] // block_rows
        piece = piece.reshape(count, block_rows, box_size)
        piece_ids = piece[:, box_size, 0].astype(jnp.int32)
        return correlate(piece_ids, live, piece, ctf, spec_real, spec_imag, tables, scaling, stats, total)

    if split_last:
        stats = run(arrivals[0], stats)
        half, stats = lax.optimization_barrier((arrivals[1], stats))
        other_half = lax.ppermute(half, "tile", [(0, 1), (1, 0)])
        total = (arrivals[0].shape[0] + 2 * half.shape[0]) // block_rows
        stats = run(jnp.concatenate([half, other_half], axis=0), stats, float(total))
    else:
        for last, piece in enumerate(arrivals, 1 - len(arrivals)):
            stats = run(piece, stats, 0 if last else float(total))
    return stats


def solution(mesh):
    return jax.shard_map(
        body,
        mesh=mesh,
        in_specs=(
            P(("groups", "orient"), "tile"),
            P("orient", None, None),
            P(("groups", "orient")),
            P("groups", None, None),
            P(("groups", "orient"), "tile"),
        ),
        out_specs=(
            P(("groups", "orient"), "tile"),
            P(("groups", "orient"), "tile"),
            P(("groups", "orient"), "tile"),
        ),
        check_vma=False,
    )
```

```python
import functools
import math

import jax
import jax.numpy as jnp
import ml_dtypes
import numpy as np
from jax import lax
from jax.experimental import pallas as pl
from jax.experimental.pallas import tpu as pltpu
from jax.sharding import PartitionSpec as P

RB = 32
CHUNK = 8


def extended(block, sides, width):
    for axis, dim in sides:
        count = lax.axis_size(axis)
        forward = [(i, i + 1) for i in range(count - 1)]
        backward = [(target, source) for source, target in forward]
        low = lax.ppermute(
            lax.slice_in_dim(block, block.shape[dim] - width, None, axis=dim), axis, forward
        )
        high = lax.ppermute(lax.slice_in_dim(block, 0, width, axis=dim), axis, backward)
        block = jnp.concatenate([low, block, high], axis=dim)
    return block


def twiddles(padded_size):
    position = np.arange(padded_size, dtype=np.int64)
    phase_index = (position[:, None] * position[None, :]) % padded_size
    angles = phase_index.astype(np.float32) * np.float32(2.0 * math.pi / padded_size)
    angles = angles.astype(np.float64)
    cosines = np.cos(angles).astype(np.float32).astype(ml_dtypes.bfloat16)
    sines = np.sin(angles).astype(np.float32).astype(ml_dtypes.bfloat16)
    return cosines, sines


def matmul(left, right):
    return jnp.dot(left, right, preferred_element_type=jnp.float32)


def exchange_rounds(block):
    size = lax.axis_size("orient")
    step = 1
    while step * 2 < size:
        step *= 2
    rounds = [block]
    held = block
    while step >= 1:
        other = lax.ppermute(held, "orient", [(i, i ^ step) for i in range(size)])
        if len(rounds) > 1:
            other, rounds[-1] = lax.optimization_barrier((other, rounds[-1]))
        rounds.append(other)
        held = jnp.concatenate([held, other], axis=0)
        step //= 2
    return rounds


def swap(payload, pairs):
    return lax.ppermute(payload, "orient", [(a, b) for a, b in pairs] + [(b, a) for a, b in pairs])


def exchange_with_rows(block, tile, width):
    size = lax.axis_size("orient")
    index = lax.axis_index("orient")
    odd = index % 2 == 1
    low_rows = tile[tile.shape[0] - width :]
    high_rows = tile[:width]
    lanes = block.shape[1]
    carried = width * tile.shape[1] // lanes

    def send(held, rows, pairs):
        payload = jnp.concatenate([held, rows.reshape(carried, lanes)], axis=0)
        got = swap(payload, pairs)
        return got[: held.shape[0]], got[held.shape[0] :].reshape(width, tile.shape[1])

    first, rows_one = send(block, jnp.where(odd, high_rows, low_rows), [(2 * i, 2 * i + 1) for i in range(size // 2)])
    held = jnp.concatenate([block, first], axis=0)
    second_pairs = [(2 * i + 1, 2 * i + 2) for i in range(size // 2 - 1)] + [(0, size - 1)]
    second, rows_two = send(held, jnp.where(odd, low_rows, high_rows), second_pairs)
    held = jnp.concatenate([held, second], axis=0)
    third_pairs = [(0, size // 2), (size - 1, size // 2 - 1), (1, size // 2 + 1), (2, size // 2 + 2)]
    cores = lax.axis_size("tile")
    share = held.shape[0] // cores
    core = lax.axis_index("tile")
    mine = lax.dynamic_slice_in_dim(held, core * share, share, 0)
    third = swap(mine, third_pairs)
    arrivals = [held, third]
    zero = jnp.zeros_like(rows_one)
    top = jnp.where(odd, rows_one, jnp.where(index == 0, zero, rows_two))
    bottom = jnp.where(odd, jnp.where(index == size - 1, zero, rows_two), rows_one)
    return arrivals, jnp.concatenate([top, tile, bottom], axis=0)


def correlate_kernel(ids_ref, live_ref, tmpl_ref, other_ref, ctf_ref, spec_r_ref, spec_i_ref, cos_rows_ref,
                     sin_rows_ref, cols_ref, rows_ref, col_cos_ref, col_sin_ref, *refs, scaling, total, block, first):
    if len(refs) == 6:
        prev_peak_ref, prev_sum_ref, prev_sq_ref, peak_ref, sum_ref, sq_ref = refs
    else:
        peak_ref, sum_ref, sq_ref = refs
    bf16 = jnp.bfloat16
    f32 = jnp.float32
    o = pl.program_id(0)

    def mm(a, b):
        return jnp.dot(a, b, preferred_element_type=f32)

    template = jnp.where(o < first, tmpl_ref[0], other_ref[0])
    part_real = mm(template, cos_rows_ref[...]).astype(bf16)
    part_imag = (-mm(template, sin_rows_ref[...])).astype(bf16)
    cols = cols_ref[...]
    n = cols.shape[0] // 2
    from_real = mm(cols, part_real)
    from_imag = mm(cols, part_imag)
    full_real = from_real[:n] + from_imag[n:]
    full_imag = from_imag[:n] - from_real[n:]
    weight = ctf_ref[0]
    w_real = (full_real * weight).astype(bf16).astype(f32)
    w_imag = (full_imag * weight).astype(bf16).astype(f32)
    spec_real = spec_r_ref[...].astype(f32)
    spec_imag = spec_i_ref[...].astype(f32)
    prod_real = (spec_real * w_real + spec_imag * w_imag).astype(bf16)
    prod_imag = (spec_imag * w_real - spec_real * w_imag).astype(bf16)
    rows = rows_ref[...]
    tile = rows.shape[0] // 2
    left_from_real = mm(rows, prod_real)
    left_from_imag = mm(rows, prod_imag)
    left_real = (left_from_real[:tile] - left_from_imag[tile:]).astype(bf16)
    left_imag = (left_from_imag[:tile] + left_from_real[tile:]).astype(bf16)
    corr = (mm(left_real, col_cos_ref[...]) - mm(left_imag, col_sin_ref[...])) * scaling

    @pl.when(o == 0)
    def _():
        if len(refs) == 6:
            peak_ref[...] = jnp.maximum(prev_peak_ref[...], corr)
            sum_ref[...] = prev_sum_ref[...] + corr
            sq_ref[...] = prev_sq_ref[...] + corr * corr
        else:
            peak_ref[...] = corr
            sum_ref[...] = corr
            sq_ref[...] = corr * corr

    @pl.when(o > 0)
    def _():
        peak_ref[...] = jnp.maximum(peak_ref[...], corr)
        sum_ref[...] = sum_ref[...] + corr
        sq_ref[...] = sq_ref[...] + corr * corr

    if total:
        @pl.when(o == pl.num_programs(0) - 1)
        def _():
            rows_at = lax.broadcasted_iota(jnp.int32, peak_ref.shape, 0)
            live = rows_at < block * live_ref[0]
            peak_ref[...] = jnp.where(live, peak_ref[...], 0.0)
            sum_ref[...] = jnp.where(live, sum_ref[...] / total, 0.0)
            sq_ref[...] = jnp.where(live, sq_ref[...] / total, 0.0)


def correlate(ids, live, pieces, ctf, spec_real, spec_imag, tables, scaling, previous, total):
    pieces = list(pieces)
    first = pieces[0].shape[0]
    count = sum(piece.shape[0] for piece in pieces)
    if len(pieces) == 1:
        pieces.append(pieces[0])
    last_other = pieces[1].shape[0] - 1
    box = pieces[0].shape[2]
    n = ctf.shape[1]
    tile = tables[4].shape[1]
    full = lambda shape: pl.BlockSpec(shape, lambda o, ids, live: (0,) * len(shape))
    in_specs = [
        pl.BlockSpec((1, box, box), lambda o, ids, live: (jnp.minimum(o, first - 1), 0, 0)),
        pl.BlockSpec((1, box, box), lambda o, ids, live: (jnp.clip(o - first, 0, last_other), 0, 0)),
        pl.BlockSpec((1, n, n), lambda o, ids, live: (ids[o], 0, 0)),
        full((n, n)),
        full((n, n)),
    ] + [full(t.shape) for t in tables] + [full((tile, tile))] * len(previous)
    out_block = full((tile, tile))
    grid_spec = pltpu.PrefetchScalarGridSpec(
        num_scalar_prefetch=2,
        grid=(count,),
        in_specs=in_specs,
        out_specs=[out_block, out_block, out_block],
    )
    out_shape = [jax.ShapeDtypeStruct((tile, tile), jnp.float32)] * 3
    kernel = functools.partial(correlate_kernel, scaling=scaling, total=total, block=RB, first=first)
    return pl.pallas_call(
        kernel,
        grid_spec=grid_spec,
        out_shape=out_shape,
        compiler_params=pltpu.CompilerParams(dimension_semantics=("arbitrary",)),
        input_output_aliases={7 + len(tables) + i: i for i in range(len(previous))},
    )(ids, live, pieces[0], pieces[1], ctf, spec_real, spec_imag, *tables, *previous)


def body(micrograph, templates, defocus, ctf, usable):
    bf16 = jnp.bfloat16
    f32 = jnp.float32
    tile_width = micrograph.shape[0]
    padded_size = ctf.shape[1]
    box_size = templates.shape[1]
    margin = (padded_size - tile_width) // 2
    scaling = 1.0 / (padded_size * padded_size)
    n = padded_size
    cos_np, sin_np = twiddles(n)

    cos_full, sin_full = lax.optimization_barrier((jnp.asarray(cos_np), jnp.asarray(sin_np)))
    low = n - box_size // 2
    cos_rows = jnp.concatenate([cos_full[low:], cos_full[: box_size - (n - low)]], axis=0)
    sin_rows = jnp.concatenate([sin_full[low:], sin_full[: box_size - (n - low)]], axis=0)
    cos_cols = cos_rows.T
    sin_cols = sin_rows.T
    row_cos = cos_full[margin : margin + tile_width]
    row_sin = sin_full[margin : margin + tile_width]
    col_cos = row_cos.T
    col_sin = row_sin.T

    local_count = templates.shape[0]
    id_rows = jnp.broadcast_to(defocus.astype(bf16)[:, None, None], (local_count, 8, box_size))
    block_rows = box_size + 8
    packed = jnp.concatenate([templates, id_rows], axis=1).reshape(local_count * block_rows, box_size)
    split_last = lax.axis_size("orient") == 8 and lax.axis_size("tile") == 2
    split_last = split_last and local_count == 1 and (margin * tile_width) % box_size == 0
    if split_last:
        arrivals, row_padded = exchange_with_rows(packed, micrograph, margin)
        core = lax.axis_index("tile")
        edge = jnp.where(core == 0, row_padded[:, tile_width - margin :], row_padded[:, :margin])
        got = lax.ppermute(edge, "tile", [(0, 1), (1, 0)])
        zero = jnp.zeros_like(got)
        padded = jnp.concatenate(
            [jnp.where(core == 0, zero, got), row_padded, jnp.where(core == 0, got, zero)], axis=1
        )
    else:
        arrivals = exchange_rounds(packed)
        padded = extended(micrograph, (("orient", 0), ("tile", 1)), margin)
    total = sum(piece.shape[0] for piece in arrivals) // block_rows

    half_real = matmul(padded, cos_full).astype(bf16)
    half_imag = (-matmul(padded, sin_full)).astype(bf16)
    spec_real = (matmul(cos_full, half_real) + matmul(sin_full, half_imag)).astype(bf16)
    spec_imag = (matmul(cos_full, half_imag) - matmul(sin_full, half_real)).astype(bf16)

    tables = (
        cos_rows,
        sin_rows,
        jnp.concatenate([cos_cols, sin_cols], axis=0),
        jnp.concatenate([row_cos, row_sin], axis=0),
        col_cos,
        col_sin,
    )
    shape = (tile_width, tile_width)
    stats = ()
    live = usable.reshape(-1)[:1]

    def run(pieces, stats, total=0):
        pieces = [piece.reshape(piece.shape[0] // block_rows, block_rows, box_size) for piece in pieces]
        piece_ids = jnp.concatenate([piece[:, box_size, 0] for piece in pieces]).astype(jnp.int32)
        return correlate(piece_ids, live, pieces, ctf, spec_real, spec_imag, tables, scaling, stats, total)

    if split_last:
        stats = run([arrivals[0]], stats)
        half, stats = lax.optimization_barrier((arrivals[1], stats))
        other_half = lax.ppermute(half, "tile", [(0, 1), (1, 0)])
        total = (arrivals[0].shape[0] + 2 * half.shape[0]) // block_rows
        stats = run([half, other_half], stats, float(total))
    else:
        for last, piece in enumerate(arrivals, 1 - len(arrivals)):
            stats = run([piece], stats, 0 if last else float(total))
    return stats


def solution(mesh):
    return jax.shard_map(
        body,
        mesh=mesh,
        in_specs=(
            P(("groups", "orient"), "tile"),
            P("orient", None, None),
            P(("groups", "orient")),
            P("groups", None, None),
            P(("groups", "orient"), "tile"),
        ),
        out_specs=(
            P(("groups", "orient"), "tile"),
            P(("groups", "orient"), "tile"),
            P(("groups", "orient"), "tile"),
        ),
        check_vma=False,
    )
```

```python
import functools
import math

import jax
import jax.numpy as jnp
import ml_dtypes
import numpy as np
from jax import lax
from jax.experimental import pallas as pl
from jax.experimental.pallas import tpu as pltpu
from jax.sharding import PartitionSpec as P

RB = 32
CHUNK = 8


def extended(block, sides, width):
    for axis, dim in sides:
        count = lax.axis_size(axis)
        forward = [(i, i + 1) for i in range(count - 1)]
        backward = [(target, source) for source, target in forward]
        low = lax.ppermute(
            lax.slice_in_dim(block, block.shape[dim] - width, None, axis=dim), axis, forward
        )
        high = lax.ppermute(lax.slice_in_dim(block, 0, width, axis=dim), axis, backward)
        block = jnp.concatenate([low, block, high], axis=dim)
    return block


def twiddles(padded_size):
    position = np.arange(padded_size, dtype=np.int64)
    phase_index = (position[:, None] * position[None, :]) % padded_size
    angles = phase_index.astype(np.float32) * np.float32(2.0 * math.pi / padded_size)
    angles = angles.astype(np.float64)
    cosines = np.cos(angles).astype(np.float32).astype(ml_dtypes.bfloat16)
    sines = np.sin(angles).astype(np.float32).astype(ml_dtypes.bfloat16)
    return cosines, sines


def matmul(left, right):
    return jnp.dot(left, right, preferred_element_type=jnp.float32)


def exchange_rounds(block):
    size = lax.axis_size("orient")
    step = 1
    while step * 2 < size:
        step *= 2
    rounds = [block]
    held = block
    while step >= 1:
        other = lax.ppermute(held, "orient", [(i, i ^ step) for i in range(size)])
        if len(rounds) > 1:
            other, rounds[-1] = lax.optimization_barrier((other, rounds[-1]))
        rounds.append(other)
        held = jnp.concatenate([held, other], axis=0)
        step //= 2
    return rounds


def swap(payload, pairs):
    return lax.ppermute(payload, "orient", [(a, b) for a, b in pairs] + [(b, a) for a, b in pairs])


def exchange_with_rows(block, tile, width):
    size = lax.axis_size("orient")
    index = lax.axis_index("orient")
    odd = index % 2 == 1
    low_rows = tile[tile.shape[0] - width :]
    high_rows = tile[:width]
    lanes = block.shape[1]
    carried = width * tile.shape[1] // lanes

    def send(held, rows, pairs):
        payload = jnp.concatenate([held, rows.reshape(carried, lanes)], axis=0)
        got = swap(payload, pairs)
        return got[: held.shape[0]], got[held.shape[0] :].reshape(width, tile.shape[1])

    first, rows_one = send(block, jnp.where(odd, high_rows, low_rows), [(2 * i, 2 * i + 1) for i in range(size // 2)])
    held = jnp.concatenate([block, first], axis=0)
    second_pairs = [(2 * i + 1, 2 * i + 2) for i in range(size // 2 - 1)] + [(0, size - 1)]
    second, rows_two = send(held, jnp.where(odd, low_rows, high_rows), second_pairs)
    held = jnp.concatenate([held, second], axis=0)
    third_pairs = [(0, size // 2), (size - 1, size // 2 - 1), (1, size // 2 + 1), (2, size // 2 + 2)]
    cores = lax.axis_size("tile")
    share = held.shape[0] // cores
    core = lax.axis_index("tile")
    mine = lax.dynamic_slice_in_dim(held, core * share, share, 0)
    third = swap(mine, third_pairs)
    arrivals = [held, third]
    zero = jnp.zeros_like(rows_one)
    top = jnp.where(odd, rows_one, jnp.where(index == 0, zero, rows_two))
    bottom = jnp.where(odd, jnp.where(index == size - 1, zero, rows_two), rows_one)
    return arrivals, jnp.concatenate([top, tile, bottom], axis=0)


def correlate_kernel(ids_ref, live_ref, tmpl_ref, other_ref, *refs, scaling, total, block, first, group):
    ctf_refs = refs[:group]
    (spec_r_ref, spec_i_ref, cos_rows_ref, sin_rows_ref, cols_ref, rows_ref, col_cos_ref, col_sin_ref) = refs[
        group : group + 8
    ]
    refs = refs[group + 8 :]
    if len(refs) == 6:
        prev_peak_ref, prev_sum_ref, prev_sq_ref, peak_ref, sum_ref, sq_ref = refs
    else:
        peak_ref, sum_ref, sq_ref = refs
    bf16 = jnp.bfloat16
    f32 = jnp.float32
    o = pl.program_id(0)

    def mm(a, b):
        return jnp.dot(a, b, preferred_element_type=f32)

    def one(g):
        template = jnp.where(o < first, tmpl_ref[g], other_ref[g])
        part_real = mm(template, cos_rows_ref[...]).astype(bf16)
        part_imag = (-mm(template, sin_rows_ref[...])).astype(bf16)
        cols = cols_ref[...]
        n = cols.shape[0] // 2
        from_real = mm(cols, part_real)
        from_imag = mm(cols, part_imag)
        full_real = from_real[:n] + from_imag[n:]
        full_imag = from_imag[:n] - from_real[n:]
        weight = ctf_refs[g][0]
        w_real = (full_real * weight).astype(bf16).astype(f32)
        w_imag = (full_imag * weight).astype(bf16).astype(f32)
        spec_real = spec_r_ref[...].astype(f32)
        spec_imag = spec_i_ref[...].astype(f32)
        prod_real = (spec_real * w_real + spec_imag * w_imag).astype(bf16)
        prod_imag = (spec_imag * w_real - spec_real * w_imag).astype(bf16)
        rows = rows_ref[...]
        tile = rows.shape[0] // 2
        left_from_real = mm(rows, prod_real)
        left_from_imag = mm(rows, prod_imag)
        left_real = (left_from_real[:tile] - left_from_imag[tile:]).astype(bf16)
        left_imag = (left_from_imag[:tile] + left_from_real[tile:]).astype(bf16)
        return (mm(left_real, col_cos_ref[...]) - mm(left_imag, col_sin_ref[...])) * scaling

    corrs = [one(g) for g in range(group)]
    step_peak = corrs[0]
    step_sum = corrs[0]
    step_sq = corrs[0] * corrs[0]
    for corr in corrs[1:]:
        step_peak = jnp.maximum(step_peak, corr)
        step_sum = step_sum + corr
        step_sq = step_sq + corr * corr

    @pl.when(o == 0)
    def _():
        if len(refs) == 6:
            peak_ref[...] = jnp.maximum(prev_peak_ref[...], step_peak)
            sum_ref[...] = prev_sum_ref[...] + step_sum
            sq_ref[...] = prev_sq_ref[...] + step_sq
        else:
            peak_ref[...] = step_peak
            sum_ref[...] = step_sum
            sq_ref[...] = step_sq

    @pl.when(o > 0)
    def _():
        peak_ref[...] = jnp.maximum(peak_ref[...], step_peak)
        sum_ref[...] = sum_ref[...] + step_sum
        sq_ref[...] = sq_ref[...] + step_sq

    if total:
        @pl.when(o == pl.num_programs(0) - 1)
        def _():
            rows_at = lax.broadcasted_iota(jnp.int32, peak_ref.shape, 0)
            live = rows_at < block * live_ref[0]
            peak_ref[...] = jnp.where(live, peak_ref[...], 0.0)
            sum_ref[...] = jnp.where(live, sum_ref[...] / total, 0.0)
            sq_ref[...] = jnp.where(live, sq_ref[...] / total, 0.0)


def correlate(ids, live, pieces, ctf, spec_real, spec_imag, tables, scaling, previous, total):
    pieces = list(pieces)
    group = 2 if all(piece.shape[0] % 2 == 0 for piece in pieces) else 1
    first = pieces[0].shape[0] // group
    steps = sum(piece.shape[0] for piece in pieces) // group
    if len(pieces) == 1:
        pieces.append(pieces[0])
    last_other = pieces[1].shape[0] // group - 1
    box = pieces[0].shape[2]
    n = ctf.shape[1]
    tile = tables[4].shape[1]
    full = lambda shape: pl.BlockSpec(shape, lambda o, ids, live: (0,) * len(shape))

    def plane(g):
        return pl.BlockSpec((1, n, n), lambda o, ids, live: (ids[o * group + g], 0, 0))

    in_specs = (
        [
            pl.BlockSpec((group, box, box), lambda o, ids, live: (jnp.minimum(o, first - 1), 0, 0)),
            pl.BlockSpec((group, box, box), lambda o, ids, live: (jnp.clip(o - first, 0, last_other), 0, 0)),
        ]
        + [plane(g) for g in range(group)]
        + [full((n, n)), full((n, n))]
        + [full(t.shape) for t in tables]
        + [full((tile, tile))] * len(previous)
    )
    out_block = full((tile, tile))
    grid_spec = pltpu.PrefetchScalarGridSpec(
        num_scalar_prefetch=2,
        grid=(steps,),
        in_specs=in_specs,
        out_specs=[out_block, out_block, out_block],
    )
    out_shape = [jax.ShapeDtypeStruct((tile, tile), jnp.float32)] * 3
    kernel = functools.partial(
        correlate_kernel, scaling=scaling, total=total, block=RB, first=first, group=group
    )
    base = 4 + group + 2 + len(tables)
    return pl.pallas_call(
        kernel,
        grid_spec=grid_spec,
        out_shape=out_shape,
        compiler_params=pltpu.CompilerParams(dimension_semantics=("arbitrary",)),
        input_output_aliases={base + i: i for i in range(len(previous))},
    )(ids, live, pieces[0], pieces[1], *([ctf] * group), spec_real, spec_imag, *tables, *previous)


def body(micrograph, templates, defocus, ctf, usable):
    bf16 = jnp.bfloat16
    f32 = jnp.float32
    tile_width = micrograph.shape[0]
    padded_size = ctf.shape[1]
    box_size = templates.shape[1]
    margin = (padded_size - tile_width) // 2
    scaling = 1.0 / (padded_size * padded_size)
    n = padded_size
    cos_np, sin_np = twiddles(n)

    cos_full, sin_full = lax.optimization_barrier((jnp.asarray(cos_np), jnp.asarray(sin_np)))
    low = n - box_size // 2
    cos_rows = jnp.concatenate([cos_full[low:], cos_full[: box_size - (n - low)]], axis=0)
    sin_rows = jnp.concatenate([sin_full[low:], sin_full[: box_size - (n - low)]], axis=0)
    cos_cols = cos_rows.T
    sin_cols = sin_rows.T
    row_cos = cos_full[margin : margin + tile_width]
    row_sin = sin_full[margin : margin + tile_width]
    col_cos = row_cos.T
    col_sin = row_sin.T

    local_count = templates.shape[0]
    id_rows = jnp.broadcast_to(defocus.astype(bf16)[:, None, None], (local_count, 8, box_size))
    block_rows = box_size + 8
    packed = jnp.concatenate([templates, id_rows], axis=1).reshape(local_count * block_rows, box_size)
    split_last = lax.axis_size("orient") == 8 and lax.axis_size("tile") == 2
    split_last = split_last and local_count == 1 and (margin * tile_width) % box_size == 0
    if split_last:
        arrivals, row_padded = exchange_with_rows(packed, micrograph, margin)
        core = lax.axis_index("tile")
        edge = jnp.where(core == 0, row_padded[:, tile_width - margin :], row_padded[:, :margin])
        got = lax.ppermute(edge, "tile", [(0, 1), (1, 0)])
        zero = jnp.zeros_like(got)
        padded = jnp.concatenate(
            [jnp.where(core == 0, zero, got), row_padded, jnp.where(core == 0, got, zero)], axis=1
        )
    else:
        arrivals = exchange_rounds(packed)
        padded = extended(micrograph, (("orient", 0), ("tile", 1)), margin)
    total = sum(piece.shape[0] for piece in arrivals) // block_rows

    half_real = matmul(padded, cos_full).astype(bf16)
    half_imag = (-matmul(padded, sin_full)).astype(bf16)
    spec_real = (matmul(cos_full, half_real) + matmul(sin_full, half_imag)).astype(bf16)
    spec_imag = (matmul(cos_full, half_imag) - matmul(sin_full, half_real)).astype(bf16)

    tables = (
        cos_rows,
        sin_rows,
        jnp.concatenate([cos_cols, sin_cols], axis=0),
        jnp.concatenate([row_cos, row_sin], axis=0),
        col_cos,
        col_sin,
    )
    shape = (tile_width, tile_width)
    stats = ()
    live = usable.reshape(-1)[:1]

    def run(pieces, stats, total=0):
        pieces = [piece.reshape(piece.shape[0] // block_rows, block_rows, box_size) for piece in pieces]
        piece_ids = jnp.concatenate([piece[:, box_size, 0] for piece in pieces]).astype(jnp.int32)
        return correlate(piece_ids, live, pieces, ctf, spec_real, spec_imag, tables, scaling, stats, total)

    if split_last:
        stats = run([arrivals[0]], stats)
        half, stats = lax.optimization_barrier((arrivals[1], stats))
        other_half = lax.ppermute(half, "tile", [(0, 1), (1, 0)])
        total = (arrivals[0].shape[0] + 2 * half.shape[0]) // block_rows
        stats = run([half, other_half], stats, float(total))
    else:
        for last, piece in enumerate(arrivals, 1 - len(arrivals)):
            stats = run([piece], stats, 0 if last else float(total))
    return stats


def solution(mesh):
    return jax.shard_map(
        body,
        mesh=mesh,
        in_specs=(
            P(("groups", "orient"), "tile"),
            P("orient", None, None),
            P(("groups", "orient")),
            P("groups", None, None),
            P(("groups", "orient"), "tile"),
        ),
        out_specs=(
            P(("groups", "orient"), "tile"),
            P(("groups", "orient"), "tile"),
            P(("groups", "orient"), "tile"),
        ),
        check_vma=False,
    )
```

```python
import functools
import math

import jax
import jax.numpy as jnp
import ml_dtypes
import numpy as np
from jax import lax
from jax.experimental import pallas as pl
from jax.experimental.pallas import tpu as pltpu
from jax.sharding import PartitionSpec as P

RB = 32
CHUNK = 8


def extended(block, sides, width):
    for axis, dim in sides:
        count = lax.axis_size(axis)
        forward = [(i, i + 1) for i in range(count - 1)]
        backward = [(target, source) for source, target in forward]
        low = lax.ppermute(
            lax.slice_in_dim(block, block.shape[dim] - width, None, axis=dim), axis, forward
        )
        high = lax.ppermute(lax.slice_in_dim(block, 0, width, axis=dim), axis, backward)
        block = jnp.concatenate([low, block, high], axis=dim)
    return block


def twiddles(padded_size):
    position = np.arange(padded_size, dtype=np.int64)
    phase_index = (position[:, None] * position[None, :]) % padded_size
    angles = phase_index.astype(np.float32) * np.float32(2.0 * math.pi / padded_size)
    angles = angles.astype(np.float64)
    cosines = np.cos(angles).astype(np.float32).astype(ml_dtypes.bfloat16)
    sines = np.sin(angles).astype(np.float32).astype(ml_dtypes.bfloat16)
    return cosines, sines


def matmul(left, right):
    return jnp.dot(left, right, preferred_element_type=jnp.float32)


def exchange_rounds(block):
    size = lax.axis_size("orient")
    step = 1
    while step * 2 < size:
        step *= 2
    rounds = [block]
    held = block
    while step >= 1:
        other = lax.ppermute(held, "orient", [(i, i ^ step) for i in range(size)])
        if len(rounds) > 1:
            other, rounds[-1] = lax.optimization_barrier((other, rounds[-1]))
        rounds.append(other)
        held = jnp.concatenate([held, other], axis=0)
        step //= 2
    return rounds


def swap(payload, pairs):
    return lax.ppermute(payload, "orient", [(a, b) for a, b in pairs] + [(b, a) for a, b in pairs])


def exchange_with_rows(block, tile, width):
    size = lax.axis_size("orient")
    index = lax.axis_index("orient")
    odd = index % 2 == 1
    low_rows = tile[tile.shape[0] - width :]
    high_rows = tile[:width]
    lanes = block.shape[1]
    carried = width * tile.shape[1] // lanes

    def send(held, rows, pairs):
        payload = jnp.concatenate([held, rows.reshape(carried, lanes)], axis=0)
        got = swap(payload, pairs)
        return got[: held.shape[0]], got[held.shape[0] :].reshape(width, tile.shape[1])

    first, rows_one = send(block, jnp.where(odd, high_rows, low_rows), [(2 * i, 2 * i + 1) for i in range(size // 2)])
    held = jnp.concatenate([block, first], axis=0)
    second_pairs = [(2 * i + 1, 2 * i + 2) for i in range(size // 2 - 1)] + [(0, size - 1)]
    second, rows_two = send(held, jnp.where(odd, low_rows, high_rows), second_pairs)
    held = jnp.concatenate([held, second], axis=0)
    third_pairs = [(0, size // 2), (size - 1, size // 2 - 1), (1, size // 2 + 1), (2, size // 2 + 2)]
    cores = lax.axis_size("tile")
    share = held.shape[0] // cores
    core = lax.axis_index("tile")
    mine = lax.dynamic_slice_in_dim(held, core * share, share, 0)
    third = swap(mine, third_pairs)
    arrivals = [held, third]
    zero = jnp.zeros_like(rows_one)
    top = jnp.where(odd, rows_one, jnp.where(index == 0, zero, rows_two))
    bottom = jnp.where(odd, jnp.where(index == size - 1, zero, rows_two), rows_one)
    return arrivals, jnp.concatenate([top, tile, bottom], axis=0)


def correlate_kernel(ids_ref, live_ref, tmpl_ref, other_ref, *refs, scaling, total, block, first, group):
    ctf_refs = refs[:group]
    (spec_r_ref, spec_i_ref, cos_rows_ref, sin_rows_ref, cols_ref, rows_ref, col_cos_ref, col_sin_ref) = refs[
        group : group + 8
    ]
    refs = refs[group + 8 :]
    if len(refs) == 6:
        prev_peak_ref, prev_sum_ref, prev_sq_ref, peak_ref, sum_ref, sq_ref = refs
    else:
        peak_ref, sum_ref, sq_ref = refs
    bf16 = jnp.bfloat16
    f32 = jnp.float32
    o = pl.program_id(0)

    def mm(a, b):
        return jnp.dot(a, b, preferred_element_type=f32)

    def one(g):
        template = jnp.where(o < first, tmpl_ref[g], other_ref[g])
        part_real = mm(template, cos_rows_ref[...]).astype(bf16)
        part_imag = (-mm(template, sin_rows_ref[...])).astype(bf16)
        cols = cols_ref[...]
        n = cols.shape[0] // 2
        from_real = mm(cols, part_real)
        from_imag = mm(cols, part_imag)
        full_real = from_real[:n] + from_imag[n:]
        full_imag = from_imag[:n] - from_real[n:]
        weight = ctf_refs[g][0]
        w_real = (full_real * weight).astype(bf16).astype(f32)
        w_imag = (full_imag * weight).astype(bf16).astype(f32)
        spec_real = spec_r_ref[...].astype(f32)
        spec_imag = spec_i_ref[...].astype(f32)
        prod_real = (spec_real * w_real + spec_imag * w_imag).astype(bf16)
        prod_imag = (spec_imag * w_real - spec_real * w_imag).astype(bf16)
        rows = rows_ref[...]
        tile = rows.shape[0] // 2
        left_from_real = mm(rows, prod_real)
        left_from_imag = mm(rows, prod_imag)
        left_real = (left_from_real[:tile] - left_from_imag[tile:]).astype(bf16)
        left_imag = (left_from_imag[:tile] + left_from_real[tile:]).astype(bf16)
        return (mm(left_real, col_cos_ref[...]) - mm(left_imag, col_sin_ref[...])) * scaling

    corrs = [one(g) for g in range(group)]
    step_peak = corrs[0]
    step_sum = corrs[0]
    step_sq = corrs[0] * corrs[0]
    for corr in corrs[1:]:
        step_peak = jnp.maximum(step_peak, corr)
        step_sum = step_sum + corr
        step_sq = step_sq + corr * corr

    @pl.when(o == 0)
    def _():
        if len(refs) == 6:
            peak_ref[...] = jnp.maximum(prev_peak_ref[...], step_peak)
            sum_ref[...] = prev_sum_ref[...] + step_sum
            sq_ref[...] = prev_sq_ref[...] + step_sq
        else:
            peak_ref[...] = step_peak
            sum_ref[...] = step_sum
            sq_ref[...] = step_sq

    @pl.when(o > 0)
    def _():
        peak_ref[...] = jnp.maximum(peak_ref[...], step_peak)
        sum_ref[...] = sum_ref[...] + step_sum
        sq_ref[...] = sq_ref[...] + step_sq

    if total:
        @pl.when(o == pl.num_programs(0) - 1)
        def _():
            rows_at = lax.broadcasted_iota(jnp.int32, peak_ref.shape, 0)
            live = rows_at < block * live_ref[0]
            peak_ref[...] = jnp.where(live, peak_ref[...], 0.0)
            sum_ref[...] = jnp.where(live, sum_ref[...] / total, 0.0)
            sq_ref[...] = jnp.where(live, sq_ref[...] / total, 0.0)


def correlate(ids, live, pieces, ctf, spec_real, spec_imag, tables, scaling, previous, total):
    pieces = list(pieces)
    group = next(g for g in (4, 2, 1) if all(piece.shape[0] % g == 0 for piece in pieces))
    first = pieces[0].shape[0] // group
    steps = sum(piece.shape[0] for piece in pieces) // group
    if len(pieces) == 1:
        pieces.append(pieces[0])
    last_other = pieces[1].shape[0] // group - 1
    box = pieces[0].shape[2]
    n = ctf.shape[1]
    tile = tables[4].shape[1]
    full = lambda shape: pl.BlockSpec(shape, lambda o, ids, live: (0,) * len(shape))

    def plane(g):
        return pl.BlockSpec((1, n, n), lambda o, ids, live: (ids[o * group + g], 0, 0))

    in_specs = (
        [
            pl.BlockSpec((group, box, box), lambda o, ids, live: (jnp.minimum(o, first - 1), 0, 0)),
            pl.BlockSpec((group, box, box), lambda o, ids, live: (jnp.clip(o - first, 0, last_other), 0, 0)),
        ]
        + [plane(g) for g in range(group)]
        + [full((n, n)), full((n, n))]
        + [full(t.shape) for t in tables]
        + [full((tile, tile))] * len(previous)
    )
    out_block = full((tile, tile))
    grid_spec = pltpu.PrefetchScalarGridSpec(
        num_scalar_prefetch=2,
        grid=(steps,),
        in_specs=in_specs,
        out_specs=[out_block, out_block, out_block],
    )
    out_shape = [jax.ShapeDtypeStruct((tile, tile), jnp.float32)] * 3
    kernel = functools.partial(
        correlate_kernel, scaling=scaling, total=total, block=RB, first=first, group=group
    )
    base = 4 + group + 2 + len(tables)
    return pl.pallas_call(
        kernel,
        grid_spec=grid_spec,
        out_shape=out_shape,
        compiler_params=pltpu.CompilerParams(dimension_semantics=("arbitrary",)),
        input_output_aliases={base + i: i for i in range(len(previous))},
    )(ids, live, pieces[0], pieces[1], *([ctf] * group), spec_real, spec_imag, *tables, *previous)


def body(micrograph, templates, defocus, ctf, usable):
    bf16 = jnp.bfloat16
    f32 = jnp.float32
    tile_width = micrograph.shape[0]
    padded_size = ctf.shape[1]
    box_size = templates.shape[1]
    margin = (padded_size - tile_width) // 2
    scaling = 1.0 / (padded_size * padded_size)
    n = padded_size
    cos_np, sin_np = twiddles(n)

    cos_full, sin_full = lax.optimization_barrier((jnp.asarray(cos_np), jnp.asarray(sin_np)))
    low = n - box_size // 2
    cos_rows = jnp.concatenate([cos_full[low:], cos_full[: box_size - (n - low)]], axis=0)
    sin_rows = jnp.concatenate([sin_full[low:], sin_full[: box_size - (n - low)]], axis=0)
    cos_cols = cos_rows.T
    sin_cols = sin_rows.T
    row_cos = cos_full[margin : margin + tile_width]
    row_sin = sin_full[margin : margin + tile_width]
    col_cos = row_cos.T
    col_sin = row_sin.T

    local_count = templates.shape[0]
    id_rows = jnp.broadcast_to(defocus.astype(bf16)[:, None, None], (local_count, 8, box_size))
    block_rows = box_size + 8
    packed = jnp.concatenate([templates, id_rows], axis=1).reshape(local_count * block_rows, box_size)
    split_last = lax.axis_size("orient") == 8 and lax.axis_size("tile") == 2
    split_last = split_last and local_count == 1 and (margin * tile_width) % box_size == 0
    if split_last:
        arrivals, row_padded = exchange_with_rows(packed, micrograph, margin)
        core = lax.axis_index("tile")
        edge = jnp.where(core == 0, row_padded[:, tile_width - margin :], row_padded[:, :margin])
        got = lax.ppermute(edge, "tile", [(0, 1), (1, 0)])
        zero = jnp.zeros_like(got)
        padded = jnp.concatenate(
            [jnp.where(core == 0, zero, got), row_padded, jnp.where(core == 0, got, zero)], axis=1
        )
    else:
        arrivals = exchange_rounds(packed)
        padded = extended(micrograph, (("orient", 0), ("tile", 1)), margin)
    total = sum(piece.shape[0] for piece in arrivals) // block_rows

    half_real = matmul(padded, cos_full).astype(bf16)
    half_imag = (-matmul(padded, sin_full)).astype(bf16)
    spec_real = (matmul(cos_full, half_real) + matmul(sin_full, half_imag)).astype(bf16)
    spec_imag = (matmul(cos_full, half_imag) - matmul(sin_full, half_real)).astype(bf16)

    tables = (
        cos_rows,
        sin_rows,
        jnp.concatenate([cos_cols, sin_cols], axis=0),
        jnp.concatenate([row_cos, row_sin], axis=0),
        col_cos,
        col_sin,
    )
    shape = (tile_width, tile_width)
    stats = ()
    live = usable.reshape(-1)[:1]

    def run(pieces, stats, total=0):
        pieces = [piece.reshape(piece.shape[0] // block_rows, block_rows, box_size) for piece in pieces]
        piece_ids = jnp.concatenate([piece[:, box_size, 0] for piece in pieces]).astype(jnp.int32)
        return correlate(piece_ids, live, pieces, ctf, spec_real, spec_imag, tables, scaling, stats, total)

    if split_last:
        stats = run([arrivals[0]], stats)
        half, stats = lax.optimization_barrier((arrivals[1], stats))
        other_half = lax.ppermute(half, "tile", [(0, 1), (1, 0)])
        total = (arrivals[0].shape[0] + 2 * half.shape[0]) // block_rows
        stats = run([half, other_half], stats, float(total))
    else:
        for last, piece in enumerate(arrivals, 1 - len(arrivals)):
            stats = run([piece], stats, 0 if last else float(total))
    return stats


def solution(mesh):
    return jax.shard_map(
        body,
        mesh=mesh,
        in_specs=(
            P(("groups", "orient"), "tile"),
            P("orient", None, None),
            P(("groups", "orient")),
            P("groups", None, None),
            P(("groups", "orient"), "tile"),
        ),
        out_specs=(
            P(("groups", "orient"), "tile"),
            P(("groups", "orient"), "tile"),
            P(("groups", "orient"), "tile"),
        ),
        check_vma=False,
    )
```

```python
import functools
import math

import jax
import jax.numpy as jnp
import ml_dtypes
import numpy as np
from jax import lax
from jax.experimental import pallas as pl
from jax.experimental.pallas import tpu as pltpu
from jax.sharding import PartitionSpec as P

RB = 32
CHUNK = 8


def extended(block, sides, width):
    for axis, dim in sides:
        count = lax.axis_size(axis)
        forward = [(i, i + 1) for i in range(count - 1)]
        backward = [(target, source) for source, target in forward]
        low = lax.ppermute(
            lax.slice_in_dim(block, block.shape[dim] - width, None, axis=dim), axis, forward
        )
        high = lax.ppermute(lax.slice_in_dim(block, 0, width, axis=dim), axis, backward)
        block = jnp.concatenate([low, block, high], axis=dim)
    return block


def twiddles(padded_size):
    position = np.arange(padded_size, dtype=np.int64)
    phase_index = (position[:, None] * position[None, :]) % padded_size
    angles = phase_index.astype(np.float32) * np.float32(2.0 * math.pi / padded_size)
    angles = angles.astype(np.float64)
    cosines = np.cos(angles).astype(np.float32).astype(ml_dtypes.bfloat16)
    sines = np.sin(angles).astype(np.float32).astype(ml_dtypes.bfloat16)
    return cosines, sines


def matmul(left, right):
    return jnp.dot(left, right, preferred_element_type=jnp.float32)


def exchange_rounds(block):
    size = lax.axis_size("orient")
    step = 1
    while step * 2 < size:
        step *= 2
    rounds = [block]
    held = block
    while step >= 1:
        other = lax.ppermute(held, "orient", [(i, i ^ step) for i in range(size)])
        if len(rounds) > 1:
            other, rounds[-1] = lax.optimization_barrier((other, rounds[-1]))
        rounds.append(other)
        held = jnp.concatenate([held, other], axis=0)
        step //= 2
    return rounds


def swap(payload, pairs):
    return lax.ppermute(payload, "orient", [(a, b) for a, b in pairs] + [(b, a) for a, b in pairs])


def exchange_with_rows(block, tile, width):
    size = lax.axis_size("orient")
    index = lax.axis_index("orient")
    odd = index % 2 == 1
    low_rows = tile[tile.shape[0] - width :]
    high_rows = tile[:width]
    lanes = block.shape[1]
    carried = width * tile.shape[1] // lanes

    def send(held, rows, pairs):
        payload = jnp.concatenate([held, rows.reshape(carried, lanes)], axis=0)
        got = swap(payload, pairs)
        return got[: held.shape[0]], got[held.shape[0] :].reshape(width, tile.shape[1])

    first, rows_one = send(block, jnp.where(odd, high_rows, low_rows), [(2 * i, 2 * i + 1) for i in range(size // 2)])
    held = jnp.concatenate([block, first], axis=0)
    second_pairs = [(2 * i + 1, 2 * i + 2) for i in range(size // 2 - 1)] + [(0, size - 1)]
    second, rows_two = send(held, jnp.where(odd, low_rows, high_rows), second_pairs)
    held = jnp.concatenate([held, second], axis=0)
    third_pairs = [(0, size // 2), (size - 1, size // 2 - 1), (1, size // 2 + 1), (2, size // 2 + 2)]
    cores = lax.axis_size("tile")
    share = held.shape[0] // cores
    core = lax.axis_index("tile")
    mine = lax.dynamic_slice_in_dim(held, core * share, share, 0)
    third = swap(mine, third_pairs)
    arrivals = [held, third]
    zero = jnp.zeros_like(rows_one)
    top = jnp.where(odd, rows_one, jnp.where(index == 0, zero, rows_two))
    bottom = jnp.where(odd, jnp.where(index == size - 1, zero, rows_two), rows_one)
    return arrivals, jnp.concatenate([top, tile, bottom], axis=0)


def correlate_kernel(ids_ref, live_ref, tmpl_ref, other_ref, *refs, scaling, total, block, first, group, from_half):
    bf16 = jnp.bfloat16
    f32 = jnp.float32
    o = pl.program_id(0)

    def mm(a, b):
        return jnp.dot(a, b, preferred_element_type=f32)

    ctf_refs = refs[:group]
    refs = refs[group:]
    if from_half:
        half_r_ref, half_i_ref, cos_ref, sin_ref = refs[:4]
        refs = refs[4:]
    else:
        spec_r_ref, spec_i_ref = refs[:2]
        refs = refs[2:]
    (cos_rows_ref, sin_rows_ref, cols_ref, rows_ref, col_cos_ref, col_sin_ref) = refs[:6]
    refs = refs[6:]
    if from_half:
        spec_r_ref, spec_i_ref = refs[-2:]
        refs = refs[:-2]

        @pl.when(o == 0)
        def _():
            cos = cos_ref[...]
            sin = sin_ref[...]
            half_real = half_r_ref[...]
            half_imag = half_i_ref[...]
            spec_r_ref[...] = (mm(cos, half_real) + mm(sin, half_imag)).astype(bf16)
            spec_i_ref[...] = (mm(cos, half_imag) - mm(sin, half_real)).astype(bf16)

    if len(refs) == 6:
        prev_peak_ref, prev_sum_ref, prev_sq_ref, peak_ref, sum_ref, sq_ref = refs
    else:
        peak_ref, sum_ref, sq_ref = refs

    def one(g):
        template = jnp.where(o < first, tmpl_ref[g], other_ref[g])
        part_real = mm(template, cos_rows_ref[...]).astype(bf16)
        part_imag = (-mm(template, sin_rows_ref[...])).astype(bf16)
        cols = cols_ref[...]
        n = cols.shape[0] // 2
        from_real = mm(cols, part_real)
        from_imag = mm(cols, part_imag)
        full_real = from_real[:n] + from_imag[n:]
        full_imag = from_imag[:n] - from_real[n:]
        weight = ctf_refs[g][0]
        w_real = (full_real * weight).astype(bf16).astype(f32)
        w_imag = (full_imag * weight).astype(bf16).astype(f32)
        spec_real = spec_r_ref[...].astype(f32)
        spec_imag = spec_i_ref[...].astype(f32)
        prod_real = (spec_real * w_real + spec_imag * w_imag).astype(bf16)
        prod_imag = (spec_imag * w_real - spec_real * w_imag).astype(bf16)
        rows = rows_ref[...]
        tile = rows.shape[0] // 2
        left_from_real = mm(rows, prod_real)
        left_from_imag = mm(rows, prod_imag)
        left_real = (left_from_real[:tile] - left_from_imag[tile:]).astype(bf16)
        left_imag = (left_from_imag[:tile] + left_from_real[tile:]).astype(bf16)
        return (mm(left_real, col_cos_ref[...]) - mm(left_imag, col_sin_ref[...])) * scaling

    corrs = [one(g) for g in range(group)]
    step_peak = corrs[0]
    step_sum = corrs[0]
    step_sq = corrs[0] * corrs[0]
    for corr in corrs[1:]:
        step_peak = jnp.maximum(step_peak, corr)
        step_sum = step_sum + corr
        step_sq = step_sq + corr * corr

    @pl.when(o == 0)
    def _():
        if len(refs) == 6:
            peak_ref[...] = jnp.maximum(prev_peak_ref[...], step_peak)
            sum_ref[...] = prev_sum_ref[...] + step_sum
            sq_ref[...] = prev_sq_ref[...] + step_sq
        else:
            peak_ref[...] = step_peak
            sum_ref[...] = step_sum
            sq_ref[...] = step_sq

    @pl.when(o > 0)
    def _():
        peak_ref[...] = jnp.maximum(peak_ref[...], step_peak)
        sum_ref[...] = sum_ref[...] + step_sum
        sq_ref[...] = sq_ref[...] + step_sq

    if total:
        @pl.when(o == pl.num_programs(0) - 1)
        def _():
            rows_at = lax.broadcasted_iota(jnp.int32, peak_ref.shape, 0)
            live = rows_at < block * live_ref[0]
            peak_ref[...] = jnp.where(live, peak_ref[...], 0.0)
            sum_ref[...] = jnp.where(live, sum_ref[...] / total, 0.0)
            sq_ref[...] = jnp.where(live, sq_ref[...] / total, 0.0)


def correlate(ids, live, pieces, ctf, spectrum, tables, scaling, previous, total, from_half=False):
    pieces = list(pieces)
    group = 2 if all(piece.shape[0] % 2 == 0 for piece in pieces) else 1
    first = pieces[0].shape[0] // group
    steps = sum(piece.shape[0] for piece in pieces) // group
    if len(pieces) == 1:
        pieces.append(pieces[0])
    last_other = pieces[1].shape[0] // group - 1
    box = pieces[0].shape[2]
    n = ctf.shape[1]
    tile = tables[4].shape[1]
    full = lambda shape: pl.BlockSpec(shape, lambda o, ids, live: (0,) * len(shape))

    def plane(g):
        return pl.BlockSpec((1, n, n), lambda o, ids, live: (ids[o * group + g], 0, 0))

    in_specs = (
        [
            pl.BlockSpec((group, box, box), lambda o, ids, live: (jnp.minimum(o, first - 1), 0, 0)),
            pl.BlockSpec((group, box, box), lambda o, ids, live: (jnp.clip(o - first, 0, last_other), 0, 0)),
        ]
        + [plane(g) for g in range(group)]
        + [full((n, n))] * len(spectrum)
        + [full(t.shape) for t in tables]
        + [full((tile, tile))] * len(previous)
    )
    out_block = full((tile, tile))
    out_specs = [out_block, out_block, out_block]
    out_shape = [jax.ShapeDtypeStruct((tile, tile), jnp.float32)] * 3
    if from_half:
        out_specs += [full((n, n)), full((n, n))]
        out_shape += [jax.ShapeDtypeStruct((n, n), jnp.bfloat16)] * 2
    grid_spec = pltpu.PrefetchScalarGridSpec(
        num_scalar_prefetch=2,
        grid=(steps,),
        in_specs=in_specs,
        out_specs=out_specs,
    )
    kernel = functools.partial(
        correlate_kernel, scaling=scaling, total=total, block=RB, first=first, group=group, from_half=from_half
    )
    base = 4 + group + len(spectrum) + len(tables)
    return pl.pallas_call(
        kernel,
        grid_spec=grid_spec,
        out_shape=out_shape,
        compiler_params=pltpu.CompilerParams(dimension_semantics=("arbitrary",)),
        input_output_aliases={base + i: i for i in range(len(previous))},
    )(ids, live, pieces[0], pieces[1], *([ctf] * group), *spectrum, *tables, *previous)


def body(micrograph, templates, defocus, ctf, usable):
    bf16 = jnp.bfloat16
    f32 = jnp.float32
    tile_width = micrograph.shape[0]
    padded_size = ctf.shape[1]
    box_size = templates.shape[1]
    margin = (padded_size - tile_width) // 2
    scaling = 1.0 / (padded_size * padded_size)
    n = padded_size
    cos_np, sin_np = twiddles(n)

    cos_full, sin_full = lax.optimization_barrier((jnp.asarray(cos_np), jnp.asarray(sin_np)))
    low = n - box_size // 2
    cos_rows = jnp.concatenate([cos_full[low:], cos_full[: box_size - (n - low)]], axis=0)
    sin_rows = jnp.concatenate([sin_full[low:], sin_full[: box_size - (n - low)]], axis=0)
    cos_cols = cos_rows.T
    sin_cols = sin_rows.T
    row_cos = cos_full[margin : margin + tile_width]
    row_sin = sin_full[margin : margin + tile_width]
    col_cos = row_cos.T
    col_sin = row_sin.T

    local_count = templates.shape[0]
    id_rows = jnp.broadcast_to(defocus.astype(bf16)[:, None, None], (local_count, 8, box_size))
    block_rows = box_size + 8
    packed = jnp.concatenate([templates, id_rows], axis=1).reshape(local_count * block_rows, box_size)
    split_last = lax.axis_size("orient") == 8 and lax.axis_size("tile") == 2
    split_last = split_last and local_count == 1 and (margin * tile_width) % box_size == 0
    if split_last:
        arrivals, row_padded = exchange_with_rows(packed, micrograph, margin)
        core = lax.axis_index("tile")
        edge = jnp.where(core == 0, row_padded[:, tile_width - margin :], row_padded[:, :margin])
        got = lax.ppermute(edge, "tile", [(0, 1), (1, 0)])
        zero = jnp.zeros_like(got)
        padded = jnp.concatenate(
            [jnp.where(core == 0, zero, got), row_padded, jnp.where(core == 0, got, zero)], axis=1
        )
    else:
        arrivals = exchange_rounds(packed)
        padded = extended(micrograph, (("orient", 0), ("tile", 1)), margin)
    total = sum(piece.shape[0] for piece in arrivals) // block_rows

    half_real = matmul(padded, cos_full).astype(bf16)
    half_imag = (-matmul(padded, sin_full)).astype(bf16)

    tables = (
        cos_rows,
        sin_rows,
        jnp.concatenate([cos_cols, sin_cols], axis=0),
        jnp.concatenate([row_cos, row_sin], axis=0),
        col_cos,
        col_sin,
    )
    shape = (tile_width, tile_width)
    stats = ()
    live = usable.reshape(-1)[:1]

    spectrum = [half_real, half_imag, cos_full, sin_full]

    def run(pieces, stats, total=0):
        pieces = [piece.reshape(piece.shape[0] // block_rows, block_rows, box_size) for piece in pieces]
        piece_ids = jnp.concatenate([piece[:, box_size, 0] for piece in pieces]).astype(jnp.int32)
        from_half = len(spectrum) == 4
        outs = correlate(piece_ids, live, pieces, ctf, spectrum, tables, scaling, stats, total, from_half)
        if from_half:
            spectrum[:] = outs[3:]
        return tuple(outs[:3])

    if split_last:
        stats = run([arrivals[0]], stats)
        half, stats = lax.optimization_barrier((arrivals[1], stats))
        other_half = lax.ppermute(half, "tile", [(0, 1), (1, 0)])
        total = (arrivals[0].shape[0] + 2 * half.shape[0]) // block_rows
        stats = run([half, other_half], stats, float(total))
    else:
        for last, piece in enumerate(arrivals, 1 - len(arrivals)):
            stats = run([piece], stats, 0 if last else float(total))
    return stats


def solution(mesh):
    return jax.shard_map(
        body,
        mesh=mesh,
        in_specs=(
            P(("groups", "orient"), "tile"),
            P("orient", None, None),
            P(("groups", "orient")),
            P("groups", None, None),
            P(("groups", "orient"), "tile"),
        ),
        out_specs=(
            P(("groups", "orient"), "tile"),
            P(("groups", "orient"), "tile"),
            P(("groups", "orient"), "tile"),
        ),
        check_vma=False,
    )
```

```python
import functools
import math

import jax
import jax.numpy as jnp
import ml_dtypes
import numpy as np
from jax import lax
from jax.experimental import pallas as pl
from jax.experimental.pallas import tpu as pltpu
from jax.sharding import PartitionSpec as P

RB = 32
CHUNK = 8


def extended(block, sides, width):
    for axis, dim in sides:
        count = lax.axis_size(axis)
        forward = [(i, i + 1) for i in range(count - 1)]
        backward = [(target, source) for source, target in forward]
        low = lax.ppermute(
            lax.slice_in_dim(block, block.shape[dim] - width, None, axis=dim), axis, forward
        )
        high = lax.ppermute(lax.slice_in_dim(block, 0, width, axis=dim), axis, backward)
        block = jnp.concatenate([low, block, high], axis=dim)
    return block


def twiddles(padded_size):
    position = np.arange(padded_size, dtype=np.int64)
    phase_index = (position[:, None] * position[None, :]) % padded_size
    angles = phase_index.astype(np.float32) * np.float32(2.0 * math.pi / padded_size)
    angles = angles.astype(np.float64)
    cosines = np.cos(angles).astype(np.float32).astype(ml_dtypes.bfloat16)
    sines = np.sin(angles).astype(np.float32).astype(ml_dtypes.bfloat16)
    return cosines, sines


def matmul(left, right):
    return jnp.dot(left, right, preferred_element_type=jnp.float32)


def exchange_rounds(block):
    size = lax.axis_size("orient")
    step = 1
    while step * 2 < size:
        step *= 2
    rounds = [block]
    held = block
    while step >= 1:
        other = lax.ppermute(held, "orient", [(i, i ^ step) for i in range(size)])
        if len(rounds) > 1:
            other, rounds[-1] = lax.optimization_barrier((other, rounds[-1]))
        rounds.append(other)
        held = jnp.concatenate([held, other], axis=0)
        step //= 2
    return rounds


def swap(payload, pairs):
    return lax.ppermute(payload, "orient", [(a, b) for a, b in pairs] + [(b, a) for a, b in pairs])


def exchange_with_rows(block, tile, width):
    size = lax.axis_size("orient")
    index = lax.axis_index("orient")
    odd = index % 2 == 1
    low_rows = tile[tile.shape[0] - width :]
    high_rows = tile[:width]
    lanes = block.shape[1]
    carried = width * tile.shape[1] // lanes

    def send(held, rows, pairs):
        payload = jnp.concatenate([held, rows.reshape(carried, lanes)], axis=0)
        got = swap(payload, pairs)
        return got[: held.shape[0]], got[held.shape[0] :].reshape(width, tile.shape[1])

    first, rows_one = send(block, jnp.where(odd, high_rows, low_rows), [(2 * i, 2 * i + 1) for i in range(size // 2)])
    held = jnp.concatenate([block, first], axis=0)
    second_pairs = [(2 * i + 1, 2 * i + 2) for i in range(size // 2 - 1)] + [(0, size - 1)]
    second, rows_two = send(held, jnp.where(odd, low_rows, high_rows), second_pairs)
    held = jnp.concatenate([held, second], axis=0)
    third_pairs = [(0, size // 2), (size - 1, size // 2 - 1), (1, size // 2 + 1), (2, size // 2 + 2)]
    cores = lax.axis_size("tile")
    share = held.shape[0] // cores
    core = lax.axis_index("tile")
    mine = lax.dynamic_slice_in_dim(held, core * share, share, 0)
    third = swap(mine, third_pairs)
    arrivals = [held, third]
    zero = jnp.zeros_like(rows_one)
    top = jnp.where(odd, rows_one, jnp.where(index == 0, zero, rows_two))
    bottom = jnp.where(odd, jnp.where(index == size - 1, zero, rows_two), rows_one)
    return arrivals, jnp.concatenate([top, tile, bottom], axis=0)


def correlate_kernel(ids_ref, live_ref, tmpl_ref, other_ref, *refs, scaling, total, block, first, group, from_half):
    bf16 = jnp.bfloat16
    f32 = jnp.float32
    o = pl.program_id(0)

    def mm(a, b):
        return jnp.dot(a, b, preferred_element_type=f32)

    ctf_refs = refs[:group]
    refs = refs[group:]
    if from_half:
        padded_ref, cos_ref, sin_ref = refs[:3]
        refs = refs[3:]
    else:
        spec_r_ref, spec_i_ref = refs[:2]
        refs = refs[2:]
    (cos_rows_ref, sin_rows_ref, cols_ref, rows_ref, col_cos_ref, col_sin_ref) = refs[:6]
    refs = refs[6:]
    if from_half:
        spec_r_ref, spec_i_ref = refs[-2:]
        refs = refs[:-2]

        @pl.when(o == 0)
        def _():
            cos = cos_ref[...]
            sin = sin_ref[...]
            padded = padded_ref[...]
            half_real = mm(padded, cos).astype(bf16)
            half_imag = (-mm(padded, sin)).astype(bf16)
            spec_r_ref[...] = (mm(cos, half_real) + mm(sin, half_imag)).astype(bf16)
            spec_i_ref[...] = (mm(cos, half_imag) - mm(sin, half_real)).astype(bf16)

    if len(refs) == 6:
        prev_peak_ref, prev_sum_ref, prev_sq_ref, peak_ref, sum_ref, sq_ref = refs
    else:
        peak_ref, sum_ref, sq_ref = refs

    def one(g):
        template = jnp.where(o < first, tmpl_ref[g], other_ref[g])
        part_real = mm(template, cos_rows_ref[...]).astype(bf16)
        part_imag = (-mm(template, sin_rows_ref[...])).astype(bf16)
        cols = cols_ref[...]
        n = cols.shape[0] // 2
        from_real = mm(cols, part_real)
        from_imag = mm(cols, part_imag)
        full_real = from_real[:n] + from_imag[n:]
        full_imag = from_imag[:n] - from_real[n:]
        weight = ctf_refs[g][0]
        w_real = (full_real * weight).astype(bf16).astype(f32)
        w_imag = (full_imag * weight).astype(bf16).astype(f32)
        spec_real = spec_r_ref[...].astype(f32)
        spec_imag = spec_i_ref[...].astype(f32)
        prod_real = (spec_real * w_real + spec_imag * w_imag).astype(bf16)
        prod_imag = (spec_imag * w_real - spec_real * w_imag).astype(bf16)
        rows = rows_ref[...]
        tile = rows.shape[0] // 2
        left_from_real = mm(rows, prod_real)
        left_from_imag = mm(rows, prod_imag)
        left_real = (left_from_real[:tile] - left_from_imag[tile:]).astype(bf16)
        left_imag = (left_from_imag[:tile] + left_from_real[tile:]).astype(bf16)
        return (mm(left_real, col_cos_ref[...]) - mm(left_imag, col_sin_ref[...])) * scaling

    corrs = [one(g) for g in range(group)]
    step_peak = corrs[0]
    step_sum = corrs[0]
    step_sq = corrs[0] * corrs[0]
    for corr in corrs[1:]:
        step_peak = jnp.maximum(step_peak, corr)
        step_sum = step_sum + corr
        step_sq = step_sq + corr * corr

    @pl.when(o == 0)
    def _():
        if len(refs) == 6:
            peak_ref[...] = jnp.maximum(prev_peak_ref[...], step_peak)
            sum_ref[...] = prev_sum_ref[...] + step_sum
            sq_ref[...] = prev_sq_ref[...] + step_sq
        else:
            peak_ref[...] = step_peak
            sum_ref[...] = step_sum
            sq_ref[...] = step_sq

    @pl.when(o > 0)
    def _():
        peak_ref[...] = jnp.maximum(peak_ref[...], step_peak)
        sum_ref[...] = sum_ref[...] + step_sum
        sq_ref[...] = sq_ref[...] + step_sq

    if total:
        @pl.when(o == pl.num_programs(0) - 1)
        def _():
            rows_at = lax.broadcasted_iota(jnp.int32, peak_ref.shape, 0)
            live = rows_at < block * live_ref[0]
            peak_ref[...] = jnp.where(live, peak_ref[...], 0.0)
            sum_ref[...] = jnp.where(live, sum_ref[...] / total, 0.0)
            sq_ref[...] = jnp.where(live, sq_ref[...] / total, 0.0)


def correlate(ids, live, pieces, ctf, spectrum, tables, scaling, previous, total, from_half=False):
    pieces = list(pieces)
    group = 2 if all(piece.shape[0] % 2 == 0 for piece in pieces) else 1
    first = pieces[0].shape[0] // group
    steps = sum(piece.shape[0] for piece in pieces) // group
    if len(pieces) == 1:
        pieces.append(pieces[0])
    last_other = pieces[1].shape[0] // group - 1
    box = pieces[0].shape[2]
    n = ctf.shape[1]
    tile = tables[4].shape[1]
    full = lambda shape: pl.BlockSpec(shape, lambda o, ids, live: (0,) * len(shape))

    def plane(g):
        return pl.BlockSpec((1, n, n), lambda o, ids, live: (ids[o * group + g], 0, 0))

    in_specs = (
        [
            pl.BlockSpec((group, box, box), lambda o, ids, live: (jnp.minimum(o, first - 1), 0, 0)),
            pl.BlockSpec((group, box, box), lambda o, ids, live: (jnp.clip(o - first, 0, last_other), 0, 0)),
        ]
        + [plane(g) for g in range(group)]
        + [full((n, n))] * len(spectrum)
        + [full(t.shape) for t in tables]
        + [full((tile, tile))] * len(previous)
    )
    out_block = full((tile, tile))
    out_specs = [out_block, out_block, out_block]
    out_shape = [jax.ShapeDtypeStruct((tile, tile), jnp.float32)] * 3
    if from_half:
        out_specs += [full((n, n)), full((n, n))]
        out_shape += [jax.ShapeDtypeStruct((n, n), jnp.bfloat16)] * 2
    grid_spec = pltpu.PrefetchScalarGridSpec(
        num_scalar_prefetch=2,
        grid=(steps,),
        in_specs=in_specs,
        out_specs=out_specs,
    )
    kernel = functools.partial(
        correlate_kernel, scaling=scaling, total=total, block=RB, first=first, group=group, from_half=from_half
    )
    base = 4 + group + len(spectrum) + len(tables)
    return pl.pallas_call(
        kernel,
        grid_spec=grid_spec,
        out_shape=out_shape,
        compiler_params=pltpu.CompilerParams(dimension_semantics=("arbitrary",)),
        input_output_aliases={base + i: i for i in range(len(previous))},
    )(ids, live, pieces[0], pieces[1], *([ctf] * group), *spectrum, *tables, *previous)


def body(micrograph, templates, defocus, ctf, usable):
    bf16 = jnp.bfloat16
    f32 = jnp.float32
    tile_width = micrograph.shape[0]
    padded_size = ctf.shape[1]
    box_size = templates.shape[1]
    margin = (padded_size - tile_width) // 2
    scaling = 1.0 / (padded_size * padded_size)
    n = padded_size
    cos_np, sin_np = twiddles(n)

    cos_full, sin_full = lax.optimization_barrier((jnp.asarray(cos_np), jnp.asarray(sin_np)))
    low = n - box_size // 2
    cos_rows = jnp.concatenate([cos_full[low:], cos_full[: box_size - (n - low)]], axis=0)
    sin_rows = jnp.concatenate([sin_full[low:], sin_full[: box_size - (n - low)]], axis=0)
    cos_cols = cos_rows.T
    sin_cols = sin_rows.T
    row_cos = cos_full[margin : margin + tile_width]
    row_sin = sin_full[margin : margin + tile_width]
    col_cos = row_cos.T
    col_sin = row_sin.T

    local_count = templates.shape[0]
    id_rows = jnp.broadcast_to(defocus.astype(bf16)[:, None, None], (local_count, 8, box_size))
    block_rows = box_size + 8
    packed = jnp.concatenate([templates, id_rows], axis=1).reshape(local_count * block_rows, box_size)
    split_last = lax.axis_size("orient") == 8 and lax.axis_size("tile") == 2
    split_last = split_last and local_count == 1 and (margin * tile_width) % box_size == 0
    if split_last:
        arrivals, row_padded = exchange_with_rows(packed, micrograph, margin)
        core = lax.axis_index("tile")
        edge = jnp.where(core == 0, row_padded[:, tile_width - margin :], row_padded[:, :margin])
        got = lax.ppermute(edge, "tile", [(0, 1), (1, 0)])
        zero = jnp.zeros_like(got)
        padded = jnp.concatenate(
            [jnp.where(core == 0, zero, got), row_padded, jnp.where(core == 0, got, zero)], axis=1
        )
    else:
        arrivals = exchange_rounds(packed)
        padded = extended(micrograph, (("orient", 0), ("tile", 1)), margin)
    total = sum(piece.shape[0] for piece in arrivals) // block_rows


    tables = (
        cos_rows,
        sin_rows,
        jnp.concatenate([cos_cols, sin_cols], axis=0),
        jnp.concatenate([row_cos, row_sin], axis=0),
        col_cos,
        col_sin,
    )
    shape = (tile_width, tile_width)
    stats = ()
    live = usable.reshape(-1)[:1]

    spectrum = [padded, cos_full, sin_full]

    def run(pieces, stats, total=0):
        pieces = [piece.reshape(piece.shape[0] // block_rows, block_rows, box_size) for piece in pieces]
        piece_ids = jnp.concatenate([piece[:, box_size, 0] for piece in pieces]).astype(jnp.int32)
        from_half = len(spectrum) == 3
        outs = correlate(piece_ids, live, pieces, ctf, spectrum, tables, scaling, stats, total, from_half)
        if from_half:
            spectrum[:] = outs[3:]
        return tuple(outs[:3])

    if split_last:
        stats = run([arrivals[0]], stats)
        half, stats = lax.optimization_barrier((arrivals[1], stats))
        other_half = lax.ppermute(half, "tile", [(0, 1), (1, 0)])
        total = (arrivals[0].shape[0] + 2 * half.shape[0]) // block_rows
        stats = run([half, other_half], stats, float(total))
    else:
        for last, piece in enumerate(arrivals, 1 - len(arrivals)):
            stats = run([piece], stats, 0 if last else float(total))
    return stats


def solution(mesh):
    return jax.shard_map(
        body,
        mesh=mesh,
        in_specs=(
            P(("groups", "orient"), "tile"),
            P("orient", None, None),
            P(("groups", "orient")),
            P("groups", None, None),
            P(("groups", "orient"), "tile"),
        ),
        out_specs=(
            P(("groups", "orient"), "tile"),
            P(("groups", "orient"), "tile"),
            P(("groups", "orient"), "tile"),
        ),
        check_vma=False,
    )
```

```python
import functools
import math

import jax
import jax.numpy as jnp
import ml_dtypes
import numpy as np
from jax import lax
from jax.experimental import pallas as pl
from jax.experimental.pallas import tpu as pltpu
from jax.sharding import PartitionSpec as P

RB = 32
CHUNK = 8


def extended(block, sides, width):
    for axis, dim in sides:
        count = lax.axis_size(axis)
        forward = [(i, i + 1) for i in range(count - 1)]
        backward = [(target, source) for source, target in forward]
        low = lax.ppermute(
            lax.slice_in_dim(block, block.shape[dim] - width, None, axis=dim), axis, forward
        )
        high = lax.ppermute(lax.slice_in_dim(block, 0, width, axis=dim), axis, backward)
        block = jnp.concatenate([low, block, high], axis=dim)
    return block


def twiddles(padded_size):
    position = np.arange(padded_size, dtype=np.int64)
    phase_index = (position[:, None] * position[None, :]) % padded_size
    angles = phase_index.astype(np.float32) * np.float32(2.0 * math.pi / padded_size)
    angles = angles.astype(np.float64)
    cosines = np.cos(angles).astype(np.float32).astype(ml_dtypes.bfloat16)
    sines = np.sin(angles).astype(np.float32).astype(ml_dtypes.bfloat16)
    return cosines, sines


def matmul(left, right):
    return jnp.dot(left, right, preferred_element_type=jnp.float32)


def exchange_rounds(block):
    size = lax.axis_size("orient")
    step = 1
    while step * 2 < size:
        step *= 2
    rounds = [block]
    held = block
    while step >= 1:
        other = lax.ppermute(held, "orient", [(i, i ^ step) for i in range(size)])
        if len(rounds) > 1:
            other, rounds[-1] = lax.optimization_barrier((other, rounds[-1]))
        rounds.append(other)
        held = jnp.concatenate([held, other], axis=0)
        step //= 2
    return rounds


def swap(payload, pairs):
    return lax.ppermute(payload, "orient", [(a, b) for a, b in pairs] + [(b, a) for a, b in pairs])


def exchange_with_rows(block, tile, width):
    size = lax.axis_size("orient")
    index = lax.axis_index("orient")
    odd = index % 2 == 1
    low_rows = tile[tile.shape[0] - width :]
    high_rows = tile[:width]
    lanes = block.shape[1]
    carried = width * tile.shape[1] // lanes

    def send(held, rows, pairs):
        payload = jnp.concatenate([held, rows.reshape(carried, lanes)], axis=0)
        got = swap(payload, pairs)
        return got[: held.shape[0]], got[held.shape[0] :].reshape(width, tile.shape[1])

    first, rows_one = send(block, jnp.where(odd, high_rows, low_rows), [(2 * i, 2 * i + 1) for i in range(size // 2)])
    held = jnp.concatenate([block, first], axis=0)
    second_pairs = [(2 * i + 1, 2 * i + 2) for i in range(size // 2 - 1)] + [(0, size - 1)]
    second, rows_two = send(held, jnp.where(odd, low_rows, high_rows), second_pairs)
    held = jnp.concatenate([held, second], axis=0)
    third_pairs = [(0, size // 2), (size - 1, size // 2 - 1), (1, size // 2 + 1), (2, size // 2 + 2)]
    cores = lax.axis_size("tile")
    share = held.shape[0] // cores
    core = lax.axis_index("tile")
    mine = lax.dynamic_slice_in_dim(held, core * share, share, 0)
    third = swap(mine, third_pairs)
    arrivals = [held, third]
    zero = jnp.zeros_like(rows_one)
    top = jnp.where(odd, rows_one, jnp.where(index == 0, zero, rows_two))
    bottom = jnp.where(odd, jnp.where(index == size - 1, zero, rows_two), rows_one)
    return arrivals, jnp.concatenate([top, tile, bottom], axis=0)


def correlate_kernel(ids_ref, other_ids_ref, live_ref, tmpl_ref, other_ref, *refs, scaling, total, block, first, group, from_half):
    bf16 = jnp.bfloat16
    f32 = jnp.float32
    o = pl.program_id(0)

    def mm(a, b):
        return jnp.dot(a, b, preferred_element_type=f32)

    ctf_refs = refs[:group]
    refs = refs[group:]
    if from_half:
        padded_ref, cos_ref, sin_ref = refs[:3]
        refs = refs[3:]
    else:
        spec_r_ref, spec_i_ref = refs[:2]
        refs = refs[2:]
    (cos_rows_ref, sin_rows_ref, cols_ref, rows_ref, col_cos_ref, col_sin_ref) = refs[:6]
    refs = refs[6:]
    if from_half:
        spec_r_ref, spec_i_ref = refs[-2:]
        refs = refs[:-2]

        @pl.when(o == 0)
        def _():
            cos = cos_ref[...]
            sin = sin_ref[...]
            padded = padded_ref[...]
            half_real = mm(padded, cos).astype(bf16)
            half_imag = (-mm(padded, sin)).astype(bf16)
            spec_r_ref[...] = (mm(cos, half_real) + mm(sin, half_imag)).astype(bf16)
            spec_i_ref[...] = (mm(cos, half_imag) - mm(sin, half_real)).astype(bf16)

    if len(refs) == 6:
        prev_peak_ref, prev_sum_ref, prev_sq_ref, peak_ref, sum_ref, sq_ref = refs
    else:
        peak_ref, sum_ref, sq_ref = refs

    def one(g):
        template = jnp.where(o < first, tmpl_ref[g], other_ref[g])
        part_real = mm(template, cos_rows_ref[...]).astype(bf16)
        part_imag = (-mm(template, sin_rows_ref[...])).astype(bf16)
        cols = cols_ref[...]
        n = cols.shape[0] // 2
        from_real = mm(cols, part_real)
        from_imag = mm(cols, part_imag)
        full_real = from_real[:n] + from_imag[n:]
        full_imag = from_imag[:n] - from_real[n:]
        weight = ctf_refs[g][0]
        w_real = (full_real * weight).astype(bf16).astype(f32)
        w_imag = (full_imag * weight).astype(bf16).astype(f32)
        spec_real = spec_r_ref[...].astype(f32)
        spec_imag = spec_i_ref[...].astype(f32)
        prod_real = (spec_real * w_real + spec_imag * w_imag).astype(bf16)
        prod_imag = (spec_imag * w_real - spec_real * w_imag).astype(bf16)
        rows = rows_ref[...]
        tile = rows.shape[0] // 2
        left_from_real = mm(rows, prod_real)
        left_from_imag = mm(rows, prod_imag)
        left_real = (left_from_real[:tile] - left_from_imag[tile:]).astype(bf16)
        left_imag = (left_from_imag[:tile] + left_from_real[tile:]).astype(bf16)
        return (mm(left_real, col_cos_ref[...]) - mm(left_imag, col_sin_ref[...])) * scaling

    corrs = [one(g) for g in range(group)]
    step_peak = corrs[0]
    step_sum = corrs[0]
    step_sq = corrs[0] * corrs[0]
    for corr in corrs[1:]:
        step_peak = jnp.maximum(step_peak, corr)
        step_sum = step_sum + corr
        step_sq = step_sq + corr * corr

    @pl.when(o == 0)
    def _():
        if len(refs) == 6:
            peak_ref[...] = jnp.maximum(prev_peak_ref[...], step_peak)
            sum_ref[...] = prev_sum_ref[...] + step_sum
            sq_ref[...] = prev_sq_ref[...] + step_sq
        else:
            peak_ref[...] = step_peak
            sum_ref[...] = step_sum
            sq_ref[...] = step_sq

    @pl.when(o > 0)
    def _():
        peak_ref[...] = jnp.maximum(peak_ref[...], step_peak)
        sum_ref[...] = sum_ref[...] + step_sum
        sq_ref[...] = sq_ref[...] + step_sq

    if total:
        @pl.when(o == pl.num_programs(0) - 1)
        def _():
            rows_at = lax.broadcasted_iota(jnp.int32, peak_ref.shape, 0)
            live = rows_at < block * live_ref[0]
            peak_ref[...] = jnp.where(live, peak_ref[...], 0.0)
            sum_ref[...] = jnp.where(live, sum_ref[...] / total, 0.0)
            sq_ref[...] = jnp.where(live, sq_ref[...] / total, 0.0)


def correlate(ids, live, pieces, ctf, spectrum, tables, scaling, previous, total, from_half=False):
    pieces = list(pieces)
    group = 2 if all(piece.shape[0] % 2 == 0 for piece in pieces) else 1
    first = pieces[0].shape[0] // group
    steps = sum(piece.shape[0] for piece in pieces) // group
    if len(pieces) == 1:
        pieces.append(pieces[0])
    last_other = pieces[1].shape[0] // group - 1
    box = pieces[0].shape[2]
    n = ctf.shape[1]
    tile = tables[4].shape[1]
    full = lambda shape: pl.BlockSpec(shape, lambda o, ids, other_ids, live: (0,) * len(shape))

    def plane(g):
        def pick(o, ids, other_ids, live):
            mine = ids[jnp.minimum(o, first - 1) * group + g]
            other = other_ids[jnp.clip(o - first, 0, last_other) * group + g]
            return (jnp.where(o < first, mine, other), 0, 0)

        return pl.BlockSpec((1, n, n), pick)

    in_specs = (
        [
            pl.BlockSpec((group, box, box), lambda o, ids, other_ids, live: (jnp.minimum(o, first - 1), 0, 0)),
            pl.BlockSpec(
                (group, box, box), lambda o, ids, other_ids, live: (jnp.clip(o - first, 0, last_other), 0, 0)
            ),
        ]
        + [plane(g) for g in range(group)]
        + [full((n, n))] * len(spectrum)
        + [full(t.shape) for t in tables]
        + [full((tile, tile))] * len(previous)
    )
    out_block = full((tile, tile))
    out_specs = [out_block, out_block, out_block]
    out_shape = [jax.ShapeDtypeStruct((tile, tile), jnp.float32)] * 3
    if from_half:
        out_specs += [full((n, n)), full((n, n))]
        out_shape += [jax.ShapeDtypeStruct((n, n), jnp.bfloat16)] * 2
    grid_spec = pltpu.PrefetchScalarGridSpec(
        num_scalar_prefetch=3,
        grid=(steps,),
        in_specs=in_specs,
        out_specs=out_specs,
    )
    kernel = functools.partial(
        correlate_kernel, scaling=scaling, total=total, block=RB, first=first, group=group, from_half=from_half
    )
    base = 5 + group + len(spectrum) + len(tables)
    return pl.pallas_call(
        kernel,
        grid_spec=grid_spec,
        out_shape=out_shape,
        compiler_params=pltpu.CompilerParams(dimension_semantics=("arbitrary",)),
        input_output_aliases={base + i: i for i in range(len(previous))},
    )(ids[0], ids[-1], live, pieces[0], pieces[1], *([ctf] * group), *spectrum, *tables, *previous)


def body(micrograph, templates, defocus, ctf, usable):
    bf16 = jnp.bfloat16
    f32 = jnp.float32
    tile_width = micrograph.shape[0]
    padded_size = ctf.shape[1]
    box_size = templates.shape[1]
    margin = (padded_size - tile_width) // 2
    scaling = 1.0 / (padded_size * padded_size)
    n = padded_size
    cos_np, sin_np = twiddles(n)

    cos_full, sin_full = lax.optimization_barrier((jnp.asarray(cos_np), jnp.asarray(sin_np)))
    low = n - box_size // 2
    cos_rows = jnp.concatenate([cos_full[low:], cos_full[: box_size - (n - low)]], axis=0)
    sin_rows = jnp.concatenate([sin_full[low:], sin_full[: box_size - (n - low)]], axis=0)
    cos_cols = cos_rows.T
    sin_cols = sin_rows.T
    row_cos = cos_full[margin : margin + tile_width]
    row_sin = sin_full[margin : margin + tile_width]
    col_cos = row_cos.T
    col_sin = row_sin.T

    local_count = templates.shape[0]
    id_rows = jnp.broadcast_to(defocus.astype(bf16)[:, None, None], (local_count, 8, box_size))
    block_rows = box_size + 8
    packed = jnp.concatenate([templates, id_rows], axis=1).reshape(local_count * block_rows, box_size)
    split_last = lax.axis_size("orient") == 8 and lax.axis_size("tile") == 2
    split_last = split_last and local_count == 1 and (margin * tile_width) % box_size == 0
    if split_last:
        arrivals, row_padded = exchange_with_rows(packed, micrograph, margin)
        core = lax.axis_index("tile")
        edge = jnp.where(core == 0, row_padded[:, tile_width - margin :], row_padded[:, :margin])
        got = lax.ppermute(edge, "tile", [(0, 1), (1, 0)])
        zero = jnp.zeros_like(got)
        padded = jnp.concatenate(
            [jnp.where(core == 0, zero, got), row_padded, jnp.where(core == 0, got, zero)], axis=1
        )
    else:
        arrivals = exchange_rounds(packed)
        padded = extended(micrograph, (("orient", 0), ("tile", 1)), margin)
    total = sum(piece.shape[0] for piece in arrivals) // block_rows


    tables = (
        cos_rows,
        sin_rows,
        jnp.concatenate([cos_cols, sin_cols], axis=0),
        jnp.concatenate([row_cos, row_sin], axis=0),
        col_cos,
        col_sin,
    )
    shape = (tile_width, tile_width)
    stats = ()
    live = usable.reshape(-1)[:1]

    spectrum = [padded, cos_full, sin_full]

    def run(pieces, stats, total=0):
        pieces = [piece.reshape(piece.shape[0] // block_rows, block_rows, box_size) for piece in pieces]
        piece_ids = [piece[:, box_size, 0].astype(jnp.int32) for piece in pieces]
        from_half = len(spectrum) == 3
        outs = correlate(piece_ids, live, pieces, ctf, spectrum, tables, scaling, stats, total, from_half)
        if from_half:
            spectrum[:] = outs[3:]
        return tuple(outs[:3])

    if split_last:
        stats = run([arrivals[0]], stats)
        half, stats = lax.optimization_barrier((arrivals[1], stats))
        other_half = lax.ppermute(half, "tile", [(0, 1), (1, 0)])
        total = (arrivals[0].shape[0] + 2 * half.shape[0]) // block_rows
        stats = run([half, other_half], stats, float(total))
    else:
        for last, piece in enumerate(arrivals, 1 - len(arrivals)):
            stats = run([piece], stats, 0 if last else float(total))
    return stats


def solution(mesh):
    return jax.shard_map(
        body,
        mesh=mesh,
        in_specs=(
            P(("groups", "orient"), "tile"),
            P("orient", None, None),
            P(("groups", "orient")),
            P("groups", None, None),
            P(("groups", "orient"), "tile"),
        ),
        out_specs=(
            P(("groups", "orient"), "tile"),
            P(("groups", "orient"), "tile"),
            P(("groups", "orient"), "tile"),
        ),
        check_vma=False,
    )
```

```python
import functools
import math

import jax
import jax.numpy as jnp
import ml_dtypes
import numpy as np
from jax import lax
from jax.experimental import pallas as pl
from jax.experimental.pallas import tpu as pltpu
from jax.sharding import PartitionSpec as P

RB = 32
CHUNK = 8


def extended(block, sides, width):
    for axis, dim in sides:
        count = lax.axis_size(axis)
        forward = [(i, i + 1) for i in range(count - 1)]
        backward = [(target, source) for source, target in forward]
        low = lax.ppermute(
            lax.slice_in_dim(block, block.shape[dim] - width, None, axis=dim), axis, forward
        )
        high = lax.ppermute(lax.slice_in_dim(block, 0, width, axis=dim), axis, backward)
        block = jnp.concatenate([low, block, high], axis=dim)
    return block


def twiddles(padded_size):
    position = np.arange(padded_size, dtype=np.int64)
    phase_index = (position[:, None] * position[None, :]) % padded_size
    angles = phase_index.astype(np.float32) * np.float32(2.0 * math.pi / padded_size)
    angles = angles.astype(np.float64)
    cosines = np.cos(angles).astype(np.float32).astype(ml_dtypes.bfloat16)
    sines = np.sin(angles).astype(np.float32).astype(ml_dtypes.bfloat16)
    return cosines, sines


def matmul(left, right):
    return jnp.dot(left, right, preferred_element_type=jnp.float32)


def exchange_rounds(block):
    size = lax.axis_size("orient")
    step = 1
    while step * 2 < size:
        step *= 2
    rounds = [block]
    held = block
    while step >= 1:
        other = lax.ppermute(held, "orient", [(i, i ^ step) for i in range(size)])
        if len(rounds) > 1:
            other, rounds[-1] = lax.optimization_barrier((other, rounds[-1]))
        rounds.append(other)
        held = jnp.concatenate([held, other], axis=0)
        step //= 2
    return rounds


def swap(payload, pairs):
    return lax.ppermute(payload, "orient", [(a, b) for a, b in pairs] + [(b, a) for a, b in pairs])


def exchange_with_rows(block, tile, width):
    size = lax.axis_size("orient")
    index = lax.axis_index("orient")
    odd = index % 2 == 1
    low_rows = tile[tile.shape[0] - width :]
    high_rows = tile[:width]
    lanes = block.shape[1]
    carried = width * tile.shape[1] // lanes

    def send(held, rows, pairs):
        payload = jnp.concatenate([held, rows.reshape(carried, lanes)], axis=0)
        got = swap(payload, pairs)
        return got[: held.shape[0]], got[held.shape[0] :].reshape(width, tile.shape[1])

    first, rows_one = send(block, jnp.where(odd, high_rows, low_rows), [(2 * i, 2 * i + 1) for i in range(size // 2)])
    held = jnp.concatenate([block, first], axis=0)
    second_pairs = [(2 * i + 1, 2 * i + 2) for i in range(size // 2 - 1)] + [(0, size - 1)]
    second, rows_two = send(held, jnp.where(odd, low_rows, high_rows), second_pairs)
    held = jnp.concatenate([held, second], axis=0)
    third_pairs = [(0, size // 2), (size - 1, size // 2 - 1), (1, size // 2 + 1), (2, size // 2 + 2)]
    cores = lax.axis_size("tile")
    share = held.shape[0] // cores
    core = lax.axis_index("tile")
    mine = lax.dynamic_slice_in_dim(held, core * share, share, 0)
    third = swap(mine, third_pairs)
    arrivals = [held, third]
    zero = jnp.zeros_like(rows_one)
    top = jnp.where(odd, rows_one, jnp.where(index == 0, zero, rows_two))
    bottom = jnp.where(odd, jnp.where(index == size - 1, zero, rows_two), rows_one)
    return arrivals, jnp.concatenate([top, tile, bottom], axis=0)


def correlate_kernel(ids_ref, live_ref, tmpl_ref, other_ref, *refs, scaling, total, block, first, group, from_half):
    bf16 = jnp.bfloat16
    f32 = jnp.float32
    o = pl.program_id(0)

    def mm(a, b):
        return jnp.dot(a, b, preferred_element_type=f32)

    ctf_refs = refs[:group]
    refs = refs[group:]
    if from_half:
        padded_ref, cos_ref, sin_ref = refs[:3]
        refs = refs[3:]
    else:
        spec_r_ref, spec_i_ref = refs[:2]
        refs = refs[2:]
    (cos_rows_ref, sin_rows_ref, cols_ref, rows_ref, col_cos_ref, col_sin_ref) = refs[:6]
    refs = refs[6:]
    if from_half:
        spec_r_ref, spec_i_ref = refs[-2:]
        refs = refs[:-2]

        @pl.when(o == 0)
        def _():
            cos = cos_ref[...]
            sin = sin_ref[...]
            padded = padded_ref[...]
            half_real = mm(padded, cos).astype(bf16)
            half_imag = (-mm(padded, sin)).astype(bf16)
            spec_r_ref[...] = (mm(cos, half_real) + mm(sin, half_imag)).astype(bf16)
            spec_i_ref[...] = (mm(cos, half_imag) - mm(sin, half_real)).astype(bf16)

    if len(refs) == 6:
        prev_peak_ref, prev_sum_ref, prev_sq_ref, peak_ref, sum_ref, sq_ref = refs
    else:
        peak_ref, sum_ref, sq_ref = refs

    cos_rows = cos_rows_ref[...]
    sin_rows = sin_rows_ref[...]
    cols = cols_ref[...]
    rows = rows_ref[...]
    col_cos = col_cos_ref[...]
    col_sin = col_sin_ref[...]
    spec_real = spec_r_ref[...].astype(f32)
    spec_imag = spec_i_ref[...].astype(f32)
    n = cols.shape[0] // 2
    tile = rows.shape[0] // 2

    def one(g):
        template = jnp.where(o < first, tmpl_ref[g], other_ref[g])
        part_real = mm(template, cos_rows).astype(bf16)
        part_imag = (-mm(template, sin_rows)).astype(bf16)
        from_real = mm(cols, part_real)
        from_imag = mm(cols, part_imag)
        full_real = from_real[:n] + from_imag[n:]
        full_imag = from_imag[:n] - from_real[n:]
        weight = ctf_refs[g][0]
        w_real = (full_real * weight).astype(bf16).astype(f32)
        w_imag = (full_imag * weight).astype(bf16).astype(f32)
        prod_real = (spec_real * w_real + spec_imag * w_imag).astype(bf16)
        prod_imag = (spec_imag * w_real - spec_real * w_imag).astype(bf16)
        left_from_real = mm(rows, prod_real)
        left_from_imag = mm(rows, prod_imag)
        left_real = (left_from_real[:tile] - left_from_imag[tile:]).astype(bf16)
        left_imag = (left_from_imag[:tile] + left_from_real[tile:]).astype(bf16)
        return (mm(left_real, col_cos) - mm(left_imag, col_sin)) * scaling

    corrs = [one(g) for g in range(group)]
    step_peak = corrs[0]
    step_sum = corrs[0]
    step_sq = corrs[0] * corrs[0]
    for corr in corrs[1:]:
        step_peak = jnp.maximum(step_peak, corr)
        step_sum = step_sum + corr
        step_sq = step_sq + corr * corr

    @pl.when(o == 0)
    def _():
        if len(refs) == 6:
            peak_ref[...] = jnp.maximum(prev_peak_ref[...], step_peak)
            sum_ref[...] = prev_sum_ref[...] + step_sum
            sq_ref[...] = prev_sq_ref[...] + step_sq
        else:
            peak_ref[...] = step_peak
            sum_ref[...] = step_sum
            sq_ref[...] = step_sq

    @pl.when(o > 0)
    def _():
        peak_ref[...] = jnp.maximum(peak_ref[...], step_peak)
        sum_ref[...] = sum_ref[...] + step_sum
        sq_ref[...] = sq_ref[...] + step_sq

    if total:
        @pl.when(o == pl.num_programs(0) - 1)
        def _():
            rows_at = lax.broadcasted_iota(jnp.int32, peak_ref.shape, 0)
            live = rows_at < block * live_ref[0]
            peak_ref[...] = jnp.where(live, peak_ref[...], 0.0)
            sum_ref[...] = jnp.where(live, sum_ref[...] / total, 0.0)
            sq_ref[...] = jnp.where(live, sq_ref[...] / total, 0.0)


def correlate(ids, live, pieces, ctf, spectrum, tables, scaling, previous, total, from_half=False):
    pieces = list(pieces)
    group = 2 if all(piece.shape[0] % 2 == 0 for piece in pieces) else 1
    first = pieces[0].shape[0] // group
    steps = sum(piece.shape[0] for piece in pieces) // group
    if len(pieces) == 1:
        pieces.append(pieces[0])
    last_other = pieces[1].shape[0] // group - 1
    box = pieces[0].shape[2]
    n = ctf.shape[1]
    tile = tables[4].shape[1]
    full = lambda shape: pl.BlockSpec(shape, lambda o, ids, live: (0,) * len(shape))

    def plane(g):
        return pl.BlockSpec((1, n, n), lambda o, ids, live: (ids[o * group + g], 0, 0))

    in_specs = (
        [
            pl.BlockSpec((group, box, box), lambda o, ids, live: (jnp.minimum(o, first - 1), 0, 0)),
            pl.BlockSpec((group, box, box), lambda o, ids, live: (jnp.clip(o - first, 0, last_other), 0, 0)),
        ]
        + [plane(g) for g in range(group)]
        + [full((n, n))] * len(spectrum)
        + [full(t.shape) for t in tables]
        + [full((tile, tile))] * len(previous)
    )
    out_block = full((tile, tile))
    out_specs = [out_block, out_block, out_block]
    out_shape = [jax.ShapeDtypeStruct((tile, tile), jnp.float32)] * 3
    if from_half:
        out_specs += [full((n, n)), full((n, n))]
        out_shape += [jax.ShapeDtypeStruct((n, n), jnp.bfloat16)] * 2
    grid_spec = pltpu.PrefetchScalarGridSpec(
        num_scalar_prefetch=2,
        grid=(steps,),
        in_specs=in_specs,
        out_specs=out_specs,
    )
    kernel = functools.partial(
        correlate_kernel, scaling=scaling, total=total, block=RB, first=first, group=group, from_half=from_half
    )
    base = 4 + group + len(spectrum) + len(tables)
    return pl.pallas_call(
        kernel,
        grid_spec=grid_spec,
        out_shape=out_shape,
        compiler_params=pltpu.CompilerParams(dimension_semantics=("arbitrary",)),
        input_output_aliases={base + i: i for i in range(len(previous))},
    )(ids, live, pieces[0], pieces[1], *([ctf] * group), *spectrum, *tables, *previous)


def body(micrograph, templates, defocus, ctf, usable):
    bf16 = jnp.bfloat16
    f32 = jnp.float32
    tile_width = micrograph.shape[0]
    padded_size = ctf.shape[1]
    box_size = templates.shape[1]
    margin = (padded_size - tile_width) // 2
    scaling = 1.0 / (padded_size * padded_size)
    n = padded_size
    cos_np, sin_np = twiddles(n)

    cos_full, sin_full = lax.optimization_barrier((jnp.asarray(cos_np), jnp.asarray(sin_np)))
    low = n - box_size // 2
    cos_rows = jnp.concatenate([cos_full[low:], cos_full[: box_size - (n - low)]], axis=0)
    sin_rows = jnp.concatenate([sin_full[low:], sin_full[: box_size - (n - low)]], axis=0)
    cos_cols = cos_rows.T
    sin_cols = sin_rows.T
    row_cos = cos_full[margin : margin + tile_width]
    row_sin = sin_full[margin : margin + tile_width]
    col_cos = row_cos.T
    col_sin = row_sin.T

    local_count = templates.shape[0]
    id_rows = jnp.broadcast_to(defocus.astype(bf16)[:, None, None], (local_count, 8, box_size))
    block_rows = box_size + 8
    packed = jnp.concatenate([templates, id_rows], axis=1).reshape(local_count * block_rows, box_size)
    split_last = lax.axis_size("orient") == 8 and lax.axis_size("tile") == 2
    split_last = split_last and local_count == 1 and (margin * tile_width) % box_size == 0
    if split_last:
        arrivals, row_padded = exchange_with_rows(packed, micrograph, margin)
        core = lax.axis_index("tile")
        edge = jnp.where(core == 0, row_padded[:, tile_width - margin :], row_padded[:, :margin])
        got = lax.ppermute(edge, "tile", [(0, 1), (1, 0)])
        zero = jnp.zeros_like(got)
        padded = jnp.concatenate(
            [jnp.where(core == 0, zero, got), row_padded, jnp.where(core == 0, got, zero)], axis=1
        )
    else:
        arrivals = exchange_rounds(packed)
        padded = extended(micrograph, (("orient", 0), ("tile", 1)), margin)
    total = sum(piece.shape[0] for piece in arrivals) // block_rows


    tables = (
        cos_rows,
        sin_rows,
        jnp.concatenate([cos_cols, sin_cols], axis=0),
        jnp.concatenate([row_cos, row_sin], axis=0),
        col_cos,
        col_sin,
    )
    shape = (tile_width, tile_width)
    stats = ()
    live = usable.reshape(-1)[:1]

    spectrum = [padded, cos_full, sin_full]

    def run(pieces, stats, total=0):
        pieces = [piece.reshape(piece.shape[0] // block_rows, block_rows, box_size) for piece in pieces]
        piece_ids = jnp.concatenate([piece[:, box_size, 0] for piece in pieces]).astype(jnp.int32)
        from_half = len(spectrum) == 3
        outs = correlate(piece_ids, live, pieces, ctf, spectrum, tables, scaling, stats, total, from_half)
        if from_half:
            spectrum[:] = outs[3:]
        return tuple(outs[:3])

    if split_last:
        stats = run([arrivals[0]], stats)
        half, stats = lax.optimization_barrier((arrivals[1], stats))
        other_half = lax.ppermute(half, "tile", [(0, 1), (1, 0)])
        total = (arrivals[0].shape[0] + 2 * half.shape[0]) // block_rows
        stats = run([half, other_half], stats, float(total))
    else:
        for last, piece in enumerate(arrivals, 1 - len(arrivals)):
            stats = run([piece], stats, 0 if last else float(total))
    return stats


def solution(mesh):
    return jax.shard_map(
        body,
        mesh=mesh,
        in_specs=(
            P(("groups", "orient"), "tile"),
            P("orient", None, None),
            P(("groups", "orient")),
            P("groups", None, None),
            P(("groups", "orient"), "tile"),
        ),
        out_specs=(
            P(("groups", "orient"), "tile"),
            P(("groups", "orient"), "tile"),
            P(("groups", "orient"), "tile"),
        ),
        check_vma=False,
    )
```

```python
import functools
import math

import jax
import jax.numpy as jnp
import ml_dtypes
import numpy as np
from jax import lax
from jax.experimental import pallas as pl
from jax.experimental.pallas import tpu as pltpu
from jax.sharding import PartitionSpec as P

RB = 32
CHUNK = 8


def extended(block, sides, width):
    for axis, dim in sides:
        count = lax.axis_size(axis)
        forward = [(i, i + 1) for i in range(count - 1)]
        backward = [(target, source) for source, target in forward]
        low = lax.ppermute(
            lax.slice_in_dim(block, block.shape[dim] - width, None, axis=dim), axis, forward
        )
        high = lax.ppermute(lax.slice_in_dim(block, 0, width, axis=dim), axis, backward)
        block = jnp.concatenate([low, block, high], axis=dim)
    return block


def twiddles(padded_size):
    position = np.arange(padded_size, dtype=np.int64)
    phase_index = (position[:, None] * position[None, :]) % padded_size
    angles = phase_index.astype(np.float32) * np.float32(2.0 * math.pi / padded_size)
    angles = angles.astype(np.float64)
    cosines = np.cos(angles).astype(np.float32).astype(ml_dtypes.bfloat16)
    sines = np.sin(angles).astype(np.float32).astype(ml_dtypes.bfloat16)
    return cosines, sines


def matmul(left, right):
    return jnp.dot(left, right, preferred_element_type=jnp.float32)


def exchange_rounds(block):
    size = lax.axis_size("orient")
    step = 1
    while step * 2 < size:
        step *= 2
    rounds = [block]
    held = block
    while step >= 1:
        other = lax.ppermute(held, "orient", [(i, i ^ step) for i in range(size)])
        if len(rounds) > 1:
            other, rounds[-1] = lax.optimization_barrier((other, rounds[-1]))
        rounds.append(other)
        held = jnp.concatenate([held, other], axis=0)
        step //= 2
    return rounds


def swap(payload, pairs):
    return lax.ppermute(payload, "orient", [(a, b) for a, b in pairs] + [(b, a) for a, b in pairs])


def exchange_with_rows(block, tile, width):
    size = lax.axis_size("orient")
    index = lax.axis_index("orient")
    odd = index % 2 == 1
    lanes = block.shape[1]

    def edge_rows(bottom):
        start = jnp.where(bottom, tile.shape[0] - width, 0)
        return lax.dynamic_slice_in_dim(tile, start, width, 0)

    def send(held, rows, pairs):
        padded_rows = jnp.pad(rows, ((0, 0), (0, lanes - rows.shape[1])))
        got = swap(jnp.concatenate([held, padded_rows], axis=0), pairs)
        return got[: held.shape[0]], got[held.shape[0] :, : tile.shape[1]]

    first, rows_one = send(block, edge_rows(jnp.logical_not(odd)), [(2 * i, 2 * i + 1) for i in range(size // 2)])
    held = jnp.concatenate([block, first], axis=0)
    second_pairs = [(2 * i + 1, 2 * i + 2) for i in range(size // 2 - 1)] + [(0, size - 1)]
    second, rows_two = send(held, edge_rows(odd), second_pairs)
    held = jnp.concatenate([held, second], axis=0)
    third_pairs = [(0, size // 2), (size - 1, size // 2 - 1), (1, size // 2 + 1), (2, size // 2 + 2)]
    cores = lax.axis_size("tile")
    share = held.shape[0] // cores
    core = lax.axis_index("tile")
    mine = lax.dynamic_slice_in_dim(held, core * share, share, 0)
    third = swap(mine, third_pairs)
    arrivals = [held, third]
    zero = jnp.zeros_like(rows_one)
    top = jnp.where(odd, rows_one, jnp.where(index == 0, zero, rows_two))
    bottom = jnp.where(odd, jnp.where(index == size - 1, zero, rows_two), rows_one)
    return arrivals, jnp.concatenate([top, tile, bottom], axis=0)


def correlate_kernel(ids_ref, live_ref, tmpl_ref, other_ref, *refs, scaling, total, block, first, group, from_half):
    bf16 = jnp.bfloat16
    f32 = jnp.float32
    o = pl.program_id(0)

    def mm(a, b):
        return jnp.dot(a, b, preferred_element_type=f32)

    ctf_refs = refs[:group]
    refs = refs[group:]
    if from_half:
        padded_ref, cos_ref, sin_ref = refs[:3]
        refs = refs[3:]
    else:
        spec_r_ref, spec_i_ref = refs[:2]
        refs = refs[2:]
    (cos_rows_ref, sin_rows_ref, cols_ref, rows_ref, col_cos_ref, col_sin_ref) = refs[:6]
    refs = refs[6:]
    if from_half:
        spec_r_ref, spec_i_ref = refs[-2:]
        refs = refs[:-2]

        @pl.when(o == 0)
        def _():
            cos = cos_ref[...]
            sin = sin_ref[...]
            padded = padded_ref[...]
            half_real = mm(padded, cos).astype(bf16)
            half_imag = (-mm(padded, sin)).astype(bf16)
            spec_r_ref[...] = (mm(cos, half_real) + mm(sin, half_imag)).astype(bf16)
            spec_i_ref[...] = (mm(cos, half_imag) - mm(sin, half_real)).astype(bf16)

    if len(refs) == 6:
        prev_peak_ref, prev_sum_ref, prev_sq_ref, peak_ref, sum_ref, sq_ref = refs
    else:
        peak_ref, sum_ref, sq_ref = refs

    def one(g):
        template = jnp.where(o < first, tmpl_ref[g], other_ref[g])
        part_real = mm(template, cos_rows_ref[...]).astype(bf16)
        part_imag = (-mm(template, sin_rows_ref[...])).astype(bf16)
        cols = cols_ref[...]
        n = cols.shape[0] // 2
        from_real = mm(cols, part_real)
        from_imag = mm(cols, part_imag)
        full_real = from_real[:n] + from_imag[n:]
        full_imag = from_imag[:n] - from_real[n:]
        weight = ctf_refs[g][0]
        w_real = (full_real * weight).astype(bf16).astype(f32)
        w_imag = (full_imag * weight).astype(bf16).astype(f32)
        spec_real = spec_r_ref[...].astype(f32)
        spec_imag = spec_i_ref[...].astype(f32)
        prod_real = (spec_real * w_real + spec_imag * w_imag).astype(bf16)
        prod_imag = (spec_imag * w_real - spec_real * w_imag).astype(bf16)
        rows = rows_ref[...]
        tile = rows.shape[0] // 2
        left_from_real = mm(rows, prod_real)
        left_from_imag = mm(rows, prod_imag)
        left_real = (left_from_real[:tile] - left_from_imag[tile:]).astype(bf16)
        left_imag = (left_from_imag[:tile] + left_from_real[tile:]).astype(bf16)
        return (mm(left_real, col_cos_ref[...]) - mm(left_imag, col_sin_ref[...])) * scaling

    corrs = [one(g) for g in range(group)]
    step_peak = corrs[0]
    step_sum = corrs[0]
    step_sq = corrs[0] * corrs[0]
    for corr in corrs[1:]:
        step_peak = jnp.maximum(step_peak, corr)
        step_sum = step_sum + corr
        step_sq = step_sq + corr * corr

    @pl.when(o == 0)
    def _():
        if len(refs) == 6:
            peak_ref[...] = jnp.maximum(prev_peak_ref[...], step_peak)
            sum_ref[...] = prev_sum_ref[...] + step_sum
            sq_ref[...] = prev_sq_ref[...] + step_sq
        else:
            peak_ref[...] = step_peak
            sum_ref[...] = step_sum
            sq_ref[...] = step_sq

    @pl.when(o > 0)
    def _():
        peak_ref[...] = jnp.maximum(peak_ref[...], step_peak)
        sum_ref[...] = sum_ref[...] + step_sum
        sq_ref[...] = sq_ref[...] + step_sq

    if total:
        @pl.when(o == pl.num_programs(0) - 1)
        def _():
            rows_at = lax.broadcasted_iota(jnp.int32, peak_ref.shape, 0)
            live = rows_at < block * live_ref[0]
            peak_ref[...] = jnp.where(live, peak_ref[...], 0.0)
            sum_ref[...] = jnp.where(live, sum_ref[...] / total, 0.0)
            sq_ref[...] = jnp.where(live, sq_ref[...] / total, 0.0)


def correlate(ids, live, pieces, ctf, spectrum, tables, scaling, previous, total, from_half=False):
    pieces = list(pieces)
    group = 2 if all(piece.shape[0] % 2 == 0 for piece in pieces) else 1
    first = pieces[0].shape[0] // group
    steps = sum(piece.shape[0] for piece in pieces) // group
    if len(pieces) == 1:
        pieces.append(pieces[0])
    last_other = pieces[1].shape[0] // group - 1
    box = pieces[0].shape[2]
    n = ctf.shape[1]
    tile = tables[4].shape[1]
    full = lambda shape: pl.BlockSpec(shape, lambda o, ids, live: (0,) * len(shape))

    def plane(g):
        return pl.BlockSpec((1, n, n), lambda o, ids, live: (ids[o * group + g], 0, 0))

    in_specs = (
        [
            pl.BlockSpec((group, box, box), lambda o, ids, live: (jnp.minimum(o, first - 1), 0, 0)),
            pl.BlockSpec((group, box, box), lambda o, ids, live: (jnp.clip(o - first, 0, last_other), 0, 0)),
        ]
        + [plane(g) for g in range(group)]
        + [full((n, n))] * len(spectrum)
        + [full(t.shape) for t in tables]
        + [full((tile, tile))] * len(previous)
    )
    out_block = full((tile, tile))
    out_specs = [out_block, out_block, out_block]
    out_shape = [jax.ShapeDtypeStruct((tile, tile), jnp.float32)] * 3
    if from_half:
        out_specs += [full((n, n)), full((n, n))]
        out_shape += [jax.ShapeDtypeStruct((n, n), jnp.bfloat16)] * 2
    grid_spec = pltpu.PrefetchScalarGridSpec(
        num_scalar_prefetch=2,
        grid=(steps,),
        in_specs=in_specs,
        out_specs=out_specs,
    )
    kernel = functools.partial(
        correlate_kernel, scaling=scaling, total=total, block=RB, first=first, group=group, from_half=from_half
    )
    base = 4 + group + len(spectrum) + len(tables)
    return pl.pallas_call(
        kernel,
        grid_spec=grid_spec,
        out_shape=out_shape,
        compiler_params=pltpu.CompilerParams(dimension_semantics=("arbitrary",)),
        input_output_aliases={base + i: i for i in range(len(previous))},
    )(ids, live, pieces[0], pieces[1], *([ctf] * group), *spectrum, *tables, *previous)


def body(micrograph, templates, defocus, ctf, usable):
    bf16 = jnp.bfloat16
    f32 = jnp.float32
    tile_width = micrograph.shape[0]
    padded_size = ctf.shape[1]
    box_size = templates.shape[1]
    margin = (padded_size - tile_width) // 2
    scaling = 1.0 / (padded_size * padded_size)
    n = padded_size
    cos_np, sin_np = twiddles(n)

    cos_full, sin_full = lax.optimization_barrier((jnp.asarray(cos_np), jnp.asarray(sin_np)))
    low = n - box_size // 2
    cos_rows = jnp.concatenate([cos_full[low:], cos_full[: box_size - (n - low)]], axis=0)
    sin_rows = jnp.concatenate([sin_full[low:], sin_full[: box_size - (n - low)]], axis=0)
    cos_cols = cos_rows.T
    sin_cols = sin_rows.T
    row_cos = cos_full[margin : margin + tile_width]
    row_sin = sin_full[margin : margin + tile_width]
    col_cos = row_cos.T
    col_sin = row_sin.T

    local_count = templates.shape[0]
    id_rows = jnp.broadcast_to(defocus.astype(bf16)[:, None, None], (local_count, 8, box_size))
    block_rows = box_size + 8
    packed = jnp.concatenate([templates, id_rows], axis=1).reshape(local_count * block_rows, box_size)
    split_last = lax.axis_size("orient") == 8 and lax.axis_size("tile") == 2
    split_last = split_last and local_count == 1 and tile_width <= box_size
    if split_last:
        arrivals, row_padded = exchange_with_rows(packed, micrograph, margin)
        core = lax.axis_index("tile")
        edge = jnp.where(core == 0, row_padded[:, tile_width - margin :], row_padded[:, :margin])
        got = lax.ppermute(edge, "tile", [(0, 1), (1, 0)])
        zero = jnp.zeros_like(got)
        padded = jnp.concatenate(
            [jnp.where(core == 0, zero, got), row_padded, jnp.where(core == 0, got, zero)], axis=1
        )
    else:
        arrivals = exchange_rounds(packed)
        padded = extended(micrograph, (("orient", 0), ("tile", 1)), margin)
    total = sum(piece.shape[0] for piece in arrivals) // block_rows


    tables = (
        cos_rows,
        sin_rows,
        jnp.concatenate([cos_cols, sin_cols], axis=0),
        jnp.concatenate([row_cos, row_sin], axis=0),
        col_cos,
        col_sin,
    )
    shape = (tile_width, tile_width)
    stats = ()
    live = usable.reshape(-1)[:1]

    spectrum = [padded, cos_full, sin_full]

    def run(pieces, stats, total=0):
        pieces = [piece.reshape(piece.shape[0] // block_rows, block_rows, box_size) for piece in pieces]
        piece_ids = jnp.concatenate([piece[:, box_size, 0] for piece in pieces]).astype(jnp.int32)
        from_half = len(spectrum) == 3
        outs = correlate(piece_ids, live, pieces, ctf, spectrum, tables, scaling, stats, total, from_half)
        if from_half:
            spectrum[:] = outs[3:]
        return tuple(outs[:3])

    if split_last:
        stats = run([arrivals[0]], stats)
        half, stats = lax.optimization_barrier((arrivals[1], stats))
        other_half = lax.ppermute(half, "tile", [(0, 1), (1, 0)])
        total = (arrivals[0].shape[0] + 2 * half.shape[0]) // block_rows
        stats = run([half, other_half], stats, float(total))
    else:
        for last, piece in enumerate(arrivals, 1 - len(arrivals)):
            stats = run([piece], stats, 0 if last else float(total))
    return stats


def solution(mesh):
    return jax.shard_map(
        body,
        mesh=mesh,
        in_specs=(
            P(("groups", "orient"), "tile"),
            P("orient", None, None),
            P(("groups", "orient")),
            P("groups", None, None),
            P(("groups", "orient"), "tile"),
        ),
        out_specs=(
            P(("groups", "orient"), "tile"),
            P(("groups", "orient"), "tile"),
            P(("groups", "orient"), "tile"),
        ),
        check_vma=False,
    )
```
